32 devices in a mesh: groups: 2 (over y), leaf: 4 (over x, core), sub: 4 (over z).
Axes of the slice: x: 2, y: 2, z: 4, core: 2. Of those that a mesh axis runs over, the one named last changes fastest.
Arguments:
- embeddings: bfloat16 [128, 32768], P(None, ('groups', 'leaf', 'sub')), parts along dimension 1
- directions: float32 [32, 32768], P(None, ('groups', 'leaf', 'sub')), parts along dimension 1, may hold values from -6 to 6
- level_basis: bfloat16 [5, 64, 32768], P(None, None, ('groups', 'leaf', 'sub')), parts along dimension 2, may hold values from -6 to 6
- neighbours: int32 [64, 8], P(('groups', 'leaf', 'sub')), parts along dimension 0, may hold values from 0 to 31, as said below
- counts: int32 [64], P(('groups', 'leaf', 'sub')), parts along dimension 0, may hold values from 2 to 8
Outputs:
- kernel_image: float32 [32, 32768], P(None, ('groups', 'leaf', 'sub')), parts along dimension 1
The draws below stay inside these ranges and needn't reach their ends.
There are 2 independent parts, one for each index of `groups`. The reference program is written for one: setup_inputs(seed, part) draws one part's arguments, and reference() takes and returns one part's arrays. A program takes and returns all parts, laid end to end along the dimension named above; each array names one. Nothing has to cross between parts.
Inputs may be any that keep to these rules, and one draw needn't show every extreme that they name: `neighbours`: every entry names the leaf just before or just after its own row's leaf; slot 0 names the leaf just before and slot 1 the leaf just after (for the first and the last leaf, both name the one adjacent leaf).
All inputs are finite; a program needn't handle non-finite values.
Results may differ from the reference program's by a relative error of at most 0.0039.
Values may be sent and summed in bfloat16 or wider, within the bound.
No kernel may reach another device: no remote copies, remote signals or barrier semaphores. Data moves between devices by JAX's collectives and lax.ppermute only.
A program may use at most 64 MiB of HBM per device.

```python
import math
import jax
import jax.numpy as jnp
from jax import lax

LEAF = 512
E = 128
NRHS = 32
RANK = 64
NBMAX = 8
LEAVES_DEV = 2
NDEV = 16
LEVELS = 5
POINTS = 16384
LEAVES = 32


def draw_embeddings(key, part):
    raw = jax.random.normal(key, (E, POINTS), jnp.float32)
    decay = 0.625 * jnp.exp(-jnp.arange(E, dtype=jnp.float32) / 64.0)
    return (raw * decay[:, None]).astype(jnp.bfloat16)


def draw_neighbours(key, part):
    own = jnp.arange(LEAVES, dtype=jnp.int32)[:, None]
    sign = 2 * jax.random.randint(key, (LEAVES, NBMAX), 0, 2).astype(jnp.int32) - 1
    slot_ids = jnp.arange(NBMAX, dtype=jnp.int32)[None, :]
    sign = jnp.where(slot_ids == 0, -1, sign)
    sign = jnp.where(slot_ids == 1, 1, sign)
    target = own + sign
    target = jnp.where(target < 0, own + 1, target)
    target = jnp.where(target >= LEAVES, own - 1, target)
    return target.astype(jnp.int32)


def draw_counts(key, part):
    key_caps = jax.random.fold_in(key, 11)
    key_fill = jax.random.fold_in(key, 12)
    key_first = jax.random.fold_in(key, 13)
    key_second = jax.random.fold_in(key, 14)
    caps = jax.random.randint(key_caps, (NDEV,), 2, NBMAX + 1).astype(jnp.int32)
    leaf_caps = jnp.repeat(caps, LEAVES_DEV)
    filled = jax.random.randint(key_fill, (LEAVES,), 2, leaf_caps + 1).astype(jnp.int32)
    first_pick = jax.random.randint(key_first, (), 0, LEAVES).astype(jnp.int32)
    second_pick = (first_pick + 1 + jax.random.randint(key_second, (), 0, LEAVES - 1).astype(jnp.int32)) % LEAVES
    filled = filled.at[first_pick].set(NBMAX)
    filled = filled.at[second_pick].set(2)
    return filled.astype(jnp.int32)


def level_of(rng, dims, pieces, low, top_value):
    factor_of = 1.0
    for dim, parts in pieces:
        heights = jax.random.uniform(jax.random.fold_in(jax.random.fold_in(rng, 6), dim), (parts,), jnp.float32, low / len(pieces), top_value / len(pieces))
        factor_of = factor_of * jnp.repeat(jnp.exp(heights), dims[dim] // parts).reshape((-1,) + (1,) * (len(dims) - 1 - dim))
    return factor_of


def centred(own_key, shape, scale, reach, pieces=(), kind=jnp.bfloat16):
    entries = jax.random.normal(own_key, shape, jnp.float32) * scale
    if len(pieces) > 0:
        entries = level_of(own_key, shape, pieces, -0.22, 0.18) * entries
    return jnp.clip(entries, min=-reach, max=reach).astype(kind)


def setup_inputs(seed: int = 0, part: int = 0) -> dict:
    arg_keys = jax.random.split(jax.random.key(seed), 6)
    part_splits = jax.random.split(jax.random.fold_in(arg_keys[5], part), 6)
    return {
        "embeddings": draw_embeddings(jax.random.fold_in(jax.random.fold_in(arg_keys[5], part), 71), part),
        "directions": centred(part_splits[1], (NRHS, POINTS), 1.0, 6.0, ((1, 16),), jnp.float32),
        "level_basis": centred(part_splits[2], (LEVELS, RANK, POINTS), 1.0, 6.0, ((2, 16),)),
        "neighbours": draw_neighbours(jax.random.fold_in(jax.random.fold_in(arg_keys[5], part), 71), part),
        "counts": draw_counts(jax.random.fold_in(jax.random.fold_in(arg_keys[5], part), 71), part),
    }


AMPLITUDE = 0.5
DISTANCE_SCALE = 0.125
RIDGE = 0.5

def kernel_apply(target_points, source_points, source_values):
    target_float = target_points.astype(jnp.float32)
    source_float = source_points.astype(jnp.float32)
    inner = jnp.dot(target_float.T, source_float)
    target_norms = lax.optimization_barrier(jnp.sum(target_float * target_float, axis=0))
    source_norms = lax.optimization_barrier(jnp.sum(source_float * source_float, axis=0))
    distance = target_norms[:, None] + source_norms[None, :] - 2.0 * inner
    weights = (AMPLITUDE * jnp.exp(-DISTANCE_SCALE * distance)).astype(jnp.bfloat16)
    return jnp.dot(source_values.astype(jnp.float32), weights.astype(jnp.float32).T)

def reference(embeddings, directions, level_basis, neighbours, counts):
    values = directions.astype(jnp.bfloat16)
    leaf_points = embeddings.reshape(E, LEAVES, LEAF)
    leaf_values = values.reshape(NRHS, LEAVES, LEAF)
    leaf_ids = jnp.arange(LEAVES, dtype=jnp.int32)
    live = jnp.arange(NBMAX, dtype=jnp.int32)[None, :] < counts[:, None]
    below = lax.optimization_barrier(jnp.sum((live & (neighbours == (leaf_ids - 1)[:, None])).astype(jnp.float32), axis=1))
    above = lax.optimization_barrier(jnp.sum((live & (neighbours == (leaf_ids + 1)[:, None])).astype(jnp.float32), axis=1))

    def one_leaf(index):
        own_points = lax.dynamic_index_in_dim(leaf_points, index, 1, keepdims=False)
        own_values = lax.dynamic_index_in_dim(leaf_values, index, 1, keepdims=False)
        lower_index = jnp.maximum(index - 1, 0).astype(jnp.int32)
        upper_index = jnp.minimum(index + 1, LEAVES - 1).astype(jnp.int32)
        lower_points = lax.dynamic_index_in_dim(leaf_points, lower_index, 1, keepdims=False)
        lower_values = lax.dynamic_index_in_dim(leaf_values, lower_index, 1, keepdims=False)
        upper_points = lax.dynamic_index_in_dim(leaf_points, upper_index, 1, keepdims=False)
        upper_values = lax.dynamic_index_in_dim(leaf_values, upper_index, 1, keepdims=False)
        total = kernel_apply(own_points, own_points, own_values)
        total = total + below[index] * kernel_apply(own_points, lower_points, lower_values)
        total = total + above[index] * kernel_apply(own_points, upper_points, upper_values)
        return total
    near = lax.map(one_leaf, leaf_ids)
    near = jnp.transpose(near, (1, 0, 2)).reshape(NRHS, POINTS)
    far = jnp.zeros((NRHS, POINTS), jnp.float32)
    for level_index in range(LEVELS):
        width = LEAF * 2 ** level_index
        blocks = POINTS // width
        basis_view = level_basis[level_index].astype(jnp.float32).reshape(RANK, blocks, width)
        value_view = values.astype(jnp.float32).reshape(NRHS, blocks, width)
        coeffs = jnp.einsum('rqn,tqn->qrt', basis_view, value_view)
        scaled = (coeffs * (1.0 / math.sqrt(RANK * width))).astype(jnp.bfloat16)
        swapped = scaled.reshape(blocks // 2, 2, RANK, NRHS)[:, ::-1].reshape(blocks, RANK, NRHS)
        far = far + jnp.einsum('qrt,rqn->tqn', swapped.astype(jnp.float32), basis_view).reshape(NRHS, POINTS)
    return RIDGE * directions + near + far
```

```python
import math

import jax
import jax.numpy as jnp
from jax import lax
from jax.sharding import PartitionSpec as P

LEAF = 512


AMPLITUDE = 0.5
DISTANCE_SCALE = 0.125
RIDGE = 0.5


def shifted(x, axis, step):
    count = lax.axis_size(axis)
    if step > 0:
        pairs = [(i, i + step) for i in range(count - step)]
    else:
        pairs = [(i - step, i) for i in range(count + step)]
    return lax.ppermute(x, axis, pairs)


def from_mask(x, axis, mask):
    pairs = [(i, i ^ mask) for i in range(lax.axis_size(axis))]
    return lax.ppermute(x, axis, pairs)


def kernel_block(target_points, source_points):
    inner = lax.dot_general(
        target_points, source_points, (((0,), (0,)), ((), ())), preferred_element_type=jnp.float32
    )
    target_float = target_points.astype(jnp.float32)
    source_float = source_points.astype(jnp.float32)
    target_norms = jnp.sum(target_float * target_float, axis=0)
    source_norms = jnp.sum(source_float * source_float, axis=0)
    distance = target_norms[:, None] + source_norms[None, :] - 2.0 * inner
    return (AMPLITUDE * jnp.exp(-DISTANCE_SCALE * distance)).astype(jnp.bfloat16)


def apply_rows(weights, source_values):
    return lax.dot_general(
        source_values, weights, (((1,), (1,)), ((), ())), preferred_element_type=jnp.float32
    )


def apply_cols(weights, source_values):
    return lax.dot_general(
        source_values, weights, (((1,), (0,)), ((), ())), preferred_element_type=jnp.float32
    )


def on_device(embeddings, directions, level_basis, neighbours, counts):
    axes = ("leaf", "sub")
    values = directions.astype(jnp.bfloat16)
    width_e = embeddings.shape[0]
    local_points = embeddings.shape[1]
    local_leaves = local_points // LEAF
    me = lax.axis_index(axes)

    packed = jnp.concatenate([embeddings, values], axis=0)
    from_left = shifted(packed[:, local_points - LEAF :], axes, 1)
    from_right = shifted(packed[:, :LEAF], axes, -1)

    slots = neighbours.shape[1]
    live = jnp.arange(slots, dtype=jnp.int32)[None, :] < counts[:, None]
    leaf_ids = me * local_leaves + jnp.arange(local_leaves, dtype=jnp.int32)
    below = jnp.sum((live & (neighbours == (leaf_ids - 1)[:, None])).astype(jnp.float32), axis=1)
    above = jnp.sum((live & (neighbours == (leaf_ids + 1)[:, None])).astype(jnp.float32), axis=1)

    points = [embeddings[:, j * LEAF : (j + 1) * LEAF] for j in range(local_leaves)]
    leaf_values = [values[:, j * LEAF : (j + 1) * LEAF] for j in range(local_leaves)]
    near = [apply_rows(kernel_block(points[j], points[j]), leaf_values[j]) for j in range(local_leaves)]
    for j in range(local_leaves - 1):
        pair = kernel_block(points[j], points[j + 1])
        near[j] = near[j] + above[j] * apply_rows(pair, leaf_values[j + 1])
        near[j + 1] = near[j + 1] + below[j + 1] * apply_cols(pair, leaf_values[j])
    lower = kernel_block(points[0], from_left[:width_e])
    near[0] = near[0] + below[0] * apply_rows(lower, from_left[width_e:])
    last = local_leaves - 1
    upper = kernel_block(points[last], from_right[:width_e])
    near[last] = near[last] + above[last] * apply_rows(upper, from_right[width_e:])
    near = jnp.concatenate(near, axis=1)

    rank = level_basis.shape[1]
    nrhs = directions.shape[0]
    sub_size = lax.axis_size("sub")
    leaf_size = lax.axis_size("leaf")
    sub_bits = sub_size.bit_length() - 1
    leaf_bits = leaf_size.bit_length() - 1
    dev_bits = sub_bits + leaf_bits
    loc_bits = level_basis.shape[0] - dev_bits

    width = LEAF
    blocks = local_points // width
    basis_view = level_basis[0].reshape(rank, blocks, width)
    value_view = values.reshape(nrhs, blocks, width)
    coeffs = jnp.einsum("rqn,tqn->qrt", basis_view, value_view, preferred_element_type=jnp.float32)
    scaled = (coeffs * (1.0 / math.sqrt(rank * width))).astype(jnp.bfloat16)
    swapped = scaled.reshape(blocks // 2, 2, rank, nrhs)[:, ::-1].reshape(blocks, rank, nrhs)
    far = jnp.einsum(
        "qrt,rqn->tqn", swapped, basis_view, preferred_element_type=jnp.float32
    ).reshape(nrhs, local_points)

    upper_basis = level_basis[loc_bits:]
    partials = jnp.einsum("krn,tn->krt", upper_basis, values, preferred_element_type=jnp.float32)

    sibling = [None] * dev_bits
    line = partials[sub_bits:]
    for mask in range(1, sub_size):
        level = mask.bit_length() - 1
        got = from_mask(jnp.concatenate([partials[level : level + 1], partials[sub_bits:]], axis=0), "sub", mask)
        sibling[level] = got[0] if sibling[level] is None else sibling[level] + got[0]
        line = line + got[1:]
    for mask in range(1, leaf_size):
        level = mask.bit_length() - 1
        got = from_mask(line[level], "leaf", mask)
        index = sub_bits + level
        sibling[index] = got if sibling[index] is None else sibling[index] + got

    factors = jnp.array(
        [1.0 / math.sqrt(rank * local_points * 2**bit) for bit in range(dev_bits)], jnp.float32
    )
    scaled_upper = (jnp.stack(sibling) * factors[:, None, None]).astype(jnp.bfloat16)
    far = far + jnp.einsum("krt,krn->tn", scaled_upper, upper_basis, preferred_element_type=jnp.float32)
    return RIDGE * directions + near + far


def solution(mesh):
    placed = (
        P(None, ("groups", "leaf", "sub")),
        P(None, ("groups", "leaf", "sub")),
        P(None, None, ("groups", "leaf", "sub")),
        P(("groups", "leaf", "sub"), None),
        P(("groups", "leaf", "sub")),
    )
    return jax.shard_map(
        on_device,
        mesh=mesh,
        in_specs=placed,
        out_specs=P(None, ("groups", "leaf", "sub")),
        check_vma=False,
    )
```

```python
import math

import jax
import jax.numpy as jnp
from jax import lax
from jax.sharding import PartitionSpec as P

LEAF = 512


AMPLITUDE = 0.5
DISTANCE_SCALE = 0.125
RIDGE = 0.5


def shifted(x, axis, step):
    count = lax.axis_size(axis)
    if step > 0:
        pairs = [(i, i + step) for i in range(count - step)]
    else:
        pairs = [(i - step, i) for i in range(count + step)]
    return lax.ppermute(x, axis, pairs)


def from_mask(x, axis, mask):
    pairs = [(i, i ^ mask) for i in range(lax.axis_size(axis))]
    return lax.ppermute(x, axis, pairs)


def kernel_block(target_points, source_points):
    inner = lax.dot_general(
        target_points, source_points, (((0,), (0,)), ((), ())), preferred_element_type=jnp.float32
    )
    target_float = target_points.astype(jnp.float32)
    source_float = source_points.astype(jnp.float32)
    target_norms = jnp.sum(target_float * target_float, axis=0)
    source_norms = jnp.sum(source_float * source_float, axis=0)
    distance = target_norms[:, None] + source_norms[None, :] - 2.0 * inner
    return (AMPLITUDE * jnp.exp(-DISTANCE_SCALE * distance)).astype(jnp.bfloat16)


def apply_rows(weights, source_values):
    return lax.dot_general(
        source_values, weights, (((1,), (1,)), ((), ())), preferred_element_type=jnp.float32
    )


def apply_cols(weights, source_values):
    return lax.dot_general(
        source_values, weights, (((1,), (0,)), ((), ())), preferred_element_type=jnp.float32
    )


def on_device(embeddings, directions, level_basis, neighbours, counts):
    axes = ("leaf", "sub")
    values = directions.astype(jnp.bfloat16)
    width_e = embeddings.shape[0]
    local_points = embeddings.shape[1]
    local_leaves = local_points // LEAF
    me = lax.axis_index(axes)

    packed = jnp.concatenate([embeddings, values], axis=0)
    from_left = shifted(packed[:, local_points - LEAF :], axes, 1)
    from_right = shifted(packed[:, :LEAF], axes, -1)

    slots = neighbours.shape[1]
    live = jnp.arange(slots, dtype=jnp.int32)[None, :] < counts[:, None]
    leaf_ids = me * local_leaves + jnp.arange(local_leaves, dtype=jnp.int32)
    below = jnp.sum((live & (neighbours == (leaf_ids - 1)[:, None])).astype(jnp.float32), axis=1)
    above = jnp.sum((live & (neighbours == (leaf_ids + 1)[:, None])).astype(jnp.float32), axis=1)

    points = [embeddings[:, j * LEAF : (j + 1) * LEAF] for j in range(local_leaves)]
    leaf_values = [values[:, j * LEAF : (j + 1) * LEAF] for j in range(local_leaves)]
    near = [apply_rows(kernel_block(points[j], points[j]), leaf_values[j]) for j in range(local_leaves)]
    for j in range(local_leaves - 1):
        pair = kernel_block(points[j], points[j + 1])
        near[j] = near[j] + above[j] * apply_rows(pair, leaf_values[j + 1])
        near[j + 1] = near[j + 1] + below[j + 1] * apply_cols(pair, leaf_values[j])
    lower = kernel_block(points[0], from_left[:width_e])
    near[0] = near[0] + below[0] * apply_rows(lower, from_left[width_e:])
    last = local_leaves - 1
    upper = kernel_block(points[last], from_right[:width_e])
    near[last] = near[last] + above[last] * apply_rows(upper, from_right[width_e:])
    near = jnp.concatenate(near, axis=1)

    rank = level_basis.shape[1]
    nrhs = directions.shape[0]
    sub_size = lax.axis_size("sub")
    leaf_size = lax.axis_size("leaf")
    sub_bits = sub_size.bit_length() - 1
    leaf_bits = leaf_size.bit_length() - 1
    dev_bits = sub_bits + leaf_bits
    loc_bits = level_basis.shape[0] - dev_bits

    width = LEAF
    blocks = local_points // width
    basis_view = level_basis[0].reshape(rank, blocks, width)
    value_view = values.reshape(nrhs, blocks, width)
    coeffs = jnp.einsum("rqn,tqn->qrt", basis_view, value_view, preferred_element_type=jnp.float32)
    scaled = (coeffs * (1.0 / math.sqrt(rank * width))).astype(jnp.bfloat16)
    swapped = scaled.reshape(blocks // 2, 2, rank, nrhs)[:, ::-1].reshape(blocks, rank, nrhs)
    far = jnp.einsum(
        "qrt,rqn->tqn", swapped, basis_view, preferred_element_type=jnp.float32
    ).reshape(nrhs, local_points)

    upper_basis = level_basis[loc_bits:]
    partials = jnp.einsum("krn,tn->krt", upper_basis, values, preferred_element_type=jnp.float32)

    ndev = lax.axis_size(axes)
    others = jnp.arange(ndev, dtype=jnp.int32) ^ me
    level_of = sum((others >= 2**bit).astype(jnp.int32) for bit in range(1, dev_bits))
    outgoing = jnp.take(partials, level_of, axis=0)
    incoming = lax.all_to_all(outgoing, axes, 0, 0, tiled=True)
    picks = (level_of[None, :] == jnp.arange(dev_bits, dtype=jnp.int32)[:, None]) & (others > 0)[None, :]
    sibling = jnp.sum(jnp.where(picks[:, :, None, None], incoming[None], 0.0), axis=1)

    factors = jnp.array(
        [1.0 / math.sqrt(rank * local_points * 2**bit) for bit in range(dev_bits)], jnp.float32
    )
    scaled_upper = (sibling * factors[:, None, None]).astype(jnp.bfloat16)
    far = far + jnp.einsum("krt,krn->tn", scaled_upper, upper_basis, preferred_element_type=jnp.float32)
    return RIDGE * directions + near + far


def solution(mesh):
    placed = (
        P(None, ("groups", "leaf", "sub")),
        P(None, ("groups", "leaf", "sub")),
        P(None, None, ("groups", "leaf", "sub")),
        P(("groups", "leaf", "sub"), None),
        P(("groups", "leaf", "sub")),
    )
    return jax.shard_map(
        on_device,
        mesh=mesh,
        in_specs=placed,
        out_specs=P(None, ("groups", "leaf", "sub")),
        check_vma=False,
    )
```

```python
import functools
import math

import jax
import jax.numpy as jnp
from jax import lax
from jax.experimental import pallas as pl
from jax.experimental.pallas import tpu as pltpu
from jax.sharding import PartitionSpec as P

LEAF = 512


AMPLITUDE = 0.5
DISTANCE_SCALE = 0.125
RIDGE = 0.5

VMEM = pl.BlockSpec(memory_space=pltpu.VMEM)
SMEM = pl.BlockSpec(memory_space=pltpu.SMEM)


def shifted(x, axis, step):
    count = lax.axis_size(axis)
    if step > 0:
        pairs = [(i, i + step) for i in range(count - step)]
    else:
        pairs = [(i - step, i) for i in range(count + step)]
    return lax.ppermute(x, axis, pairs)


def top_bit(x, dev_bits):
    level = jnp.int32(0)
    for bit in range(1, dev_bits):
        level = level + (x >= 2**bit).astype(jnp.int32)
    return level


def nt_dot(a, b):
    return lax.dot_general(a, b, (((1,), (1,)), ((), ())), preferred_element_type=jnp.float32)


def nn_dot(a, b):
    return lax.dot_general(a, b, (((1,), (0,)), ((), ())), preferred_element_type=jnp.float32)


def send_kernel(sub_size, dev_bits, ndev, emb_ref, dirs_ref, basis_ref, first_ref, last_ref, out_ref, part_ref):
    width_e = emb_ref.shape[0]
    local_points = emb_ref.shape[1]
    values = dirs_ref[...].astype(jnp.bfloat16)
    first_ref[:width_e, :] = emb_ref[:, :LEAF]
    first_ref[width_e:, :] = values[:, :LEAF]
    last_ref[:width_e, :] = emb_ref[:, local_points - LEAF :]
    last_ref[width_e:, :] = values[:, local_points - LEAF :]
    for level in range(dev_bits):
        part_ref[level] = nt_dot(values, basis_ref[level])
    me = lax.axis_index("leaf") * sub_size + lax.axis_index("sub")

    def one(target, carry):
        other = jnp.bitwise_xor(target, me)
        level = top_bit(jnp.maximum(other, 1), dev_bits)
        out_ref[target] = part_ref[level]
        return carry

    lax.fori_loop(0, ndev, one, 0)


def main_kernel(
    sub_size, dev_bits, ndev, loc_bits,
    emb_ref, dirs_ref, left_ref, right_ref, basis_ref, incoming_ref, neighbours_ref, counts_ref,
    out_ref, sibling_ref,
):
    width_e = emb_ref.shape[0]
    local_points = emb_ref.shape[1]
    local_leaves = local_points // LEAF
    rank = basis_ref.shape[1]
    slots = neighbours_ref.shape[1]
    me = lax.axis_index("leaf") * sub_size + lax.axis_index("sub")

    directions = dirs_ref[...]
    values = directions.astype(jnp.bfloat16)
    emb_float = emb_ref[...].astype(jnp.float32)
    row_norms = jnp.sum(emb_float * emb_float, axis=0, keepdims=True)
    emb_t = emb_float.T
    col_norms = jnp.sum(emb_t * emb_t, axis=1, keepdims=True)
    emb_t = emb_t.astype(jnp.bfloat16)

    def block(j, source_points, source_norms):
        inner = nn_dot(emb_t[j * LEAF : (j + 1) * LEAF], source_points)
        distance = col_norms[j * LEAF : (j + 1) * LEAF] + source_norms - 2.0 * inner
        return (AMPLITUDE * jnp.exp(-DISTANCE_SCALE * distance)).astype(jnp.bfloat16)

    def weight(j, offset):
        leaf = me * local_leaves + j
        total = jnp.int32(0)
        for slot in range(slots):
            hit = (slot < counts_ref[j]) & (neighbours_ref[j, slot] == leaf + offset)
            total = total + hit.astype(jnp.int32)
        return total.astype(jnp.float32)

    points = [emb_ref[:, j * LEAF : (j + 1) * LEAF] for j in range(local_leaves)]
    norms = [row_norms[:, j * LEAF : (j + 1) * LEAF] for j in range(local_leaves)]
    leaf_values = [values[:, j * LEAF : (j + 1) * LEAF] for j in range(local_leaves)]
    near = [nt_dot(leaf_values[j], block(j, points[j], norms[j])) for j in range(local_leaves)]
    for j in range(local_leaves - 1):
        pair = block(j, points[j + 1], norms[j + 1])
        near[j] = near[j] + weight(j, 1) * nt_dot(leaf_values[j + 1], pair)
        near[j + 1] = near[j + 1] + weight(j + 1, -1) * nn_dot(leaf_values[j], pair)
    for j, halo_ref, offset in ((0, left_ref, -1), (local_leaves - 1, right_ref, 1)):
        halo_points = halo_ref[:width_e, :]
        halo_float = halo_points.astype(jnp.float32)
        halo_norms = jnp.sum(halo_float * halo_float, axis=0, keepdims=True)
        lower = block(j, halo_points, halo_norms)
        near[j] = near[j] + weight(j, offset) * nt_dot(halo_ref[width_e:, :], lower)

    sibling_ref[...] = jnp.zeros_like(sibling_ref)

    def gather(source, carry):
        other = jnp.bitwise_xor(source, me)
        level = top_bit(jnp.maximum(other, 1), dev_bits)

        @pl.when(other > 0)
        def _():
            sibling_ref[level] = sibling_ref[level] + incoming_ref[source]

        return carry

    lax.fori_loop(0, ndev, gather, 0)

    far = jnp.zeros((values.shape[0], local_points), jnp.float32)
    for bit in range(dev_bits):
        factor = 1.0 / math.sqrt(rank * local_points * 2**bit)
        scaled = (sibling_ref[bit] * factor).astype(jnp.bfloat16)
        far = far + nn_dot(scaled, basis_ref[loc_bits + bit])

    basis0 = basis_ref[0]
    coeffs = [nt_dot(leaf_values[q], basis0[:, q * LEAF : (q + 1) * LEAF]) for q in range(local_leaves)]
    factor0 = 1.0 / math.sqrt(rank * LEAF)
    scaled0 = [(c * factor0).astype(jnp.bfloat16) for c in coeffs]
    for q in range(local_leaves):
        near[q] = near[q] + nn_dot(scaled0[q ^ 1], basis0[:, q * LEAF : (q + 1) * LEAF])
    for j in range(local_leaves):
        out_ref[:, j * LEAF : (j + 1) * LEAF] = (
            RIDGE * directions[:, j * LEAF : (j + 1) * LEAF] + near[j] + far[:, j * LEAF : (j + 1) * LEAF]
        )


def on_device(embeddings, directions, level_basis, neighbours, counts):
    axes = ("leaf", "sub")
    width_e = embeddings.shape[0]
    local_points = embeddings.shape[1]
    rank = level_basis.shape[1]
    nrhs = directions.shape[0]
    sub_size = lax.axis_size("sub")
    leaf_size = lax.axis_size("leaf")
    ndev = sub_size * leaf_size
    dev_bits = ndev.bit_length() - 1
    loc_bits = level_basis.shape[0] - dev_bits

    halo = jax.ShapeDtypeStruct((width_e + nrhs, LEAF), jnp.bfloat16)
    first, last, outgoing = pl.pallas_call(
        functools.partial(send_kernel, sub_size, dev_bits, ndev),
        out_shape=(halo, halo, jax.ShapeDtypeStruct((ndev, nrhs, rank), jnp.float32)),
        in_specs=[VMEM, VMEM, VMEM],
        out_specs=(VMEM, VMEM, VMEM),
        scratch_shapes=[pltpu.VMEM((dev_bits, nrhs, rank), jnp.float32)],
    )(embeddings, directions, level_basis[loc_bits:])

    from_left = shifted(last, axes, 1)
    from_right = shifted(first, axes, -1)
    incoming = lax.all_to_all(outgoing, axes, 0, 0, tiled=True)

    return pl.pallas_call(
        functools.partial(main_kernel, sub_size, dev_bits, ndev, loc_bits),
        out_shape=jax.ShapeDtypeStruct((nrhs, local_points), jnp.float32),
        in_specs=[VMEM, VMEM, VMEM, VMEM, VMEM, VMEM, SMEM, SMEM],
        out_specs=VMEM,
        scratch_shapes=[pltpu.VMEM((dev_bits, nrhs, rank), jnp.float32)],
    )(embeddings, directions, from_left, from_right, level_basis, incoming, neighbours, counts)


def solution(mesh):
    placed = (
        P(None, ("groups", "leaf", "sub")),
        P(None, ("groups", "leaf", "sub")),
        P(None, None, ("groups", "leaf", "sub")),
        P(("groups", "leaf", "sub"), None),
        P(("groups", "leaf", "sub")),
    )
    return jax.shard_map(
        on_device,
        mesh=mesh,
        in_specs=placed,
        out_specs=P(None, ("groups", "leaf", "sub")),
        check_vma=False,
    )
```

```python
import functools
import math

import jax
import jax.numpy as jnp
from jax import lax
from jax.experimental import pallas as pl
from jax.experimental.pallas import tpu as pltpu
from jax.sharding import PartitionSpec as P

LEAF = 512


AMPLITUDE = 0.5
DISTANCE_SCALE = 0.125
RIDGE = 0.5

VMEM = pl.BlockSpec(memory_space=pltpu.VMEM)
SMEM = pl.BlockSpec(memory_space=pltpu.SMEM)


def shifted(x, axis, step):
    count = lax.axis_size(axis)
    if step > 0:
        pairs = [(i, i + step) for i in range(count - step)]
    else:
        pairs = [(i - step, i) for i in range(count + step)]
    return lax.ppermute(x, axis, pairs)


def top_bit(x, dev_bits):
    level = jnp.int32(0)
    for bit in range(1, dev_bits):
        level = level + (x >= 2**bit).astype(jnp.int32)
    return level


def nt_dot(a, b):
    return lax.dot_general(a, b, (((1,), (1,)), ((), ())), preferred_element_type=jnp.float32)


def nn_dot(a, b):
    return lax.dot_general(a, b, (((1,), (0,)), ((), ())), preferred_element_type=jnp.float32)


def send_kernel(loc_bits, emb_ref, dirs_ref, basis_ref, first_ref, last_ref, part_ref):
    width_e = emb_ref.shape[0]
    local_points = emb_ref.shape[1]
    values = dirs_ref[...].astype(jnp.bfloat16)
    first_ref[:width_e, :] = emb_ref[:, :LEAF]
    first_ref[width_e:, :] = values[:, :LEAF]
    last_ref[:width_e, :] = emb_ref[:, local_points - LEAF :]
    last_ref[width_e:, :] = values[:, local_points - LEAF :]
    for level in range(part_ref.shape[0]):
        part_ref[level] = nt_dot(values, basis_ref[loc_bits + level])


def main_kernel(
    sub_size, dev_bits, ndev, loc_bits,
    emb_ref, dirs_ref, left_ref, right_ref, basis_ref, incoming_ref, neighbours_ref, counts_ref,
    out_ref, sibling_ref,
):
    width_e = emb_ref.shape[0]
    local_points = emb_ref.shape[1]
    local_leaves = local_points // LEAF
    rank = basis_ref.shape[1]
    slots = neighbours_ref.shape[1]
    me = lax.axis_index("leaf") * sub_size + lax.axis_index("sub")

    directions = dirs_ref[...]
    values = directions.astype(jnp.bfloat16)
    emb_float = emb_ref[...].astype(jnp.float32)
    row_norms = jnp.sum(emb_float * emb_float, axis=0, keepdims=True)
    emb_t = emb_float.T
    col_norms = jnp.sum(emb_t * emb_t, axis=1, keepdims=True)
    emb_t = emb_t.astype(jnp.bfloat16)

    def block(j, source_points, source_norms):
        inner = nn_dot(emb_t[j * LEAF : (j + 1) * LEAF], source_points)
        distance = col_norms[j * LEAF : (j + 1) * LEAF] + source_norms - 2.0 * inner
        return (AMPLITUDE * jnp.exp(-DISTANCE_SCALE * distance)).astype(jnp.bfloat16)

    def weight(j, offset):
        leaf = me * local_leaves + j
        total = jnp.int32(0)
        for slot in range(slots):
            hit = (slot < counts_ref[j]) & (neighbours_ref[j, slot] == leaf + offset)
            total = total + hit.astype(jnp.int32)
        return total.astype(jnp.float32)

    points = [emb_ref[:, j * LEAF : (j + 1) * LEAF] for j in range(local_leaves)]
    norms = [row_norms[:, j * LEAF : (j + 1) * LEAF] for j in range(local_leaves)]
    leaf_values = [values[:, j * LEAF : (j + 1) * LEAF] for j in range(local_leaves)]
    near = [nt_dot(leaf_values[j], block(j, points[j], norms[j])) for j in range(local_leaves)]
    for j in range(local_leaves - 1):
        pair = block(j, points[j + 1], norms[j + 1])
        near[j] = near[j] + weight(j, 1) * nt_dot(leaf_values[j + 1], pair)
        near[j + 1] = near[j + 1] + weight(j + 1, -1) * nn_dot(leaf_values[j], pair)
    for j, halo_ref, offset in ((0, left_ref, -1), (local_leaves - 1, right_ref, 1)):
        halo_points = halo_ref[:width_e, :]
        halo_float = halo_points.astype(jnp.float32)
        halo_norms = jnp.sum(halo_float * halo_float, axis=0, keepdims=True)
        lower = block(j, halo_points, halo_norms)
        near[j] = near[j] + weight(j, offset) * nt_dot(halo_ref[width_e:, :], lower)

    sibling_ref[...] = jnp.zeros_like(sibling_ref)

    def gather(source, carry):
        other = jnp.bitwise_xor(source, me)
        level = top_bit(jnp.maximum(other, 1), dev_bits)

        @pl.when(other > 0)
        def _():
            sibling_ref[level] = sibling_ref[level] + incoming_ref[source, level]

        return carry

    lax.fori_loop(0, ndev, gather, 0)

    far = jnp.zeros((values.shape[0], local_points), jnp.float32)
    for bit in range(dev_bits):
        factor = 1.0 / math.sqrt(rank * local_points * 2**bit)
        scaled = (sibling_ref[bit] * factor).astype(jnp.bfloat16)
        far = far + nn_dot(scaled, basis_ref[loc_bits + bit])

    basis0 = basis_ref[0]
    coeffs = [nt_dot(leaf_values[q], basis0[:, q * LEAF : (q + 1) * LEAF]) for q in range(local_leaves)]
    factor0 = 1.0 / math.sqrt(rank * LEAF)
    scaled0 = [(c * factor0).astype(jnp.bfloat16) for c in coeffs]
    for q in range(local_leaves):
        near[q] = near[q] + nn_dot(scaled0[q ^ 1], basis0[:, q * LEAF : (q + 1) * LEAF])
    for j in range(local_leaves):
        out_ref[:, j * LEAF : (j + 1) * LEAF] = (
            RIDGE * directions[:, j * LEAF : (j + 1) * LEAF] + near[j] + far[:, j * LEAF : (j + 1) * LEAF]
        )


def on_device(embeddings, directions, level_basis, neighbours, counts):
    axes = ("leaf", "sub")
    width_e = embeddings.shape[0]
    local_points = embeddings.shape[1]
    rank = level_basis.shape[1]
    nrhs = directions.shape[0]
    sub_size = lax.axis_size("sub")
    leaf_size = lax.axis_size("leaf")
    ndev = sub_size * leaf_size
    dev_bits = ndev.bit_length() - 1
    loc_bits = level_basis.shape[0] - dev_bits

    halo = jax.ShapeDtypeStruct((width_e + nrhs, LEAF), jnp.bfloat16)
    first, last, partials = pl.pallas_call(
        functools.partial(send_kernel, loc_bits),
        out_shape=(halo, halo, jax.ShapeDtypeStruct((dev_bits, nrhs, rank), jnp.float32)),
        in_specs=[VMEM, VMEM, VMEM],
        out_specs=(VMEM, VMEM, VMEM),
    )(embeddings, directions, level_basis)

    from_left = shifted(last, axes, 1)
    from_right = shifted(first, axes, -1)
    incoming = lax.all_gather(partials, axes, axis=0, tiled=False)

    return pl.pallas_call(
        functools.partial(main_kernel, sub_size, dev_bits, ndev, loc_bits),
        out_shape=jax.ShapeDtypeStruct((nrhs, local_points), jnp.float32),
        in_specs=[VMEM, VMEM, VMEM, VMEM, VMEM, VMEM, SMEM, SMEM],
        out_specs=VMEM,
        scratch_shapes=[pltpu.VMEM((dev_bits, nrhs, rank), jnp.float32)],
    )(embeddings, directions, from_left, from_right, level_basis, incoming, neighbours, counts)


def solution(mesh):
    placed = (
        P(None, ("groups", "leaf", "sub")),
        P(None, ("groups", "leaf", "sub")),
        P(None, None, ("groups", "leaf", "sub")),
        P(("groups", "leaf", "sub"), None),
        P(("groups", "leaf", "sub")),
    )
    return jax.shard_map(
        on_device,
        mesh=mesh,
        in_specs=placed,
        out_specs=P(None, ("groups", "leaf", "sub")),
        check_vma=False,
    )
```

```python
import functools
import math

import jax
import jax.numpy as jnp
from jax import lax
from jax.experimental import pallas as pl
from jax.experimental.pallas import tpu as pltpu
from jax.sharding import PartitionSpec as P

LEAF = 512


AMPLITUDE = 0.5
DISTANCE_SCALE = 0.125
RIDGE = 0.5

VMEM = pl.BlockSpec(memory_space=pltpu.VMEM)
SMEM = pl.BlockSpec(memory_space=pltpu.SMEM)


def shifted(x, axis, step):
    count = lax.axis_size(axis)
    if step > 0:
        pairs = [(i, i + step) for i in range(count - step)]
    else:
        pairs = [(i - step, i) for i in range(count + step)]
    return lax.ppermute(x, axis, pairs)


def from_mask(x, axis, mask):
    pairs = [(i, i ^ mask) for i in range(lax.axis_size(axis))]
    return lax.ppermute(x, axis, pairs)


def nt_dot(a, b):
    return lax.dot_general(a, b, (((1,), (1,)), ((), ())), preferred_element_type=jnp.float32)


def nn_dot(a, b):
    return lax.dot_general(a, b, (((1,), (0,)), ((), ())), preferred_element_type=jnp.float32)


def send_kernel(loc_bits, sub_bits, emb_ref, dirs_ref, basis_ref, first_ref, last_ref, upper_ref, *payload_refs):
    width_e = emb_ref.shape[0]
    local_points = emb_ref.shape[1]
    values = dirs_ref[...].astype(jnp.bfloat16)
    first_ref[:width_e, :] = emb_ref[:, :LEAF]
    first_ref[width_e:, :] = values[:, :LEAF]
    last_ref[:width_e, :] = emb_ref[:, local_points - LEAF :]
    last_ref[width_e:, :] = values[:, local_points - LEAF :]
    for level in range(upper_ref.shape[0]):
        part = nt_dot(values, basis_ref[loc_bits + sub_bits + level])
        upper_ref[level] = part
        for payload_ref in payload_refs:
            payload_ref[1 + level] = part
    for level, payload_ref in enumerate(payload_refs):
        payload_ref[0] = nt_dot(values, basis_ref[loc_bits + level])


class Leaves:
    def __init__(self, emb_ref, dirs_ref, neighbours_ref, counts_ref, sub_size):
        self.width_e = emb_ref.shape[0]
        self.local_points = emb_ref.shape[1]
        self.count = self.local_points // LEAF
        self.directions = dirs_ref[...]
        self.values = self.directions.astype(jnp.bfloat16)
        emb_float = emb_ref[...].astype(jnp.float32)
        row_norms = jnp.sum(emb_float * emb_float, axis=0, keepdims=True)
        emb_t = emb_float.T
        self.col_norms = jnp.sum(emb_t * emb_t, axis=1, keepdims=True)
        self.emb_t = emb_t.astype(jnp.bfloat16)
        self.points = [emb_ref[:, j * LEAF : (j + 1) * LEAF] for j in range(self.count)]
        self.norms = [row_norms[:, j * LEAF : (j + 1) * LEAF] for j in range(self.count)]
        self.leaf_values = [self.values[:, j * LEAF : (j + 1) * LEAF] for j in range(self.count)]
        self.neighbours_ref = neighbours_ref
        self.counts_ref = counts_ref
        self.me = lax.axis_index("leaf") * sub_size + lax.axis_index("sub")

    def block(self, j, source_points, source_norms):
        inner = nn_dot(self.emb_t[j * LEAF : (j + 1) * LEAF], source_points)
        distance = self.col_norms[j * LEAF : (j + 1) * LEAF] + source_norms - 2.0 * inner
        return (AMPLITUDE * jnp.exp(-DISTANCE_SCALE * distance)).astype(jnp.bfloat16)

    def weight(self, j, offset):
        leaf = self.me * self.count + j
        total = jnp.int32(0)
        for slot in range(self.neighbours_ref.shape[1]):
            hit = (slot < self.counts_ref[j]) & (self.neighbours_ref[j, slot] == leaf + offset)
            total = total + hit.astype(jnp.int32)
        return total.astype(jnp.float32)


def local_kernel(sub_size, emb_ref, dirs_ref, basis_ref, neighbours_ref, counts_ref, out_ref):
    lv = Leaves(emb_ref, dirs_ref, neighbours_ref, counts_ref, sub_size)
    rank = basis_ref.shape[1]
    near = [nt_dot(lv.leaf_values[j], lv.block(j, lv.points[j], lv.norms[j])) for j in range(lv.count)]
    for j in range(lv.count - 1):
        pair = lv.block(j, lv.points[j + 1], lv.norms[j + 1])
        near[j] = near[j] + lv.weight(j, 1) * nt_dot(lv.leaf_values[j + 1], pair)
        near[j + 1] = near[j + 1] + lv.weight(j + 1, -1) * nn_dot(lv.leaf_values[j], pair)
    basis0 = basis_ref[0]
    factor0 = 1.0 / math.sqrt(rank * LEAF)
    scaled0 = [
        (nt_dot(lv.leaf_values[q], basis0[:, q * LEAF : (q + 1) * LEAF]) * factor0).astype(jnp.bfloat16)
        for q in range(lv.count)
    ]
    for q in range(lv.count):
        far0 = nn_dot(scaled0[q ^ 1], basis0[:, q * LEAF : (q + 1) * LEAF])
        out_ref[:, q * LEAF : (q + 1) * LEAF] = (
            RIDGE * lv.directions[:, q * LEAF : (q + 1) * LEAF] + near[q] + far0
        )


def final_kernel(sub_size, sub_bits, leaf_bits, loc_bits, *refs):
    sub_masks = 2**sub_bits - 1
    leaf_masks = 2**leaf_bits - 1
    emb_ref, dirs_ref, local_ref, left_ref, right_ref, basis_ref, neighbours_ref, counts_ref = refs[:8]
    round_one = refs[8 : 8 + sub_masks]
    round_two = refs[8 + sub_masks : 8 + sub_masks + leaf_masks]
    out_ref = refs[8 + sub_masks + leaf_masks]
    lv = Leaves(emb_ref, dirs_ref, neighbours_ref, counts_ref, sub_size)
    rank = basis_ref.shape[1]
    local_points = lv.local_points

    sibling = [None] * (sub_bits + leaf_bits)
    line = None
    for mask, got_ref in enumerate(round_one, start=1):
        level = mask.bit_length() - 1
        got = got_ref[0]
        sibling[level] = got if sibling[level] is None else sibling[level] + got
    for mask, got_ref in enumerate(round_two, start=1):
        level = sub_bits + mask.bit_length() - 1
        got = got_ref[level - sub_bits]
        sibling[level] = got if sibling[level] is None else sibling[level] + got

    far = None
    for bit in range(sub_bits + leaf_bits):
        factor = 1.0 / math.sqrt(rank * local_points * 2**bit)
        scaled = (sibling[bit] * factor).astype(jnp.bfloat16)
        term = nn_dot(scaled, basis_ref[loc_bits + bit])
        far = term if far is None else far + term

    halo = {}
    for j, halo_ref, offset in ((0, left_ref, -1), (lv.count - 1, right_ref, 1)):
        halo_points = halo_ref[: lv.width_e, :]
        halo_float = halo_points.astype(jnp.float32)
        halo_norms = jnp.sum(halo_float * halo_float, axis=0, keepdims=True)
        weights = lv.block(j, halo_points, halo_norms)
        term = lv.weight(j, offset) * nt_dot(halo_ref[lv.width_e :, :], weights)
        halo[j] = term if j not in halo else halo[j] + term
    for j in range(lv.count):
        total = local_ref[:, j * LEAF : (j + 1) * LEAF] + far[:, j * LEAF : (j + 1) * LEAF]
        if j in halo:
            total = total + halo[j]
        out_ref[:, j * LEAF : (j + 1) * LEAF] = total


def on_device(embeddings, directions, level_basis, neighbours, counts):
    axes = ("leaf", "sub")
    width_e = embeddings.shape[0]
    local_points = embeddings.shape[1]
    rank = level_basis.shape[1]
    nrhs = directions.shape[0]
    sub_size = lax.axis_size("sub")
    leaf_size = lax.axis_size("leaf")
    sub_bits = sub_size.bit_length() - 1
    leaf_bits = leaf_size.bit_length() - 1
    dev_bits = sub_bits + leaf_bits
    loc_bits = level_basis.shape[0] - dev_bits

    halo = jax.ShapeDtypeStruct((width_e + nrhs, LEAF), jnp.bfloat16)
    upper = jax.ShapeDtypeStruct((leaf_bits, nrhs, rank), jnp.float32)
    payload = jax.ShapeDtypeStruct((1 + leaf_bits, nrhs, rank), jnp.float32)
    first, last, upper_own, *payloads = pl.pallas_call(
        functools.partial(send_kernel, loc_bits, sub_bits),
        out_shape=(halo, halo, upper) + (payload,) * sub_bits,
        in_specs=[VMEM, VMEM, VMEM],
        out_specs=(VMEM,) * (3 + sub_bits),
    )(embeddings, directions, level_basis)

    from_left = shifted(last, axes, 1)
    from_right = shifted(first, axes, -1)
    round_one = [from_mask(payloads[mask.bit_length() - 1], "sub", mask) for mask in range(1, sub_size)]
    line = upper_own
    for got in round_one:
        line = line + got[1:]
    round_two = [from_mask(line, "leaf", mask) for mask in range(1, leaf_size)]

    out = jax.ShapeDtypeStruct((nrhs, local_points), jnp.float32)
    local = pl.pallas_call(
        functools.partial(local_kernel, sub_size),
        out_shape=out,
        in_specs=[VMEM, VMEM, VMEM, SMEM, SMEM],
        out_specs=VMEM,
    )(embeddings, directions, level_basis, neighbours, counts)

    remote = round_one + round_two
    return pl.pallas_call(
        functools.partial(final_kernel, sub_size, sub_bits, leaf_bits, loc_bits),
        out_shape=out,
        in_specs=[VMEM] * 6 + [SMEM, SMEM] + [VMEM] * len(remote),
        out_specs=VMEM,
        input_output_aliases={2: 0},
    )(embeddings, directions, local, from_left, from_right, level_basis, neighbours, counts, *remote)


def solution(mesh):
    placed = (
        P(None, ("groups", "leaf", "sub")),
        P(None, ("groups", "leaf", "sub")),
        P(None, None, ("groups", "leaf", "sub")),
        P(("groups", "leaf", "sub"), None),
        P(("groups", "leaf", "sub")),
    )
    return jax.shard_map(
        on_device,
        mesh=mesh,
        in_specs=placed,
        out_specs=P(None, ("groups", "leaf", "sub")),
        check_vma=False,
    )
```

```python
import functools
import math

import jax
import jax.numpy as jnp
from jax import lax
from jax.experimental import pallas as pl
from jax.experimental.pallas import tpu as pltpu
from jax.sharding import PartitionSpec as P

LEAF = 512


AMPLITUDE = 0.5
DISTANCE_SCALE = 0.125
RIDGE = 0.5

VMEM = pl.BlockSpec(memory_space=pltpu.VMEM)
SMEM = pl.BlockSpec(memory_space=pltpu.SMEM)


def from_mask(x, axis, mask):
    pairs = [(i, i ^ mask) for i in range(lax.axis_size(axis))]
    return lax.ppermute(x, axis, pairs)


def nt_dot(a, b):
    return lax.dot_general(a, b, (((1,), (1,)), ((), ())), preferred_element_type=jnp.float32)


def nn_dot(a, b):
    return lax.dot_general(a, b, (((1,), (0,)), ((), ())), preferred_element_type=jnp.float32)


def send_kernel(loc_bits, sub_bits, emb_ref, dirs_ref, basis_ref, first_ref, last_ref, upper_ref, *payload_refs):
    width_e = emb_ref.shape[0]
    local_points = emb_ref.shape[1]
    values = dirs_ref[...].astype(jnp.bfloat16)
    even = lax.axis_index("sub") % 2 == 0
    head_points, tail_points = emb_ref[:, :LEAF], emb_ref[:, local_points - LEAF :]
    head_values, tail_values = values[:, :LEAF], values[:, local_points - LEAF :]
    first_ref[:width_e, :] = jnp.where(even, tail_points, head_points)
    first_ref[width_e:, :] = jnp.where(even, tail_values, head_values)
    last_ref[:width_e, :] = jnp.where(even, head_points, tail_points)
    last_ref[width_e:, :] = jnp.where(even, head_values, tail_values)
    for level in range(upper_ref.shape[0]):
        part = nt_dot(values, basis_ref[loc_bits + sub_bits + level])
        upper_ref[level] = part
        for payload_ref in payload_refs:
            payload_ref[1 + level] = part
    for level, payload_ref in enumerate(payload_refs):
        payload_ref[0] = nt_dot(values, basis_ref[loc_bits + level])


class Leaves:
    def __init__(self, emb_ref, dirs_ref, neighbours_ref, counts_ref, sub_size):
        self.width_e = emb_ref.shape[0]
        self.local_points = emb_ref.shape[1]
        self.count = self.local_points // LEAF
        self.directions = dirs_ref[...]
        self.values = self.directions.astype(jnp.bfloat16)
        emb_float = emb_ref[...].astype(jnp.float32)
        row_norms = jnp.sum(emb_float * emb_float, axis=0, keepdims=True)
        emb_t = emb_float.T
        self.col_norms = jnp.sum(emb_t * emb_t, axis=1, keepdims=True)
        self.emb_t = emb_t.astype(jnp.bfloat16)
        self.points = [emb_ref[:, j * LEAF : (j + 1) * LEAF] for j in range(self.count)]
        self.norms = [row_norms[:, j * LEAF : (j + 1) * LEAF] for j in range(self.count)]
        self.leaf_values = [self.values[:, j * LEAF : (j + 1) * LEAF] for j in range(self.count)]
        self.neighbours_ref = neighbours_ref
        self.counts_ref = counts_ref
        self.me = lax.axis_index("leaf") * sub_size + lax.axis_index("sub")

    def block(self, j, source_points, source_norms):
        inner = nn_dot(self.emb_t[j * LEAF : (j + 1) * LEAF], source_points)
        distance = self.col_norms[j * LEAF : (j + 1) * LEAF] + source_norms - 2.0 * inner
        return (AMPLITUDE * jnp.exp(-DISTANCE_SCALE * distance)).astype(jnp.bfloat16)

    def weight(self, j, offset):
        leaf = self.me * self.count + j
        total = jnp.int32(0)
        for slot in range(self.neighbours_ref.shape[1]):
            hit = (slot < self.counts_ref[j]) & (self.neighbours_ref[j, slot] == leaf + offset)
            total = total + hit.astype(jnp.int32)
        return total.astype(jnp.float32)


def local_kernel(sub_size, emb_ref, dirs_ref, basis_ref, neighbours_ref, counts_ref, out_ref):
    lv = Leaves(emb_ref, dirs_ref, neighbours_ref, counts_ref, sub_size)
    rank = basis_ref.shape[1]
    near = [nt_dot(lv.leaf_values[j], lv.block(j, lv.points[j], lv.norms[j])) for j in range(lv.count)]
    for j in range(lv.count - 1):
        pair = lv.block(j, lv.points[j + 1], lv.norms[j + 1])
        near[j] = near[j] + lv.weight(j, 1) * nt_dot(lv.leaf_values[j + 1], pair)
        near[j + 1] = near[j + 1] + lv.weight(j + 1, -1) * nn_dot(lv.leaf_values[j], pair)
    basis0 = basis_ref[0]
    factor0 = 1.0 / math.sqrt(rank * LEAF)
    scaled0 = [
        (nt_dot(lv.leaf_values[q], basis0[:, q * LEAF : (q + 1) * LEAF]) * factor0).astype(jnp.bfloat16)
        for q in range(lv.count)
    ]
    for q in range(lv.count):
        far0 = nn_dot(scaled0[q ^ 1], basis0[:, q * LEAF : (q + 1) * LEAF])
        out_ref[:, q * LEAF : (q + 1) * LEAF] = (
            RIDGE * lv.directions[:, q * LEAF : (q + 1) * LEAF] + near[q] + far0
        )


def final_kernel(sub_size, sub_bits, leaf_bits, loc_bits, *refs):
    sub_masks = 2**sub_bits - 1
    leaf_masks = 2**leaf_bits - 1
    emb_ref, dirs_ref, local_ref, pair_ref, cross_ref, basis_ref, neighbours_ref, counts_ref = refs[:8]
    round_one = refs[8 : 8 + sub_masks]
    round_two = refs[8 + sub_masks : 8 + sub_masks + leaf_masks]
    out_ref = refs[8 + sub_masks + leaf_masks]
    lv = Leaves(emb_ref, dirs_ref, neighbours_ref, counts_ref, sub_size)
    rank = basis_ref.shape[1]
    local_points = lv.local_points

    sibling = [None] * (sub_bits + leaf_bits)
    line = None
    for mask, got_ref in enumerate(round_one, start=1):
        level = mask.bit_length() - 1
        got = got_ref[0]
        sibling[level] = got if sibling[level] is None else sibling[level] + got
    for mask, got_ref in enumerate(round_two, start=1):
        level = sub_bits + mask.bit_length() - 1
        got = got_ref[level - sub_bits]
        sibling[level] = got if sibling[level] is None else sibling[level] + got

    far = None
    for bit in range(sub_bits + leaf_bits):
        factor = 1.0 / math.sqrt(rank * local_points * 2**bit)
        scaled = (sibling[bit] * factor).astype(jnp.bfloat16)
        term = nn_dot(scaled, basis_ref[loc_bits + bit])
        far = term if far is None else far + term

    even = lax.axis_index("sub") % 2 == 0
    pair, cross = pair_ref[...], cross_ref[...]
    left, right = jnp.where(even, cross, pair), jnp.where(even, pair, cross)
    halo = {}
    for j, received, offset in ((0, left, -1), (lv.count - 1, right, 1)):
        halo_points = received[: lv.width_e, :]
        halo_float = halo_points.astype(jnp.float32)
        halo_norms = jnp.sum(halo_float * halo_float, axis=0, keepdims=True)
        weights = lv.block(j, halo_points, halo_norms)
        term = lv.weight(j, offset) * nt_dot(received[lv.width_e :, :], weights)
        halo[j] = term if j not in halo else halo[j] + term
    for j in range(lv.count):
        total = local_ref[:, j * LEAF : (j + 1) * LEAF] + far[:, j * LEAF : (j + 1) * LEAF]
        if j in halo:
            total = total + halo[j]
        out_ref[:, j * LEAF : (j + 1) * LEAF] = total


def on_device(embeddings, directions, level_basis, neighbours, counts):
    axes = ("leaf", "sub")
    width_e = embeddings.shape[0]
    local_points = embeddings.shape[1]
    rank = level_basis.shape[1]
    nrhs = directions.shape[0]
    sub_size = lax.axis_size("sub")
    leaf_size = lax.axis_size("leaf")
    sub_bits = sub_size.bit_length() - 1
    leaf_bits = leaf_size.bit_length() - 1
    dev_bits = sub_bits + leaf_bits
    loc_bits = level_basis.shape[0] - dev_bits

    halo = jax.ShapeDtypeStruct((width_e + nrhs, LEAF), jnp.bfloat16)
    upper = jax.ShapeDtypeStruct((leaf_bits, nrhs, rank), jnp.float32)
    payload = jax.ShapeDtypeStruct((1 + leaf_bits, nrhs, rank), jnp.float32)
    first, last, upper_own, *payloads = pl.pallas_call(
        functools.partial(send_kernel, loc_bits, sub_bits),
        out_shape=(halo, halo, upper) + (payload,) * sub_bits,
        in_specs=[VMEM, VMEM, VMEM],
        out_specs=(VMEM,) * (3 + sub_bits),
    )(embeddings, directions, level_basis)

    ndev = sub_size * leaf_size
    from_pair = lax.ppermute(first, axes, [(i, i ^ 1) for i in range(ndev)])
    from_cross = lax.ppermute(last, axes, [(i, i - 1 + 2 * (i % 2)) for i in range(1, ndev - 1)])
    round_one = [from_mask(payloads[mask.bit_length() - 1], "sub", mask) for mask in range(1, sub_size)]
    line = upper_own
    for got in round_one:
        line = line + got[1:]
    round_two = [from_mask(line, "leaf", mask) for mask in range(1, leaf_size)]

    out = jax.ShapeDtypeStruct((nrhs, local_points), jnp.float32)
    local = pl.pallas_call(
        functools.partial(local_kernel, sub_size),
        out_shape=out,
        in_specs=[VMEM, VMEM, VMEM, SMEM, SMEM],
        out_specs=VMEM,
    )(embeddings, directions, level_basis, neighbours, counts)

    remote = round_one + round_two
    return pl.pallas_call(
        functools.partial(final_kernel, sub_size, sub_bits, leaf_bits, loc_bits),
        out_shape=out,
        in_specs=[VMEM] * 6 + [SMEM, SMEM] + [VMEM] * len(remote),
        out_specs=VMEM,
        input_output_aliases={2: 0},
    )(embeddings, directions, local, from_pair, from_cross, level_basis, neighbours, counts, *remote)


def solution(mesh):
    placed = (
        P(None, ("groups", "leaf", "sub")),
        P(None, ("groups", "leaf", "sub")),
        P(None, None, ("groups", "leaf", "sub")),
        P(("groups", "leaf", "sub"), None),
        P(("groups", "leaf", "sub")),
    )
    return jax.shard_map(
        on_device,
        mesh=mesh,
        in_specs=placed,
        out_specs=P(None, ("groups", "leaf", "sub")),
        check_vma=False,
    )
```

```python
import functools
import math

import jax
import jax.numpy as jnp
from jax import lax
from jax.experimental import pallas as pl
from jax.experimental.pallas import tpu as pltpu
from jax.sharding import PartitionSpec as P

LEAF = 512


AMPLITUDE = 0.5
DISTANCE_SCALE = 0.125
RIDGE = 0.5

VMEM = pl.BlockSpec(memory_space=pltpu.VMEM)
SMEM = pl.BlockSpec(memory_space=pltpu.SMEM)


def from_mask(x, axis, mask):
    pairs = [(i, i ^ mask) for i in range(lax.axis_size(axis))]
    return lax.ppermute(x, axis, pairs)


def nt_dot(a, b):
    return lax.dot_general(a, b, (((1,), (1,)), ((), ())), preferred_element_type=jnp.float32)


def nn_dot(a, b):
    return lax.dot_general(a, b, (((1,), (0,)), ((), ())), preferred_element_type=jnp.float32)


def send_kernel(loc_bits, sub_bits, emb_ref, dirs_ref, basis_ref, first_ref, last_ref, upper_ref, *payload_refs):
    width_e = emb_ref.shape[0]
    local_points = emb_ref.shape[1]
    values = dirs_ref[...].astype(jnp.bfloat16)
    even = lax.axis_index("sub") % 2 == 0
    head_points, tail_points = emb_ref[:, :LEAF], emb_ref[:, local_points - LEAF :]
    head_values, tail_values = values[:, :LEAF], values[:, local_points - LEAF :]
    first_ref[:width_e, :] = jnp.where(even, tail_points, head_points)
    first_ref[width_e:, :] = jnp.where(even, tail_values, head_values)
    last_ref[:width_e, :] = jnp.where(even, head_points, tail_points)
    last_ref[width_e:, :] = jnp.where(even, head_values, tail_values)
    for level in range(upper_ref.shape[0]):
        part = nt_dot(values, basis_ref[loc_bits + sub_bits + level])
        upper_ref[level] = part
        for payload_ref in payload_refs:
            payload_ref[1 + level] = part
    for level, payload_ref in enumerate(payload_refs):
        payload_ref[0] = nt_dot(values, basis_ref[loc_bits + level])


class Leaves:
    def __init__(self, emb_ref, dirs_ref, neighbours_ref, counts_ref, sub_size):
        self.width_e = emb_ref.shape[0]
        self.local_points = emb_ref.shape[1]
        self.count = self.local_points // LEAF
        self.directions = dirs_ref[...]
        self.values = self.directions.astype(jnp.bfloat16)
        emb_float = emb_ref[...].astype(jnp.float32)
        row_norms = jnp.sum(emb_float * emb_float, axis=0, keepdims=True)
        emb_t = emb_float.T
        self.col_norms = jnp.sum(emb_t * emb_t, axis=1, keepdims=True)
        self.emb_t = emb_t.astype(jnp.bfloat16)
        self.points = [emb_ref[:, j * LEAF : (j + 1) * LEAF] for j in range(self.count)]
        self.norms = [row_norms[:, j * LEAF : (j + 1) * LEAF] for j in range(self.count)]
        self.leaf_values = [self.values[:, j * LEAF : (j + 1) * LEAF] for j in range(self.count)]
        self.neighbours_ref = neighbours_ref
        self.counts_ref = counts_ref
        self.me = lax.axis_index("leaf") * sub_size + lax.axis_index("sub")

    def block(self, j, source_points, source_norms):
        inner = nn_dot(self.emb_t[j * LEAF : (j + 1) * LEAF], source_points)
        distance = self.col_norms[j * LEAF : (j + 1) * LEAF] + source_norms - 2.0 * inner
        return (AMPLITUDE * jnp.exp(-DISTANCE_SCALE * distance)).astype(jnp.bfloat16)

    def weight(self, j, offset):
        leaf = self.me * self.count + j
        total = jnp.int32(0)
        for slot in range(self.neighbours_ref.shape[1]):
            hit = (slot < self.counts_ref[j]) & (self.neighbours_ref[j, slot] == leaf + offset)
            total = total + hit.astype(jnp.int32)
        return total.astype(jnp.float32)


def local_kernel(sub_size, emb_ref, dirs_ref, basis_ref, neighbours_ref, counts_ref, out_ref):
    lv = Leaves(emb_ref, dirs_ref, neighbours_ref, counts_ref, sub_size)
    rank = basis_ref.shape[1]
    near = [nt_dot(lv.leaf_values[j], lv.block(j, lv.points[j], lv.norms[j])) for j in range(lv.count)]
    for j in range(lv.count - 1):
        pair = lv.block(j, lv.points[j + 1], lv.norms[j + 1])
        near[j] = near[j] + lv.weight(j, 1) * nt_dot(lv.leaf_values[j + 1], pair)
        near[j + 1] = near[j + 1] + lv.weight(j + 1, -1) * nn_dot(lv.leaf_values[j], pair)
    basis0 = basis_ref[0]
    factor0 = 1.0 / math.sqrt(rank * LEAF)
    scaled0 = [
        (nt_dot(lv.leaf_values[q], basis0[:, q * LEAF : (q + 1) * LEAF]) * factor0).astype(jnp.bfloat16)
        for q in range(lv.count)
    ]
    for q in range(lv.count):
        far0 = nn_dot(scaled0[q ^ 1], basis0[:, q * LEAF : (q + 1) * LEAF])
        out_ref[:, q * LEAF : (q + 1) * LEAF] = (
            RIDGE * lv.directions[:, q * LEAF : (q + 1) * LEAF] + near[q] + far0
        )


def final_kernel(sub_size, sub_bits, leaf_bits, loc_bits, *refs):
    sub_masks = 2**sub_bits - 1
    leaf_masks = 2**leaf_bits - 1
    emb_ref, dirs_ref, local_ref, pair_ref, cross_ref, basis_ref, neighbours_ref, counts_ref = refs[:8]
    round_one = refs[8 : 8 + sub_masks]
    round_two = refs[8 + sub_masks : 8 + sub_masks + leaf_masks]
    out_ref = refs[8 + sub_masks + leaf_masks]
    lv = Leaves(emb_ref, dirs_ref, neighbours_ref, counts_ref, sub_size)
    rank = basis_ref.shape[1]
    local_points = lv.local_points

    sibling = [None] * (sub_bits + leaf_bits)
    line = None
    for mask, got_ref in enumerate(round_one, start=1):
        level = mask.bit_length() - 1
        got = got_ref[0]
        sibling[level] = got if sibling[level] is None else sibling[level] + got
    for mask, got_ref in enumerate(round_two, start=1):
        level = sub_bits + mask.bit_length() - 1
        got = got_ref[level - sub_bits]
        sibling[level] = got if sibling[level] is None else sibling[level] + got

    far = None
    for bit in range(sub_bits + leaf_bits):
        factor = 1.0 / math.sqrt(rank * local_points * 2**bit)
        scaled = (sibling[bit] * factor).astype(jnp.bfloat16)
        term = nn_dot(scaled, basis_ref[loc_bits + bit])
        far = term if far is None else far + term

    even = lax.axis_index("sub") % 2 == 0
    pair, cross = pair_ref[...], cross_ref[...]
    left, right = jnp.where(even, cross, pair), jnp.where(even, pair, cross)
    halo = {}
    for j, received, offset in ((0, left, -1), (lv.count - 1, right, 1)):
        halo_points = received[: lv.width_e, :]
        halo_float = halo_points.astype(jnp.float32)
        halo_norms = jnp.sum(halo_float * halo_float, axis=0, keepdims=True)
        weights = lv.block(j, halo_points, halo_norms)
        term = lv.weight(j, offset) * nt_dot(received[lv.width_e :, :], weights)
        halo[j] = term if j not in halo else halo[j] + term
    for j in range(lv.count):
        total = local_ref[:, j * LEAF : (j + 1) * LEAF] + far[:, j * LEAF : (j + 1) * LEAF]
        if j in halo:
            total = total + halo[j]
        out_ref[:, j * LEAF : (j + 1) * LEAF] = total


def on_device(embeddings, directions, level_basis, neighbours, counts):
    axes = ("leaf", "sub")
    width_e = embeddings.shape[0]
    local_points = embeddings.shape[1]
    rank = level_basis.shape[1]
    nrhs = directions.shape[0]
    sub_size = lax.axis_size("sub")
    leaf_size = lax.axis_size("leaf")
    sub_bits = sub_size.bit_length() - 1
    leaf_bits = leaf_size.bit_length() - 1
    dev_bits = sub_bits + leaf_bits
    loc_bits = level_basis.shape[0] - dev_bits

    halo = jax.ShapeDtypeStruct((width_e + nrhs, LEAF), jnp.bfloat16)
    upper = jax.ShapeDtypeStruct((leaf_bits, nrhs, rank), jnp.float32)
    payload = jax.ShapeDtypeStruct((1 + leaf_bits, nrhs, rank), jnp.float32)
    first, last, upper_own, *payloads = pl.pallas_call(
        functools.partial(send_kernel, loc_bits, sub_bits),
        out_shape=(halo, halo, upper) + (payload,) * sub_bits,
        in_specs=[VMEM, VMEM, VMEM],
        out_specs=(VMEM,) * (3 + sub_bits),
    )(embeddings, directions, level_basis)

    ndev = sub_size * leaf_size
    round_one = [from_mask(payloads[mask.bit_length() - 1], "sub", mask) for mask in range(1, sub_size)]
    line = upper_own
    for got in round_one:
        line = line + got[1:]
    first, last, line = lax.optimization_barrier((first, last, line))
    from_pair = lax.ppermute(first, axes, [(i, i ^ 1) for i in range(ndev)])
    from_cross = lax.ppermute(last, axes, [(i, i - 1 + 2 * (i % 2)) for i in range(1, ndev - 1)])
    round_two = [from_mask(line, "leaf", mask) for mask in range(1, leaf_size)]

    out = jax.ShapeDtypeStruct((nrhs, local_points), jnp.float32)
    local = pl.pallas_call(
        functools.partial(local_kernel, sub_size),
        out_shape=out,
        in_specs=[VMEM, VMEM, VMEM, SMEM, SMEM],
        out_specs=VMEM,
    )(embeddings, directions, level_basis, neighbours, counts)

    remote = round_one + round_two
    return pl.pallas_call(
        functools.partial(final_kernel, sub_size, sub_bits, leaf_bits, loc_bits),
        out_shape=out,
        in_specs=[VMEM] * 6 + [SMEM, SMEM] + [VMEM] * len(remote),
        out_specs=VMEM,
        input_output_aliases={2: 0},
    )(embeddings, directions, local, from_pair, from_cross, level_basis, neighbours, counts, *remote)


def solution(mesh):
    placed = (
        P(None, ("groups", "leaf", "sub")),
        P(None, ("groups", "leaf", "sub")),
        P(None, None, ("groups", "leaf", "sub")),
        P(("groups", "leaf", "sub"), None),
        P(("groups", "leaf", "sub")),
    )
    return jax.shard_map(
        on_device,
        mesh=mesh,
        in_specs=placed,
        out_specs=P(None, ("groups", "leaf", "sub")),
        check_vma=False,
    )
```

```python
import functools
import math

import jax
import jax.numpy as jnp
from jax import lax
from jax.experimental import pallas as pl
from jax.experimental.pallas import tpu as pltpu
from jax.sharding import PartitionSpec as P

LEAF = 512


AMPLITUDE = 0.5
DISTANCE_SCALE = 0.125
RIDGE = 0.5

VMEM = pl.BlockSpec(memory_space=pltpu.VMEM)
SMEM = pl.BlockSpec(memory_space=pltpu.SMEM)


def from_mask(x, axis, mask):
    pairs = [(i, i ^ mask) for i in range(lax.axis_size(axis))]
    return lax.ppermute(x, axis, pairs)


def nt_dot(a, b):
    return lax.dot_general(a, b, (((1,), (1,)), ((), ())), preferred_element_type=jnp.float32)


def nn_dot(a, b):
    return lax.dot_general(a, b, (((1,), (0,)), ((), ())), preferred_element_type=jnp.float32)


def send_kernel(loc_bits, sub_bits, emb_ref, dirs_ref, basis_ref, first_ref, last_ref, upper_ref, *payload_refs):
    width_e = emb_ref.shape[0]
    local_points = emb_ref.shape[1]
    values = dirs_ref[...].astype(jnp.bfloat16)
    even = lax.axis_index("sub") % 2 == 0
    head_points, tail_points = emb_ref[:, :LEAF], emb_ref[:, local_points - LEAF :]
    head_values, tail_values = values[:, :LEAF], values[:, local_points - LEAF :]
    first_ref[:width_e, :] = jnp.where(even, tail_points, head_points)
    first_ref[width_e:, :] = jnp.where(even, tail_values, head_values)
    last_ref[:width_e, :] = jnp.where(even, head_points, tail_points)
    last_ref[width_e:, :] = jnp.where(even, head_values, tail_values)
    for level in range(upper_ref.shape[0]):
        part = nt_dot(values, basis_ref[loc_bits + sub_bits + level])
        upper_ref[level] = part
        for payload_ref in payload_refs:
            payload_ref[1 + level] = part
    for level, payload_ref in enumerate(payload_refs):
        payload_ref[0] = nt_dot(values, basis_ref[loc_bits + level])


class Leaves:
    def __init__(self, emb_ref, dirs_ref, neighbours_ref, counts_ref, sub_size):
        self.width_e = emb_ref.shape[0]
        self.local_points = emb_ref.shape[1]
        self.count = self.local_points // LEAF
        self.directions = dirs_ref[...]
        self.values = self.directions.astype(jnp.bfloat16)
        emb_float = emb_ref[...].astype(jnp.float32)
        row_norms = jnp.sum(emb_float * emb_float, axis=0, keepdims=True)
        emb_t = emb_float.T
        self.col_terms = -DISTANCE_SCALE * jnp.sum(emb_t * emb_t, axis=1, keepdims=True)
        self.emb_t = (emb_t * (2.0 * DISTANCE_SCALE)).astype(jnp.bfloat16)
        self.points = [emb_ref[:, j * LEAF : (j + 1) * LEAF] for j in range(self.count)]
        self.norms = [-DISTANCE_SCALE * row_norms[:, j * LEAF : (j + 1) * LEAF] for j in range(self.count)]
        self.leaf_values = [self.values[:, j * LEAF : (j + 1) * LEAF] for j in range(self.count)]
        self.neighbours_ref = neighbours_ref
        self.counts_ref = counts_ref
        self.me = lax.axis_index("leaf") * sub_size + lax.axis_index("sub")

    def block(self, j, source_points, source_terms):
        inner = nn_dot(self.emb_t[j * LEAF : (j + 1) * LEAF], source_points)
        exponent = (self.col_terms[j * LEAF : (j + 1) * LEAF] + source_terms) + inner
        return (AMPLITUDE * jnp.exp(exponent)).astype(jnp.bfloat16)

    def weight(self, j, offset):
        leaf = self.me * self.count + j
        total = jnp.int32(0)
        for slot in range(self.neighbours_ref.shape[1]):
            hit = (slot < self.counts_ref[j]) & (self.neighbours_ref[j, slot] == leaf + offset)
            total = total + hit.astype(jnp.int32)
        return total.astype(jnp.float32)


def local_kernel(sub_size, emb_ref, dirs_ref, basis_ref, neighbours_ref, counts_ref, out_ref):
    lv = Leaves(emb_ref, dirs_ref, neighbours_ref, counts_ref, sub_size)
    rank = basis_ref.shape[1]
    near = [nt_dot(lv.leaf_values[j], lv.block(j, lv.points[j], lv.norms[j])) for j in range(lv.count)]
    for j in range(lv.count - 1):
        pair = lv.block(j, lv.points[j + 1], lv.norms[j + 1])
        near[j] = near[j] + lv.weight(j, 1) * nt_dot(lv.leaf_values[j + 1], pair)
        near[j + 1] = near[j + 1] + lv.weight(j + 1, -1) * nn_dot(lv.leaf_values[j], pair)
    basis0 = basis_ref[0]
    factor0 = 1.0 / math.sqrt(rank * LEAF)
    scaled0 = [
        (nt_dot(lv.leaf_values[q], basis0[:, q * LEAF : (q + 1) * LEAF]) * factor0).astype(jnp.bfloat16)
        for q in range(lv.count)
    ]
    for q in range(lv.count):
        far0 = nn_dot(scaled0[q ^ 1], basis0[:, q * LEAF : (q + 1) * LEAF])
        out_ref[:, q * LEAF : (q + 1) * LEAF] = (
            RIDGE * lv.directions[:, q * LEAF : (q + 1) * LEAF] + near[q] + far0
        )


def final_kernel(sub_size, sub_bits, leaf_bits, loc_bits, *refs):
    sub_masks = 2**sub_bits - 1
    leaf_masks = 2**leaf_bits - 1
    emb_ref, dirs_ref, local_ref, pair_ref, cross_ref, basis_ref, neighbours_ref, counts_ref = refs[:8]
    round_one = refs[8 : 8 + sub_masks]
    round_two = refs[8 + sub_masks : 8 + sub_masks + leaf_masks]
    out_ref = refs[8 + sub_masks + leaf_masks]
    lv = Leaves(emb_ref, dirs_ref, neighbours_ref, counts_ref, sub_size)
    rank = basis_ref.shape[1]
    local_points = lv.local_points

    sibling = [None] * (sub_bits + leaf_bits)
    line = None
    for mask, got_ref in enumerate(round_one, start=1):
        level = mask.bit_length() - 1
        got = got_ref[0]
        sibling[level] = got if sibling[level] is None else sibling[level] + got
    for mask, got_ref in enumerate(round_two, start=1):
        level = sub_bits + mask.bit_length() - 1
        got = got_ref[level - sub_bits]
        sibling[level] = got if sibling[level] is None else sibling[level] + got

    far = None
    for bit in range(sub_bits + leaf_bits):
        factor = 1.0 / math.sqrt(rank * local_points * 2**bit)
        scaled = (sibling[bit] * factor).astype(jnp.bfloat16)
        term = nn_dot(scaled, basis_ref[loc_bits + bit])
        far = term if far is None else far + term

    even = lax.axis_index("sub") % 2 == 0
    pair, cross = pair_ref[...], cross_ref[...]
    left, right = jnp.where(even, cross, pair), jnp.where(even, pair, cross)
    halo = {}
    for j, received, offset in ((0, left, -1), (lv.count - 1, right, 1)):
        halo_points = received[: lv.width_e, :]
        halo_float = halo_points.astype(jnp.float32)
        halo_norms = -DISTANCE_SCALE * jnp.sum(halo_float * halo_float, axis=0, keepdims=True)
        weights = lv.block(j, halo_points, halo_norms)
        term = lv.weight(j, offset) * nt_dot(received[lv.width_e :, :], weights)
        halo[j] = term if j not in halo else halo[j] + term
    for j in range(lv.count):
        total = local_ref[:, j * LEAF : (j + 1) * LEAF] + far[:, j * LEAF : (j + 1) * LEAF]
        if j in halo:
            total = total + halo[j]
        out_ref[:, j * LEAF : (j + 1) * LEAF] = total


def on_device(embeddings, directions, level_basis, neighbours, counts):
    axes = ("leaf", "sub")
    width_e = embeddings.shape[0]
    local_points = embeddings.shape[1]
    rank = level_basis.shape[1]
    nrhs = directions.shape[0]
    sub_size = lax.axis_size("sub")
    leaf_size = lax.axis_size("leaf")
    sub_bits = sub_size.bit_length() - 1
    leaf_bits = leaf_size.bit_length() - 1
    dev_bits = sub_bits + leaf_bits
    loc_bits = level_basis.shape[0] - dev_bits

    halo = jax.ShapeDtypeStruct((width_e + nrhs, LEAF), jnp.bfloat16)
    upper = jax.ShapeDtypeStruct((leaf_bits, nrhs, rank), jnp.float32)
    payload = jax.ShapeDtypeStruct((1 + leaf_bits, nrhs, rank), jnp.float32)
    first, last, upper_own, *payloads = pl.pallas_call(
        functools.partial(send_kernel, loc_bits, sub_bits),
        out_shape=(halo, halo, upper) + (payload,) * sub_bits,
        in_specs=[VMEM, VMEM, VMEM],
        out_specs=(VMEM,) * (3 + sub_bits),
    )(embeddings, directions, level_basis)

    ndev = sub_size * leaf_size
    from_pair = lax.ppermute(first, axes, [(i, i ^ 1) for i in range(ndev)])
    from_cross = lax.ppermute(last, axes, [(i, i - 1 + 2 * (i % 2)) for i in range(1, ndev - 1)])
    round_one = [from_mask(payloads[mask.bit_length() - 1], "sub", mask) for mask in range(1, sub_size)]
    line = upper_own
    for got in round_one:
        line = line + got[1:]
    round_two = [from_mask(line, "leaf", mask) for mask in range(1, leaf_size)]

    out = jax.ShapeDtypeStruct((nrhs, local_points), jnp.float32)
    local = pl.pallas_call(
        functools.partial(local_kernel, sub_size),
        out_shape=out,
        in_specs=[VMEM, VMEM, VMEM, SMEM, SMEM],
        out_specs=VMEM,
    )(embeddings, directions, level_basis, neighbours, counts)

    remote = round_one + round_two
    return pl.pallas_call(
        functools.partial(final_kernel, sub_size, sub_bits, leaf_bits, loc_bits),
        out_shape=out,
        in_specs=[VMEM] * 6 + [SMEM, SMEM] + [VMEM] * len(remote),
        out_specs=VMEM,
        input_output_aliases={2: 0},
    )(embeddings, directions, local, from_pair, from_cross, level_basis, neighbours, counts, *remote)


def solution(mesh):
    placed = (
        P(None, ("groups", "leaf", "sub")),
        P(None, ("groups", "leaf", "sub")),
        P(None, None, ("groups", "leaf", "sub")),
        P(("groups", "leaf", "sub"), None),
        P(("groups", "leaf", "sub")),
    )
    return jax.shard_map(
        on_device,
        mesh=mesh,
        in_specs=placed,
        out_specs=P(None, ("groups", "leaf", "sub")),
        check_vma=False,
    )
```

```python
import functools
import math

import jax
import jax.numpy as jnp
from jax import lax
from jax.experimental import pallas as pl
from jax.experimental.pallas import tpu as pltpu
from jax.sharding import PartitionSpec as P

LEAF = 512


AMPLITUDE = 0.5
DISTANCE_SCALE = 0.125
RIDGE = 0.5

VMEM = pl.BlockSpec(memory_space=pltpu.VMEM)
SMEM = pl.BlockSpec(memory_space=pltpu.SMEM)


def nt_dot(a, b):
    return lax.dot_general(a, b, (((1,), (1,)), ((), ())), preferred_element_type=jnp.float32)


def nn_dot(a, b):
    return lax.dot_general(a, b, (((1,), (0,)), ((), ())), preferred_element_type=jnp.float32)


def send_kernel(loc_bits, sub_bits, emb_ref, dirs_ref, basis_ref, first_ref, last_ref, chunks_ref):
    width_e = emb_ref.shape[0]
    local_points = emb_ref.shape[1]
    values = dirs_ref[...].astype(jnp.bfloat16)
    me = lax.axis_index("sub")
    even = me % 2 == 0
    head_points, tail_points = emb_ref[:, :LEAF], emb_ref[:, local_points - LEAF :]
    head_values, tail_values = values[:, :LEAF], values[:, local_points - LEAF :]
    first_ref[:width_e, :] = jnp.where(even, tail_points, head_points)
    first_ref[width_e:, :] = jnp.where(even, tail_values, head_values)
    last_ref[:width_e, :] = jnp.where(even, head_points, tail_points)
    last_ref[width_e:, :] = jnp.where(even, head_values, tail_values)
    for level in range(chunks_ref.shape[1] - 1):
        part = nt_dot(values, basis_ref[loc_bits + sub_bits + level])
        for target in range(chunks_ref.shape[0]):
            chunks_ref[target, 1 + level] = part
    lower = [nt_dot(values, basis_ref[loc_bits + level]) for level in range(sub_bits)]
    for target in range(chunks_ref.shape[0]):
        other = jnp.bitwise_xor(me, target)
        picked = lower[0]
        for level in range(1, sub_bits):
            picked = jnp.where(other >= 2**level, lower[level], picked)
        chunks_ref[target, 0] = picked


def top_level(other, bits):
    level = jnp.int32(0)
    for bit in range(1, bits):
        level = level + (other >= 2**bit).astype(jnp.int32)
    return level


def sibling_sums(got_ref, index, me, bits):
    sums = [None] * bits
    for source in range(got_ref.shape[0]):
        other = jnp.bitwise_xor(me, source)
        level = top_level(other, bits)
        for bit in range(bits):
            term = jnp.where((other > 0) & (level == bit), got_ref[source, index(bit)], 0.0)
            sums[bit] = term if sums[bit] is None else sums[bit] + term
    return sums


class Leaves:
    def __init__(self, emb_ref, dirs_ref, neighbours_ref, counts_ref, sub_size):
        self.width_e = emb_ref.shape[0]
        self.local_points = emb_ref.shape[1]
        self.count = self.local_points // LEAF
        self.directions = dirs_ref[...]
        self.values = self.directions.astype(jnp.bfloat16)
        emb_float = emb_ref[...].astype(jnp.float32)
        row_norms = jnp.sum(emb_float * emb_float, axis=0, keepdims=True)
        emb_t = emb_float.T
        self.col_terms = -DISTANCE_SCALE * jnp.sum(emb_t * emb_t, axis=1, keepdims=True)
        self.emb_t = (emb_t * (2.0 * DISTANCE_SCALE)).astype(jnp.bfloat16)
        self.points = [emb_ref[:, j * LEAF : (j + 1) * LEAF] for j in range(self.count)]
        self.norms = [-DISTANCE_SCALE * row_norms[:, j * LEAF : (j + 1) * LEAF] for j in range(self.count)]
        self.leaf_values = [self.values[:, j * LEAF : (j + 1) * LEAF] for j in range(self.count)]
        self.neighbours_ref = neighbours_ref
        self.counts_ref = counts_ref
        self.me = lax.axis_index("leaf") * sub_size + lax.axis_index("sub")

    def block(self, j, source_points, source_terms):
        inner = nn_dot(self.emb_t[j * LEAF : (j + 1) * LEAF], source_points)
        exponent = (self.col_terms[j * LEAF : (j + 1) * LEAF] + source_terms) + inner
        return (AMPLITUDE * jnp.exp(exponent)).astype(jnp.bfloat16)

    def weight(self, j, offset):
        leaf = self.me * self.count + j
        total = jnp.int32(0)
        for slot in range(self.neighbours_ref.shape[1]):
            hit = (slot < self.counts_ref[j]) & (self.neighbours_ref[j, slot] == leaf + offset)
            total = total + hit.astype(jnp.int32)
        return total.astype(jnp.float32)


def local_kernel(sub_size, emb_ref, dirs_ref, basis_ref, neighbours_ref, counts_ref, out_ref):
    lv = Leaves(emb_ref, dirs_ref, neighbours_ref, counts_ref, sub_size)
    rank = basis_ref.shape[1]
    near = [nt_dot(lv.leaf_values[j], lv.block(j, lv.points[j], lv.norms[j])) for j in range(lv.count)]
    for j in range(lv.count - 1):
        pair = lv.block(j, lv.points[j + 1], lv.norms[j + 1])
        near[j] = near[j] + lv.weight(j, 1) * nt_dot(lv.leaf_values[j + 1], pair)
        near[j + 1] = near[j + 1] + lv.weight(j + 1, -1) * nn_dot(lv.leaf_values[j], pair)
    basis0 = basis_ref[0]
    factor0 = 1.0 / math.sqrt(rank * LEAF)
    scaled0 = [
        (nt_dot(lv.leaf_values[q], basis0[:, q * LEAF : (q + 1) * LEAF]) * factor0).astype(jnp.bfloat16)
        for q in range(lv.count)
    ]
    for q in range(lv.count):
        far0 = nn_dot(scaled0[q ^ 1], basis0[:, q * LEAF : (q + 1) * LEAF])
        out_ref[:, q * LEAF : (q + 1) * LEAF] = (
            RIDGE * lv.directions[:, q * LEAF : (q + 1) * LEAF] + near[q] + far0
        )


def final_kernel(sub_size, sub_bits, leaf_bits, loc_bits, *refs):
    emb_ref, dirs_ref, local_ref, pair_ref, cross_ref, basis_ref, neighbours_ref, counts_ref, one_ref, two_ref, out_ref = refs
    lv = Leaves(emb_ref, dirs_ref, neighbours_ref, counts_ref, sub_size)
    rank = basis_ref.shape[1]
    local_points = lv.local_points

    sibling = sibling_sums(one_ref, lambda bit: 0, lax.axis_index("sub"), sub_bits)
    sibling += sibling_sums(two_ref, lambda bit: bit, lax.axis_index("leaf"), leaf_bits)

    far = None
    for bit in range(sub_bits + leaf_bits):
        factor = 1.0 / math.sqrt(rank * local_points * 2**bit)
        scaled = (sibling[bit] * factor).astype(jnp.bfloat16)
        term = nn_dot(scaled, basis_ref[loc_bits + bit])
        far = term if far is None else far + term

    even = lax.axis_index("sub") % 2 == 0
    pair, cross = pair_ref[...], cross_ref[...]
    left, right = jnp.where(even, cross, pair), jnp.where(even, pair, cross)
    halo = {}
    for j, received, offset in ((0, left, -1), (lv.count - 1, right, 1)):
        halo_points = received[: lv.width_e, :]
        halo_float = halo_points.astype(jnp.float32)
        halo_norms = -DISTANCE_SCALE * jnp.sum(halo_float * halo_float, axis=0, keepdims=True)
        weights = lv.block(j, halo_points, halo_norms)
        term = lv.weight(j, offset) * nt_dot(received[lv.width_e :, :], weights)
        halo[j] = term if j not in halo else halo[j] + term
    for j in range(lv.count):
        total = local_ref[:, j * LEAF : (j + 1) * LEAF] + far[:, j * LEAF : (j + 1) * LEAF]
        if j in halo:
            total = total + halo[j]
        out_ref[:, j * LEAF : (j + 1) * LEAF] = total


def on_device(embeddings, directions, level_basis, neighbours, counts):
    axes = ("leaf", "sub")
    width_e = embeddings.shape[0]
    local_points = embeddings.shape[1]
    rank = level_basis.shape[1]
    nrhs = directions.shape[0]
    sub_size = lax.axis_size("sub")
    leaf_size = lax.axis_size("leaf")
    sub_bits = sub_size.bit_length() - 1
    leaf_bits = leaf_size.bit_length() - 1
    dev_bits = sub_bits + leaf_bits
    loc_bits = level_basis.shape[0] - dev_bits

    halo = jax.ShapeDtypeStruct((width_e + nrhs, LEAF), jnp.bfloat16)
    chunks = jax.ShapeDtypeStruct((sub_size, 1 + leaf_bits, nrhs, rank), jnp.float32)
    first, last, outgoing = pl.pallas_call(
        functools.partial(send_kernel, loc_bits, sub_bits),
        out_shape=(halo, halo, chunks),
        in_specs=[VMEM, VMEM, VMEM],
        out_specs=(VMEM, VMEM, VMEM),
    )(embeddings, directions, level_basis)

    ndev = sub_size * leaf_size
    from_pair = lax.ppermute(first, axes, [(i, i ^ 1) for i in range(ndev)])
    from_cross = lax.ppermute(last, axes, [(i, i - 1 + 2 * (i % 2)) for i in range(1, ndev - 1)])
    round_one = lax.all_to_all(outgoing, "sub", 0, 0, tiled=True)
    line = jnp.sum(round_one[:, 1:], axis=0)
    round_two = lax.all_to_all(jnp.broadcast_to(line[None], (leaf_size,) + line.shape), "leaf", 0, 0, tiled=True)

    out = jax.ShapeDtypeStruct((nrhs, local_points), jnp.float32)
    local = pl.pallas_call(
        functools.partial(local_kernel, sub_size),
        out_shape=out,
        in_specs=[VMEM, VMEM, VMEM, SMEM, SMEM],
        out_specs=VMEM,
    )(embeddings, directions, level_basis, neighbours, counts)

    return pl.pallas_call(
        functools.partial(final_kernel, sub_size, sub_bits, leaf_bits, loc_bits),
        out_shape=out,
        in_specs=[VMEM] * 6 + [SMEM, SMEM] + [VMEM] * 2,
        out_specs=VMEM,
        input_output_aliases={2: 0},
    )(embeddings, directions, local, from_pair, from_cross, level_basis, neighbours, counts, round_one, round_two)


def solution(mesh):
    placed = (
        P(None, ("groups", "leaf", "sub")),
        P(None, ("groups", "leaf", "sub")),
        P(None, None, ("groups", "leaf", "sub")),
        P(("groups", "leaf", "sub"), None),
        P(("groups", "leaf", "sub")),
    )
    return jax.shard_map(
        on_device,
        mesh=mesh,
        in_specs=placed,
        out_specs=P(None, ("groups", "leaf", "sub")),
        check_vma=False,
    )
```

```python
import functools
import math

import jax
import jax.numpy as jnp
from jax import lax
from jax.experimental import pallas as pl
from jax.experimental.pallas import tpu as pltpu
from jax.sharding import PartitionSpec as P

LEAF = 512


AMPLITUDE = 0.5
DISTANCE_SCALE = 0.125
RIDGE = 0.5

VMEM = pl.BlockSpec(memory_space=pltpu.VMEM)
SMEM = pl.BlockSpec(memory_space=pltpu.SMEM)


def from_mask(x, axis, mask):
    pairs = [(i, i ^ mask) for i in range(lax.axis_size(axis))]
    return lax.ppermute(x, axis, pairs)


def nt_dot(a, b):
    return lax.dot_general(a, b, (((1,), (1,)), ((), ())), preferred_element_type=jnp.float32)


def nn_dot(a, b):
    return lax.dot_general(a, b, (((1,), (0,)), ((), ())), preferred_element_type=jnp.float32)


def send_kernel(loc_bits, emb_ref, dirs_ref, basis_ref, first_ref, last_ref, lower_ref, upper_ref):
    width_e = emb_ref.shape[0]
    local_points = emb_ref.shape[1]
    values = dirs_ref[...].astype(jnp.bfloat16)
    even = lax.axis_index("sub") % 2 == 0
    head_points, tail_points = emb_ref[:, :LEAF], emb_ref[:, local_points - LEAF :]
    head_values, tail_values = values[:, :LEAF], values[:, local_points - LEAF :]
    first_ref[:width_e, :] = jnp.where(even, tail_points, head_points)
    first_ref[width_e:, :] = jnp.where(even, tail_values, head_values)
    last_ref[:width_e, :] = jnp.where(even, head_points, tail_points)
    last_ref[width_e:, :] = jnp.where(even, head_values, tail_values)
    for level in range(lower_ref.shape[0]):
        lower_ref[level] = nt_dot(values, basis_ref[loc_bits + level])
    for level in range(upper_ref.shape[0]):
        upper_ref[level] = nt_dot(values, basis_ref[loc_bits + lower_ref.shape[0] + level])


class Leaves:
    def __init__(self, emb_ref, dirs_ref, neighbours_ref, counts_ref, sub_size):
        self.width_e = emb_ref.shape[0]
        self.local_points = emb_ref.shape[1]
        self.count = self.local_points // LEAF
        self.directions = dirs_ref[...]
        self.values = self.directions.astype(jnp.bfloat16)
        emb_float = emb_ref[...].astype(jnp.float32)
        row_norms = jnp.sum(emb_float * emb_float, axis=0, keepdims=True)
        emb_t = emb_float.T
        self.col_terms = -DISTANCE_SCALE * jnp.sum(emb_t * emb_t, axis=1, keepdims=True)
        self.emb_t = (emb_t * (2.0 * DISTANCE_SCALE)).astype(jnp.bfloat16)
        self.points = [emb_ref[:, j * LEAF : (j + 1) * LEAF] for j in range(self.count)]
        self.norms = [-DISTANCE_SCALE * row_norms[:, j * LEAF : (j + 1) * LEAF] for j in range(self.count)]
        self.leaf_values = [self.values[:, j * LEAF : (j + 1) * LEAF] for j in range(self.count)]
        self.neighbours_ref = neighbours_ref
        self.counts_ref = counts_ref
        self.me = lax.axis_index("leaf") * sub_size + lax.axis_index("sub")

    def block(self, j, source_points, source_terms):
        inner = nn_dot(self.emb_t[j * LEAF : (j + 1) * LEAF], source_points)
        exponent = (self.col_terms[j * LEAF : (j + 1) * LEAF] + source_terms) + inner
        return (AMPLITUDE * jnp.exp(exponent)).astype(jnp.bfloat16)

    def weight(self, j, offset):
        leaf = self.me * self.count + j
        total = jnp.int32(0)
        for slot in range(self.neighbours_ref.shape[1]):
            hit = (slot < self.counts_ref[j]) & (self.neighbours_ref[j, slot] == leaf + offset)
            total = total + hit.astype(jnp.int32)
        return total.astype(jnp.float32)


def local_kernel(sub_size, emb_ref, dirs_ref, basis_ref, neighbours_ref, counts_ref, out_ref):
    lv = Leaves(emb_ref, dirs_ref, neighbours_ref, counts_ref, sub_size)
    rank = basis_ref.shape[1]
    near = [nt_dot(lv.leaf_values[j], lv.block(j, lv.points[j], lv.norms[j])) for j in range(lv.count)]
    for j in range(lv.count - 1):
        pair = lv.block(j, lv.points[j + 1], lv.norms[j + 1])
        near[j] = near[j] + lv.weight(j, 1) * nt_dot(lv.leaf_values[j + 1], pair)
        near[j + 1] = near[j + 1] + lv.weight(j + 1, -1) * nn_dot(lv.leaf_values[j], pair)
    basis0 = basis_ref[0]
    factor0 = 1.0 / math.sqrt(rank * LEAF)
    scaled0 = [
        (nt_dot(lv.leaf_values[q], basis0[:, q * LEAF : (q + 1) * LEAF]) * factor0).astype(jnp.bfloat16)
        for q in range(lv.count)
    ]
    for q in range(lv.count):
        far0 = nn_dot(scaled0[q ^ 1], basis0[:, q * LEAF : (q + 1) * LEAF])
        out_ref[:, q * LEAF : (q + 1) * LEAF] = (
            RIDGE * lv.directions[:, q * LEAF : (q + 1) * LEAF] + near[q] + far0
        )


def final_kernel(sub_size, sub_bits, leaf_bits, loc_bits, *refs):
    sub_masks = 2**sub_bits - 1
    emb_ref, dirs_ref, local_ref, pair_ref, cross_ref, basis_ref, neighbours_ref, counts_ref, own_ref = refs[:9]
    round_two = refs[9 : 9 + sub_masks]
    out_ref = refs[9 + sub_masks]
    lv = Leaves(emb_ref, dirs_ref, neighbours_ref, counts_ref, sub_size)
    rank = basis_ref.shape[1]
    local_points = lv.local_points

    sibling = [None] * sub_bits + [own_ref[sub_bits + bit] for bit in range(leaf_bits)]
    for mask, got_ref in enumerate(round_two, start=1):
        level = mask.bit_length() - 1
        got = got_ref[level]
        sibling[level] = got if sibling[level] is None else sibling[level] + got
        for bit in range(leaf_bits):
            sibling[sub_bits + bit] = sibling[sub_bits + bit] + got_ref[sub_bits + bit]

    far = None
    for bit in range(sub_bits + leaf_bits):
        factor = 1.0 / math.sqrt(rank * local_points * 2**bit)
        scaled = (sibling[bit] * factor).astype(jnp.bfloat16)
        term = nn_dot(scaled, basis_ref[loc_bits + bit])
        far = term if far is None else far + term

    even = lax.axis_index("sub") % 2 == 0
    pair, cross = pair_ref[...], cross_ref[...]
    left, right = jnp.where(even, cross, pair), jnp.where(even, pair, cross)
    halo = {}
    for j, received, offset in ((0, left, -1), (lv.count - 1, right, 1)):
        halo_points = received[: lv.width_e, :]
        halo_float = halo_points.astype(jnp.float32)
        halo_norms = -DISTANCE_SCALE * jnp.sum(halo_float * halo_float, axis=0, keepdims=True)
        weights = lv.block(j, halo_points, halo_norms)
        term = lv.weight(j, offset) * nt_dot(received[lv.width_e :, :], weights)
        halo[j] = term if j not in halo else halo[j] + term
    for j in range(lv.count):
        total = local_ref[:, j * LEAF : (j + 1) * LEAF] + far[:, j * LEAF : (j + 1) * LEAF]
        if j in halo:
            total = total + halo[j]
        out_ref[:, j * LEAF : (j + 1) * LEAF] = total


def on_device(embeddings, directions, level_basis, neighbours, counts):
    axes = ("leaf", "sub")
    width_e = embeddings.shape[0]
    local_points = embeddings.shape[1]
    rank = level_basis.shape[1]
    nrhs = directions.shape[0]
    sub_size = lax.axis_size("sub")
    leaf_size = lax.axis_size("leaf")
    sub_bits = sub_size.bit_length() - 1
    leaf_bits = leaf_size.bit_length() - 1
    dev_bits = sub_bits + leaf_bits
    loc_bits = level_basis.shape[0] - dev_bits

    halo = jax.ShapeDtypeStruct((width_e + nrhs, LEAF), jnp.bfloat16)
    first, last, lower, upper = pl.pallas_call(
        functools.partial(send_kernel, loc_bits),
        out_shape=(
            halo,
            halo,
            jax.ShapeDtypeStruct((sub_bits, nrhs, rank), jnp.float32),
            jax.ShapeDtypeStruct((leaf_bits, nrhs, rank), jnp.float32),
        ),
        in_specs=[VMEM, VMEM, VMEM],
        out_specs=(VMEM,) * 4,
    )(embeddings, directions, level_basis)

    ndev = sub_size * leaf_size
    round_one = [from_mask(upper, "leaf", mask) for mask in range(1, leaf_size)]
    from_pair = lax.ppermute(first, axes, [(i, i ^ 1) for i in range(ndev)])
    from_cross = lax.ppermute(last, axes, [(i, i - 1 + 2 * (i % 2)) for i in range(1, ndev - 1)])
    blocks = [None] * leaf_bits
    for mask, got in enumerate(round_one, start=1):
        level = mask.bit_length() - 1
        blocks[level] = got[level] if blocks[level] is None else blocks[level] + got[level]
    own = jnp.concatenate([lower, jnp.stack(blocks)], axis=0)
    round_two = [from_mask(own, "sub", mask) for mask in range(1, sub_size)]

    out = jax.ShapeDtypeStruct((nrhs, local_points), jnp.float32)
    local = pl.pallas_call(
        functools.partial(local_kernel, sub_size),
        out_shape=out,
        in_specs=[VMEM, VMEM, VMEM, SMEM, SMEM],
        out_specs=VMEM,
    )(embeddings, directions, level_basis, neighbours, counts)

    return pl.pallas_call(
        functools.partial(final_kernel, sub_size, sub_bits, leaf_bits, loc_bits),
        out_shape=out,
        in_specs=[VMEM] * 6 + [SMEM, SMEM] + [VMEM] * (1 + len(round_two)),
        out_specs=VMEM,
        input_output_aliases={2: 0},
    )(embeddings, directions, local, from_pair, from_cross, level_basis, neighbours, counts, own, *round_two)


def solution(mesh):
    placed = (
        P(None, ("groups", "leaf", "sub")),
        P(None, ("groups", "leaf", "sub")),
        P(None, None, ("groups", "leaf", "sub")),
        P(("groups", "leaf", "sub"), None),
        P(("groups", "leaf", "sub")),
    )
    return jax.shard_map(
        on_device,
        mesh=mesh,
        in_specs=placed,
        out_specs=P(None, ("groups", "leaf", "sub")),
        check_vma=False,
    )
```

```python
import functools
import math

import jax
import jax.numpy as jnp
from jax import lax
from jax.experimental import pallas as pl
from jax.experimental.pallas import tpu as pltpu
from jax.sharding import PartitionSpec as P

LEAF = 512


AMPLITUDE = 0.5
DISTANCE_SCALE = 0.125
RIDGE = 0.5

VMEM = pl.BlockSpec(memory_space=pltpu.VMEM)
SMEM = pl.BlockSpec(memory_space=pltpu.SMEM)


def from_mask(x, axis, mask):
    pairs = [(i, i ^ mask) for i in range(lax.axis_size(axis))]
    return lax.ppermute(x, axis, pairs)


def nt_dot(a, b):
    return lax.dot_general(a, b, (((1,), (1,)), ((), ())), preferred_element_type=jnp.float32)


def nn_dot(a, b):
    return lax.dot_general(a, b, (((1,), (0,)), ((), ())), preferred_element_type=jnp.float32)


def send_kernel(loc_bits, sub_bits, emb_ref, dirs_ref, basis_ref, first_ref, last_ref, upper_ref, *payload_refs):
    width_e = emb_ref.shape[0]
    local_points = emb_ref.shape[1]
    values = dirs_ref[...].astype(jnp.bfloat16)
    even = lax.axis_index("sub") % 2 == 0
    head_points, tail_points = emb_ref[:, :LEAF], emb_ref[:, local_points - LEAF :]
    head_values, tail_values = values[:, :LEAF], values[:, local_points - LEAF :]
    first_ref[:width_e, :] = jnp.where(even, tail_points, head_points)
    first_ref[width_e:, :] = jnp.where(even, tail_values, head_values)
    last_ref[:width_e, :] = jnp.where(even, head_points, tail_points)
    last_ref[width_e:, :] = jnp.where(even, head_values, tail_values)
    for level in range(upper_ref.shape[0]):
        part = nt_dot(values, basis_ref[loc_bits + sub_bits + level])
        upper_ref[level] = part
        for payload_ref in payload_refs:
            payload_ref[1 + level] = part
    for level, payload_ref in enumerate(payload_refs):
        payload_ref[0] = nt_dot(values, basis_ref[loc_bits + level])


class Leaves:
    def __init__(self, emb_ref, dirs_ref, neighbours_ref, counts_ref, sub_size):
        self.width_e = emb_ref.shape[0]
        self.local_points = emb_ref.shape[1]
        self.count = self.local_points // LEAF
        self.directions = dirs_ref[...]
        self.values = self.directions.astype(jnp.bfloat16)
        emb_float = emb_ref[...].astype(jnp.float32)
        row_norms = jnp.sum(emb_float * emb_float, axis=0, keepdims=True)
        emb_t = emb_float.T
        self.col_terms = -DISTANCE_SCALE * jnp.sum(emb_t * emb_t, axis=1, keepdims=True)
        self.emb_t = (emb_t * (2.0 * DISTANCE_SCALE)).astype(jnp.bfloat16)
        self.points = [emb_ref[:, j * LEAF : (j + 1) * LEAF] for j in range(self.count)]
        self.norms = [-DISTANCE_SCALE * row_norms[:, j * LEAF : (j + 1) * LEAF] for j in range(self.count)]
        self.leaf_values = [self.values[:, j * LEAF : (j + 1) * LEAF] for j in range(self.count)]
        self.neighbours_ref = neighbours_ref
        self.counts_ref = counts_ref
        self.me = lax.axis_index("leaf") * sub_size + lax.axis_index("sub")

    def block(self, j, source_points, source_terms):
        inner = nn_dot(self.emb_t[j * LEAF : (j + 1) * LEAF], source_points)
        exponent = (self.col_terms[j * LEAF : (j + 1) * LEAF] + source_terms) + inner
        return (AMPLITUDE * jnp.exp(exponent)).astype(jnp.bfloat16)

    def weight(self, j, offset):
        leaf = self.me * self.count + j
        total = jnp.int32(0)
        for slot in range(self.neighbours_ref.shape[1]):
            hit = (slot < self.counts_ref[j]) & (self.neighbours_ref[j, slot] == leaf + offset)
            total = total + hit.astype(jnp.int32)
        return total.astype(jnp.float32)


def local_kernel(sub_size, emb_ref, dirs_ref, basis_ref, neighbours_ref, counts_ref, out_ref):
    lv = Leaves(emb_ref, dirs_ref, neighbours_ref, counts_ref, sub_size)
    rank = basis_ref.shape[1]
    near = [nt_dot(lv.leaf_values[j], lv.block(j, lv.points[j], lv.norms[j])) for j in range(lv.count)]
    for j in range(lv.count - 1):
        pair = lv.block(j, lv.points[j + 1], lv.norms[j + 1])
        near[j] = near[j] + lv.weight(j, 1) * nt_dot(lv.leaf_values[j + 1], pair)
        near[j + 1] = near[j + 1] + lv.weight(j + 1, -1) * nn_dot(lv.leaf_values[j], pair)
    basis0 = basis_ref[0]
    factor0 = 1.0 / math.sqrt(rank * LEAF)
    scaled0 = [
        (nt_dot(lv.leaf_values[q], basis0[:, q * LEAF : (q + 1) * LEAF]) * factor0).astype(jnp.bfloat16)
        for q in range(lv.count)
    ]
    for q in range(lv.count):
        far0 = nn_dot(scaled0[q ^ 1], basis0[:, q * LEAF : (q + 1) * LEAF])
        out_ref[:, q * LEAF : (q + 1) * LEAF] = (
            RIDGE * lv.directions[:, q * LEAF : (q + 1) * LEAF] + near[q] + far0
        )


def final_kernel(sub_size, sub_bits, leaf_bits, loc_bits, *refs):
    sub_masks = 2**sub_bits - 1
    leaf_masks = 2**leaf_bits - 1
    emb_ref, dirs_ref, local_ref, pair_ref, cross_ref, basis_ref, neighbours_ref, counts_ref = refs[:8]
    round_one = refs[8 : 8 + sub_masks]
    round_two = refs[8 + sub_masks : 8 + sub_masks + leaf_masks]
    out_ref = refs[8 + sub_masks + leaf_masks]
    lv = Leaves(emb_ref, dirs_ref, neighbours_ref, counts_ref, sub_size)
    rank = basis_ref.shape[1]
    local_points = lv.local_points

    sibling = [None] * (sub_bits + leaf_bits)
    line = None
    for mask, got_ref in enumerate(round_one, start=1):
        level = mask.bit_length() - 1
        got = got_ref[0]
        sibling[level] = got if sibling[level] is None else sibling[level] + got
    for mask, got_ref in enumerate(round_two, start=1):
        level = sub_bits + mask.bit_length() - 1
        got = got_ref[level - sub_bits]
        sibling[level] = got if sibling[level] is None else sibling[level] + got

    far = None
    for bit in range(sub_bits + leaf_bits):
        factor = 1.0 / math.sqrt(rank * local_points * 2**bit)
        scaled = (sibling[bit] * factor).astype(jnp.bfloat16)
        term = nn_dot(scaled, basis_ref[loc_bits + bit])
        far = term if far is None else far + term

    even = lax.axis_index("sub") % 2 == 0
    pair, cross = pair_ref[...], cross_ref[...]
    left, right = jnp.where(even, cross, pair), jnp.where(even, pair, cross)
    halo = {}
    for j, received, offset in ((0, left, -1), (lv.count - 1, right, 1)):
        halo_points = received[: lv.width_e, :]
        halo_float = halo_points.astype(jnp.float32)
        halo_norms = -DISTANCE_SCALE * jnp.sum(halo_float * halo_float, axis=0, keepdims=True)
        weights = lv.block(j, halo_points, halo_norms)
        term = lv.weight(j, offset) * nt_dot(received[lv.width_e :, :], weights)
        halo[j] = term if j not in halo else halo[j] + term
    for j in range(lv.count):
        total = local_ref[:, j * LEAF : (j + 1) * LEAF] + far[:, j * LEAF : (j + 1) * LEAF]
        if j in halo:
            total = total + halo[j]
        out_ref[:, j * LEAF : (j + 1) * LEAF] = total


def on_device(embeddings, directions, level_basis, neighbours, counts):
    axes = ("leaf", "sub")
    width_e = embeddings.shape[0]
    local_points = embeddings.shape[1]
    rank = level_basis.shape[1]
    nrhs = directions.shape[0]
    sub_size = lax.axis_size("sub")
    leaf_size = lax.axis_size("leaf")
    sub_bits = sub_size.bit_length() - 1
    leaf_bits = leaf_size.bit_length() - 1
    dev_bits = sub_bits + leaf_bits
    loc_bits = level_basis.shape[0] - dev_bits

    halo = jax.ShapeDtypeStruct((width_e + nrhs, LEAF), jnp.bfloat16)
    upper = jax.ShapeDtypeStruct((leaf_bits, nrhs, rank), jnp.float32)
    payload = jax.ShapeDtypeStruct((1 + leaf_bits, nrhs, rank), jnp.float32)
    first, last, upper_own, *payloads = pl.pallas_call(
        functools.partial(send_kernel, loc_bits, sub_bits),
        out_shape=(halo, halo, upper) + (payload,) * sub_bits,
        in_specs=[VMEM, VMEM, VMEM],
        out_specs=(VMEM,) * (3 + sub_bits),
    )(embeddings, directions, level_basis)

    ndev = sub_size * leaf_size
    from_pair = lax.ppermute(first, axes, [(i, i ^ 1) for i in range(ndev)])
    from_cross = lax.ppermute(last, axes, [(i, i - 1 + 2 * (i % 2)) for i in range(1, ndev - 1)])
    round_one = [from_mask(payloads[mask.bit_length() - 1], "sub", mask) for mask in range(1, sub_size)]
    out = jax.ShapeDtypeStruct((nrhs, local_points), jnp.float32)
    local = pl.pallas_call(
        functools.partial(local_kernel, sub_size),
        out_shape=out,
        in_specs=[VMEM, VMEM, VMEM, SMEM, SMEM],
        out_specs=VMEM,
    )(embeddings, directions, level_basis, neighbours, counts)
    local, *round_one = lax.optimization_barrier((local, *round_one))
    line = upper_own
    for got in round_one:
        line = line + got[1:]
    round_two = [from_mask(line, "leaf", mask) for mask in range(1, leaf_size)]

    remote = round_one + round_two
    return pl.pallas_call(
        functools.partial(final_kernel, sub_size, sub_bits, leaf_bits, loc_bits),
        out_shape=out,
        in_specs=[VMEM] * 6 + [SMEM, SMEM] + [VMEM] * len(remote),
        out_specs=VMEM,
        input_output_aliases={2: 0},
    )(embeddings, directions, local, from_pair, from_cross, level_basis, neighbours, counts, *remote)


def solution(mesh):
    placed = (
        P(None, ("groups", "leaf", "sub")),
        P(None, ("groups", "leaf", "sub")),
        P(None, None, ("groups", "leaf", "sub")),
        P(("groups", "leaf", "sub"), None),
        P(("groups", "leaf", "sub")),
    )
    return jax.shard_map(
        on_device,
        mesh=mesh,
        in_specs=placed,
        out_specs=P(None, ("groups", "leaf", "sub")),
        check_vma=False,
    )
```

```python
import functools
import math

import jax
import jax.numpy as jnp
from jax import lax
from jax.experimental import pallas as pl
from jax.experimental.pallas import tpu as pltpu
from jax.sharding import PartitionSpec as P

LEAF = 512


AMPLITUDE = 0.5
DISTANCE_SCALE = 0.125
RIDGE = 0.5

VMEM = pl.BlockSpec(memory_space=pltpu.VMEM)
SMEM = pl.BlockSpec(memory_space=pltpu.SMEM)


def from_mask(x, axis, mask):
    pairs = [(i, i ^ mask) for i in range(lax.axis_size(axis))]
    return lax.ppermute(x, axis, pairs)


def nt_dot(a, b):
    return lax.dot_general(a, b, (((1,), (1,)), ((), ())), preferred_element_type=jnp.float32)


def nn_dot(a, b):
    return lax.dot_general(a, b, (((1,), (0,)), ((), ())), preferred_element_type=jnp.float32)


def split_rows(x, width):
    groups = width // x.shape[1]
    step = x.shape[0] // groups
    return jnp.concatenate([x[g * step : (g + 1) * step] for g in range(groups)], axis=1)


def join_rows(x, columns):
    groups = x.shape[1] // columns
    return jnp.concatenate([x[:, g * columns : (g + 1) * columns] for g in range(groups)], axis=0)


def send_kernel(loc_bits, emb_ref, dirs_ref, basis_ref, pair_ref, cross_ref, parts_ref):
    width_e = emb_ref.shape[0]
    local_points = emb_ref.shape[1]
    nrhs = dirs_ref.shape[0]
    values = dirs_ref[...].astype(jnp.bfloat16)
    even = lax.axis_index("sub") % 2 == 0
    head_points, tail_points = emb_ref[:, :LEAF], emb_ref[:, local_points - LEAF :]
    head_values, tail_values = values[:, :LEAF], values[:, local_points - LEAF :]
    pair_ref[:width_e, :] = jnp.where(even, tail_points, head_points)
    pair_ref[width_e : width_e + nrhs, :] = jnp.where(even, tail_values, head_values)
    cross_ref[:width_e, :] = jnp.where(even, head_points, tail_points)
    cross_ref[width_e:, :] = jnp.where(even, head_values, tail_values)
    levels, rank = parts_ref.shape[1] // basis_ref.shape[1], basis_ref.shape[1]
    stacked = basis_ref[loc_bits : loc_bits + levels].reshape(levels * rank, local_points)
    parts = nt_dot(values, stacked)
    parts_ref[...] = parts
    rows = split_rows(parts, LEAF)
    high = rows.astype(jnp.bfloat16)
    rest = rows - high.astype(jnp.float32)
    middle = rest.astype(jnp.bfloat16)
    low = (rest - middle.astype(jnp.float32)).astype(jnp.bfloat16)
    start = width_e + nrhs
    step = rows.shape[0]
    pair_ref[start : start + step, :] = high
    pair_ref[start + step : start + 2 * step, :] = middle
    pair_ref[start + 2 * step : start + 3 * step, :] = low


def unpack_parts(pair, start, step, columns):
    pieces = pair[start : start + 3 * step].astype(jnp.float32)
    rows = (pieces[:step] + pieces[step : 2 * step]) + pieces[2 * step :]
    return join_rows(rows, columns)


class Leaves:
    def __init__(self, emb_ref, dirs_ref, neighbours_ref, counts_ref, sub_size):
        self.width_e = emb_ref.shape[0]
        self.local_points = emb_ref.shape[1]
        self.count = self.local_points // LEAF
        self.directions = dirs_ref[...]
        self.values = self.directions.astype(jnp.bfloat16)
        emb_float = emb_ref[...].astype(jnp.float32)
        row_norms = jnp.sum(emb_float * emb_float, axis=0, keepdims=True)
        emb_t = emb_float.T
        self.col_terms = -DISTANCE_SCALE * jnp.sum(emb_t * emb_t, axis=1, keepdims=True)
        self.emb_t = (emb_t * (2.0 * DISTANCE_SCALE)).astype(jnp.bfloat16)
        self.points = [emb_ref[:, j * LEAF : (j + 1) * LEAF] for j in range(self.count)]
        self.norms = [-DISTANCE_SCALE * row_norms[:, j * LEAF : (j + 1) * LEAF] for j in range(self.count)]
        self.leaf_values = [self.values[:, j * LEAF : (j + 1) * LEAF] for j in range(self.count)]
        self.neighbours_ref = neighbours_ref
        self.counts_ref = counts_ref
        self.me = lax.axis_index("leaf") * sub_size + lax.axis_index("sub")

    def block(self, j, source_points, source_terms):
        inner = nn_dot(self.emb_t[j * LEAF : (j + 1) * LEAF], source_points)
        exponent = (self.col_terms[j * LEAF : (j + 1) * LEAF] + source_terms) + inner
        return (AMPLITUDE * jnp.exp(exponent)).astype(jnp.bfloat16)

    def weight(self, j, offset):
        leaf = self.me * self.count + j
        total = jnp.int32(0)
        for slot in range(self.neighbours_ref.shape[1]):
            hit = (slot < self.counts_ref[j]) & (self.neighbours_ref[j, slot] == leaf + offset)
            total = total + hit.astype(jnp.int32)
        return total.astype(jnp.float32)


def local_kernel(sub_size, emb_ref, dirs_ref, basis_ref, neighbours_ref, counts_ref, out_ref):
    lv = Leaves(emb_ref, dirs_ref, neighbours_ref, counts_ref, sub_size)
    rank = basis_ref.shape[1]
    near = [nt_dot(lv.leaf_values[j], lv.block(j, lv.points[j], lv.norms[j])) for j in range(lv.count)]
    for j in range(lv.count - 1):
        pair = lv.block(j, lv.points[j + 1], lv.norms[j + 1])
        near[j] = near[j] + lv.weight(j, 1) * nt_dot(lv.leaf_values[j + 1], pair)
        near[j + 1] = near[j + 1] + lv.weight(j + 1, -1) * nn_dot(lv.leaf_values[j], pair)
    basis0 = basis_ref[0]
    factor0 = 1.0 / math.sqrt(rank * LEAF)
    scaled0 = [
        (nt_dot(lv.leaf_values[q], basis0[:, q * LEAF : (q + 1) * LEAF]) * factor0).astype(jnp.bfloat16)
        for q in range(lv.count)
    ]
    for q in range(lv.count):
        far0 = nn_dot(scaled0[q ^ 1], basis0[:, q * LEAF : (q + 1) * LEAF])
        out_ref[:, q * LEAF : (q + 1) * LEAF] = (
            RIDGE * lv.directions[:, q * LEAF : (q + 1) * LEAF] + near[q] + far0
        )


def final_kernel(sub_size, sub_bits, leaf_bits, loc_bits, *refs):
    sub_masks = 2**sub_bits - 1
    leaf_masks = 2**leaf_bits - 1
    emb_ref, dirs_ref, local_ref, pair_ref, cross_ref, basis_ref, neighbours_ref, counts_ref = refs[:8]
    round_one = refs[8 : 8 + sub_masks - 1]
    round_two = refs[8 + sub_masks - 1 : 8 + sub_masks - 1 + leaf_masks]
    out_ref = refs[8 + sub_masks - 1 + leaf_masks]
    lv = Leaves(emb_ref, dirs_ref, neighbours_ref, counts_ref, sub_size)
    rank = basis_ref.shape[1]
    nrhs = dirs_ref.shape[0]
    local_points = lv.local_points
    levels = sub_bits + leaf_bits
    lower_width = rank * sub_bits

    pair, cross = pair_ref[...], cross_ref[...]
    step = nrhs * rank * levels // LEAF
    from_pair = unpack_parts(pair, lv.width_e + nrhs, step, rank * levels)
    column_level = lax.broadcasted_iota(jnp.int32, (1, rank * levels), 1) // rank
    lower_level = column_level[:, :lower_width]
    upper_level = column_level[:, : rank * leaf_bits]
    lower = jnp.where(lower_level == 0, from_pair[:, :lower_width], 0.0)
    for mask, got_ref in enumerate(round_one, start=2):
        lower = lower + jnp.where(lower_level == mask.bit_length() - 1, got_ref[:, :lower_width], 0.0)
    upper = None
    for mask, got_ref in enumerate(round_two, start=1):
        term = jnp.where(upper_level == mask.bit_length() - 1, got_ref[...], 0.0)
        upper = term if upper is None else upper + term
    sibling = jnp.concatenate([lower, upper], axis=1)
    factor = jnp.zeros((1, rank * levels), jnp.float32)
    for bit in range(levels):
        factor = jnp.where(column_level == bit, 1.0 / math.sqrt(rank * local_points * 2**bit), factor)
    scaled = (sibling * factor).astype(jnp.bfloat16)
    stacked = basis_ref[loc_bits : loc_bits + levels].reshape(levels * rank, local_points)
    far = nn_dot(scaled, stacked)

    even = lax.axis_index("sub") % 2 == 0
    halo_pair = pair[: lv.width_e + nrhs]
    left, right = jnp.where(even, cross, halo_pair), jnp.where(even, halo_pair, cross)
    halo = {}
    for j, received, offset in ((0, left, -1), (lv.count - 1, right, 1)):
        halo_points = received[: lv.width_e, :]
        halo_float = halo_points.astype(jnp.float32)
        halo_norms = -DISTANCE_SCALE * jnp.sum(halo_float * halo_float, axis=0, keepdims=True)
        weights = lv.block(j, halo_points, halo_norms)
        term = lv.weight(j, offset) * nt_dot(received[lv.width_e :, :], weights)
        halo[j] = term if j not in halo else halo[j] + term
    for j in range(lv.count):
        total = local_ref[:, j * LEAF : (j + 1) * LEAF] + far[:, j * LEAF : (j + 1) * LEAF]
        if j in halo:
            total = total + halo[j]
        out_ref[:, j * LEAF : (j + 1) * LEAF] = total


def on_device(embeddings, directions, level_basis, neighbours, counts):
    axes = ("leaf", "sub")
    width_e = embeddings.shape[0]
    local_points = embeddings.shape[1]
    rank = level_basis.shape[1]
    nrhs = directions.shape[0]
    sub_size = lax.axis_size("sub")
    leaf_size = lax.axis_size("leaf")
    sub_bits = sub_size.bit_length() - 1
    leaf_bits = leaf_size.bit_length() - 1
    dev_bits = sub_bits + leaf_bits
    loc_bits = level_basis.shape[0] - dev_bits

    step = nrhs * rank * dev_bits // LEAF
    pair_shape = jax.ShapeDtypeStruct((width_e + nrhs + 3 * step, LEAF), jnp.bfloat16)
    cross_shape = jax.ShapeDtypeStruct((width_e + nrhs, LEAF), jnp.bfloat16)
    parts_shape = jax.ShapeDtypeStruct((nrhs, rank * dev_bits), jnp.float32)
    pair, cross, parts = pl.pallas_call(
        functools.partial(send_kernel, loc_bits),
        out_shape=(pair_shape, cross_shape, parts_shape),
        in_specs=[VMEM, VMEM, VMEM],
        out_specs=(VMEM, VMEM, VMEM),
    )(embeddings, directions, level_basis)

    ndev = sub_size * leaf_size
    from_pair = lax.ppermute(pair, axes, [(i, i ^ 1) for i in range(ndev)])
    round_one = [from_mask(parts, "sub", mask) for mask in range(2, sub_size)]
    from_cross = lax.ppermute(cross, axes, [(i, i - 1 + 2 * (i % 2)) for i in range(1, ndev - 1)])
    upper = slice(rank * sub_bits, rank * dev_bits)
    line = parts[:, upper] + unpack_parts(from_pair, width_e + nrhs, step, rank * dev_bits)[:, upper]
    for got in round_one:
        line = line + got[:, upper]
    round_two = [from_mask(line, "leaf", mask) for mask in range(1, leaf_size)]

    out = jax.ShapeDtypeStruct((nrhs, local_points), jnp.float32)
    local = pl.pallas_call(
        functools.partial(local_kernel, sub_size),
        out_shape=out,
        in_specs=[VMEM, VMEM, VMEM, SMEM, SMEM],
        out_specs=VMEM,
    )(embeddings, directions, level_basis, neighbours, counts)

    remote = round_one + round_two
    return pl.pallas_call(
        functools.partial(final_kernel, sub_size, sub_bits, leaf_bits, loc_bits),
        out_shape=out,
        in_specs=[VMEM] * 6 + [SMEM, SMEM] + [VMEM] * len(remote),
        out_specs=VMEM,
        input_output_aliases={2: 0},
    )(embeddings, directions, local, from_pair, from_cross, level_basis, neighbours, counts, *remote)


def solution(mesh):
    placed = (
        P(None, ("groups", "leaf", "sub")),
        P(None, ("groups", "leaf", "sub")),
        P(None, None, ("groups", "leaf", "sub")),
        P(("groups", "leaf", "sub"), None),
        P(("groups", "leaf", "sub")),
    )
    return jax.shard_map(
        on_device,
        mesh=mesh,
        in_specs=placed,
        out_specs=P(None, ("groups", "leaf", "sub")),
        check_vma=False,
    )
```

```python
import functools
import math

import jax
import jax.numpy as jnp
from jax import lax
from jax.experimental import pallas as pl
from jax.experimental.pallas import tpu as pltpu
from jax.sharding import PartitionSpec as P

LEAF = 512


AMPLITUDE = 0.5
DISTANCE_SCALE = 0.125
RIDGE = 0.5

VMEM = pl.BlockSpec(memory_space=pltpu.VMEM)
SMEM = pl.BlockSpec(memory_space=pltpu.SMEM)


def from_mask(x, axis, mask):
    pairs = [(i, i ^ mask) for i in range(lax.axis_size(axis))]
    return lax.ppermute(x, axis, pairs)


def nt_dot(a, b):
    return lax.dot_general(a, b, (((1,), (1,)), ((), ())), preferred_element_type=jnp.float32)


def nn_dot(a, b):
    return lax.dot_general(a, b, (((1,), (0,)), ((), ())), preferred_element_type=jnp.float32)


def split_rows(x, width):
    groups = width // x.shape[1]
    step = x.shape[0] // groups
    return jnp.concatenate([x[g * step : (g + 1) * step] for g in range(groups)], axis=1)


def join_rows(x, columns):
    groups = x.shape[1] // columns
    return jnp.concatenate([x[:, g * columns : (g + 1) * columns] for g in range(groups)], axis=0)


def send_kernel(loc_bits, emb_ref, dirs_ref, basis_ref, pair_ref, cross_ref, parts_ref):
    width_e = emb_ref.shape[0]
    local_points = emb_ref.shape[1]
    nrhs = dirs_ref.shape[0]
    values = dirs_ref[...].astype(jnp.bfloat16)
    even = lax.axis_index("sub") % 2 == 0
    head_points, tail_points = emb_ref[:, :LEAF], emb_ref[:, local_points - LEAF :]
    head_values, tail_values = values[:, :LEAF], values[:, local_points - LEAF :]
    pair_ref[:width_e, :] = jnp.where(even, tail_points, head_points)
    pair_ref[width_e : width_e + nrhs, :] = jnp.where(even, tail_values, head_values)
    cross_ref[:width_e, :] = jnp.where(even, head_points, tail_points)
    cross_ref[width_e:, :] = jnp.where(even, head_values, tail_values)
    levels, rank = parts_ref.shape[1] // basis_ref.shape[1], basis_ref.shape[1]
    stacked = basis_ref[loc_bits : loc_bits + levels].reshape(levels * rank, local_points)
    parts = nt_dot(values, stacked)
    parts_ref[...] = parts
    rows = split_rows(parts, LEAF)
    high = rows.astype(jnp.bfloat16)
    rest = rows - high.astype(jnp.float32)
    middle = rest.astype(jnp.bfloat16)
    low = (rest - middle.astype(jnp.float32)).astype(jnp.bfloat16)
    start = width_e + nrhs
    step = rows.shape[0]
    pair_ref[start : start + step, :] = high
    pair_ref[start + step : start + 2 * step, :] = middle
    pair_ref[start + 2 * step : start + 3 * step, :] = low


def unpack_parts(pair, start, step, columns):
    pieces = pair[start : start + 3 * step].astype(jnp.float32)
    rows = (pieces[:step] + pieces[step : 2 * step]) + pieces[2 * step :]
    return join_rows(rows, columns)


class Leaves:
    def __init__(self, emb_ref, dirs_ref, neighbours_ref, counts_ref, sub_size):
        self.width_e = emb_ref.shape[0]
        self.local_points = emb_ref.shape[1]
        self.count = self.local_points // LEAF
        self.directions = dirs_ref[...]
        self.values = self.directions.astype(jnp.bfloat16)
        emb_float = emb_ref[...].astype(jnp.float32)
        row_norms = jnp.sum(emb_float * emb_float, axis=0, keepdims=True)
        emb_t = emb_float.T
        self.col_terms = -DISTANCE_SCALE * jnp.sum(emb_t * emb_t, axis=1, keepdims=True)
        self.emb_t = (emb_t * (2.0 * DISTANCE_SCALE)).astype(jnp.bfloat16)
        self.points = [emb_ref[:, j * LEAF : (j + 1) * LEAF] for j in range(self.count)]
        self.norms = [-DISTANCE_SCALE * row_norms[:, j * LEAF : (j + 1) * LEAF] for j in range(self.count)]
        self.leaf_values = [self.values[:, j * LEAF : (j + 1) * LEAF] for j in range(self.count)]
        self.neighbours_ref = neighbours_ref
        self.counts_ref = counts_ref
        self.me = lax.axis_index("leaf") * sub_size + lax.axis_index("sub")

    def block(self, j, source_points, source_terms):
        inner = nn_dot(self.emb_t[j * LEAF : (j + 1) * LEAF], source_points)
        exponent = (self.col_terms[j * LEAF : (j + 1) * LEAF] + source_terms) + inner
        return (AMPLITUDE * jnp.exp(exponent)).astype(jnp.bfloat16)

    def weight(self, j, offset):
        leaf = self.me * self.count + j
        total = jnp.int32(0)
        for slot in range(self.neighbours_ref.shape[1]):
            hit = (slot < self.counts_ref[j]) & (self.neighbours_ref[j, slot] == leaf + offset)
            total = total + hit.astype(jnp.int32)
        return total.astype(jnp.float32)


def local_kernel(sub_size, emb_ref, dirs_ref, basis_ref, neighbours_ref, counts_ref, out_ref):
    lv = Leaves(emb_ref, dirs_ref, neighbours_ref, counts_ref, sub_size)
    rank = basis_ref.shape[1]
    near = [nt_dot(lv.leaf_values[j], lv.block(j, lv.points[j], lv.norms[j])) for j in range(lv.count)]
    for j in range(lv.count - 1):
        pair = lv.block(j, lv.points[j + 1], lv.norms[j + 1])
        near[j] = near[j] + lv.weight(j, 1) * nt_dot(lv.leaf_values[j + 1], pair)
        near[j + 1] = near[j + 1] + lv.weight(j + 1, -1) * nn_dot(lv.leaf_values[j], pair)
    basis0 = basis_ref[0]
    factor0 = 1.0 / math.sqrt(rank * LEAF)
    scaled0 = [
        (nt_dot(lv.leaf_values[q], basis0[:, q * LEAF : (q + 1) * LEAF]) * factor0).astype(jnp.bfloat16)
        for q in range(lv.count)
    ]
    for q in range(lv.count):
        far0 = nn_dot(scaled0[q ^ 1], basis0[:, q * LEAF : (q + 1) * LEAF])
        out_ref[:, q * LEAF : (q + 1) * LEAF] = (
            RIDGE * lv.directions[:, q * LEAF : (q + 1) * LEAF] + near[q] + far0
        )


def halo_kernel(sub_size, emb_ref, dirs_ref, local_ref, pair_ref, cross_ref, neighbours_ref, counts_ref, out_ref):
    lv = Leaves(emb_ref, dirs_ref, neighbours_ref, counts_ref, sub_size)
    nrhs = dirs_ref.shape[0]
    even = lax.axis_index("sub") % 2 == 0
    halo_pair = pair_ref[: lv.width_e + nrhs, :]
    cross = cross_ref[...]
    left, right = jnp.where(even, cross, halo_pair), jnp.where(even, halo_pair, cross)
    halo = {}
    for j, received, offset in ((0, left, -1), (lv.count - 1, right, 1)):
        halo_points = received[: lv.width_e, :]
        halo_float = halo_points.astype(jnp.float32)
        halo_norms = -DISTANCE_SCALE * jnp.sum(halo_float * halo_float, axis=0, keepdims=True)
        weights = lv.block(j, halo_points, halo_norms)
        term = lv.weight(j, offset) * nt_dot(received[lv.width_e :, :], weights)
        halo[j] = term if j not in halo else halo[j] + term
    for j in range(lv.count):
        total = local_ref[:, j * LEAF : (j + 1) * LEAF]
        if j in halo:
            total = total + halo[j]
        out_ref[:, j * LEAF : (j + 1) * LEAF] = total


def far_kernel(sub_bits, leaf_bits, loc_bits, *refs):
    sub_masks = 2**sub_bits - 1
    leaf_masks = 2**leaf_bits - 1
    near_ref, pair_ref, basis_ref = refs[:3]
    round_one = refs[3 : 3 + sub_masks - 1]
    round_two = refs[3 + sub_masks - 1 : 3 + sub_masks - 1 + leaf_masks]
    out_ref = refs[3 + sub_masks - 1 + leaf_masks]
    rank = basis_ref.shape[1]
    nrhs, local_points = near_ref.shape
    width_e = pair_ref.shape[0] - nrhs - 3 * (nrhs * rank * (sub_bits + leaf_bits) // LEAF)
    levels = sub_bits + leaf_bits
    lower_width = rank * sub_bits

    step = nrhs * rank * levels // LEAF
    from_pair = unpack_parts(pair_ref[...], width_e + nrhs, step, rank * levels)
    column_level = lax.broadcasted_iota(jnp.int32, (1, rank * levels), 1) // rank
    lower_level = column_level[:, :lower_width]
    upper_level = column_level[:, : rank * leaf_bits]
    lower = jnp.where(lower_level == 0, from_pair[:, :lower_width], 0.0)
    for mask, got_ref in enumerate(round_one, start=2):
        lower = lower + jnp.where(lower_level == mask.bit_length() - 1, got_ref[:, :lower_width], 0.0)
    upper = None
    for mask, got_ref in enumerate(round_two, start=1):
        term = jnp.where(upper_level == mask.bit_length() - 1, got_ref[...], 0.0)
        upper = term if upper is None else upper + term
    sibling = jnp.concatenate([lower, upper], axis=1)
    factor = jnp.zeros((1, rank * levels), jnp.float32)
    for bit in range(levels):
        factor = jnp.where(column_level == bit, 1.0 / math.sqrt(rank * local_points * 2**bit), factor)
    scaled = (sibling * factor).astype(jnp.bfloat16)
    stacked = basis_ref[loc_bits : loc_bits + levels].reshape(levels * rank, local_points)
    out_ref[...] = near_ref[...] + nn_dot(scaled, stacked)


def on_device(embeddings, directions, level_basis, neighbours, counts):
    axes = ("leaf", "sub")
    width_e = embeddings.shape[0]
    local_points = embeddings.shape[1]
    rank = level_basis.shape[1]
    nrhs = directions.shape[0]
    sub_size = lax.axis_size("sub")
    leaf_size = lax.axis_size("leaf")
    sub_bits = sub_size.bit_length() - 1
    leaf_bits = leaf_size.bit_length() - 1
    dev_bits = sub_bits + leaf_bits
    loc_bits = level_basis.shape[0] - dev_bits

    step = nrhs * rank * dev_bits // LEAF
    pair_shape = jax.ShapeDtypeStruct((width_e + nrhs + 3 * step, LEAF), jnp.bfloat16)
    cross_shape = jax.ShapeDtypeStruct((width_e + nrhs, LEAF), jnp.bfloat16)
    parts_shape = jax.ShapeDtypeStruct((nrhs, rank * dev_bits), jnp.float32)
    pair, cross, parts = pl.pallas_call(
        functools.partial(send_kernel, loc_bits),
        out_shape=(pair_shape, cross_shape, parts_shape),
        in_specs=[VMEM, VMEM, VMEM],
        out_specs=(VMEM, VMEM, VMEM),
    )(embeddings, directions, level_basis)

    ndev = sub_size * leaf_size
    from_pair = lax.ppermute(pair, axes, [(i, i ^ 1) for i in range(ndev)])
    round_one = [from_mask(parts, "sub", mask) for mask in range(2, sub_size)]
    from_cross = lax.ppermute(cross, axes, [(i, i - 1 + 2 * (i % 2)) for i in range(1, ndev - 1)])
    out = jax.ShapeDtypeStruct((nrhs, local_points), jnp.float32)
    local = pl.pallas_call(
        functools.partial(local_kernel, sub_size),
        out_shape=out,
        in_specs=[VMEM, VMEM, VMEM, SMEM, SMEM],
        out_specs=VMEM,
    )(embeddings, directions, level_basis, neighbours, counts)
    local, from_pair, *round_one = lax.optimization_barrier((local, from_pair, *round_one))
    upper = slice(rank * sub_bits, rank * dev_bits)
    line = parts[:, upper] + unpack_parts(from_pair, width_e + nrhs, step, rank * dev_bits)[:, upper]
    for got in round_one:
        line = line + got[:, upper]
    round_two = [from_mask(line, "leaf", mask) for mask in range(1, leaf_size)]

    near = pl.pallas_call(
        functools.partial(halo_kernel, sub_size),
        out_shape=out,
        in_specs=[VMEM] * 5 + [SMEM, SMEM],
        out_specs=VMEM,
        input_output_aliases={2: 0},
    )(embeddings, directions, local, from_pair, from_cross, neighbours, counts)
    remote = round_one + round_two
    return pl.pallas_call(
        functools.partial(far_kernel, sub_bits, leaf_bits, loc_bits),
        out_shape=out,
        in_specs=[VMEM] * (3 + len(remote)),
        out_specs=VMEM,
        input_output_aliases={0: 0},
    )(near, from_pair, level_basis, *remote)


def solution(mesh):
    placed = (
        P(None, ("groups", "leaf", "sub")),
        P(None, ("groups", "leaf", "sub")),
        P(None, None, ("groups", "leaf", "sub")),
        P(("groups", "leaf", "sub"), None),
        P(("groups", "leaf", "sub")),
    )
    return jax.shard_map(
        on_device,
        mesh=mesh,
        in_specs=placed,
        out_specs=P(None, ("groups", "leaf", "sub")),
        check_vma=False,
    )
```

```python
import functools
import math

import jax
import jax.numpy as jnp
from jax import lax
from jax.experimental import pallas as pl
from jax.experimental.pallas import tpu as pltpu
from jax.sharding import PartitionSpec as P

LEAF = 512


AMPLITUDE = 0.5
DISTANCE_SCALE = 0.125
RIDGE = 0.5

VMEM = pl.BlockSpec(memory_space=pltpu.VMEM)
SMEM = pl.BlockSpec(memory_space=pltpu.SMEM)


def from_mask(x, axis, mask):
    pairs = [(i, i ^ mask) for i in range(lax.axis_size(axis))]
    return lax.ppermute(x, axis, pairs)


def in_vmem(*arrays):
    return [pltpu.with_memory_space_constraint(a, pltpu.VMEM) for a in arrays]


def nt_dot(a, b):
    return lax.dot_general(a, b, (((1,), (1,)), ((), ())), preferred_element_type=jnp.float32)


def nn_dot(a, b):
    return lax.dot_general(a, b, (((1,), (0,)), ((), ())), preferred_element_type=jnp.float32)


def split_rows(x, width):
    groups = width // x.shape[1]
    step = x.shape[0] // groups
    return jnp.concatenate([x[g * step : (g + 1) * step] for g in range(groups)], axis=1)


def join_rows(x, columns):
    groups = x.shape[1] // columns
    return jnp.concatenate([x[:, g * columns : (g + 1) * columns] for g in range(groups)], axis=0)


def send_kernel(loc_bits, emb_ref, dirs_ref, basis_ref, pair_ref, cross_ref, parts_ref):
    width_e = emb_ref.shape[0]
    local_points = emb_ref.shape[1]
    nrhs = dirs_ref.shape[0]
    values = dirs_ref[...].astype(jnp.bfloat16)
    even = lax.axis_index("sub") % 2 == 0
    head_points, tail_points = emb_ref[:, :LEAF], emb_ref[:, local_points - LEAF :]
    head_values, tail_values = values[:, :LEAF], values[:, local_points - LEAF :]
    pair_ref[:width_e, :] = jnp.where(even, tail_points, head_points)
    pair_ref[width_e : width_e + nrhs, :] = jnp.where(even, tail_values, head_values)
    cross_ref[:width_e, :] = jnp.where(even, head_points, tail_points)
    cross_ref[width_e:, :] = jnp.where(even, head_values, tail_values)
    levels, rank = parts_ref.shape[1] // basis_ref.shape[1], basis_ref.shape[1]
    stacked = basis_ref[loc_bits : loc_bits + levels].reshape(levels * rank, local_points)
    parts = nt_dot(values, stacked)
    parts_ref[...] = parts
    rows = split_rows(parts, LEAF)
    high = rows.astype(jnp.bfloat16)
    rest = rows - high.astype(jnp.float32)
    middle = rest.astype(jnp.bfloat16)
    low = (rest - middle.astype(jnp.float32)).astype(jnp.bfloat16)
    start = width_e + nrhs
    step = rows.shape[0]
    pair_ref[start : start + step, :] = high
    pair_ref[start + step : start + 2 * step, :] = middle
    pair_ref[start + 2 * step : start + 3 * step, :] = low


def unpack_parts(pair, start, step, columns):
    pieces = pair[start : start + 3 * step].astype(jnp.float32)
    rows = (pieces[:step] + pieces[step : 2 * step]) + pieces[2 * step :]
    return join_rows(rows, columns)


class Leaves:
    def __init__(self, emb_ref, dirs_ref, neighbours_ref, counts_ref, sub_size):
        self.width_e = emb_ref.shape[0]
        self.local_points = emb_ref.shape[1]
        self.count = self.local_points // LEAF
        self.directions = dirs_ref[...]
        self.values = self.directions.astype(jnp.bfloat16)
        emb_float = emb_ref[...].astype(jnp.float32)
        row_norms = jnp.sum(emb_float * emb_float, axis=0, keepdims=True)
        emb_t = emb_float.T
        self.col_terms = -DISTANCE_SCALE * jnp.sum(emb_t * emb_t, axis=1, keepdims=True)
        self.emb_t = (emb_t * (2.0 * DISTANCE_SCALE)).astype(jnp.bfloat16)
        self.points = [emb_ref[:, j * LEAF : (j + 1) * LEAF] for j in range(self.count)]
        self.norms = [-DISTANCE_SCALE * row_norms[:, j * LEAF : (j + 1) * LEAF] for j in range(self.count)]
        self.leaf_values = [self.values[:, j * LEAF : (j + 1) * LEAF] for j in range(self.count)]
        self.neighbours_ref = neighbours_ref
        self.counts_ref = counts_ref
        self.me = lax.axis_index("leaf") * sub_size + lax.axis_index("sub")

    def block(self, j, source_points, source_terms):
        inner = nn_dot(self.emb_t[j * LEAF : (j + 1) * LEAF], source_points)
        exponent = (self.col_terms[j * LEAF : (j + 1) * LEAF] + source_terms) + inner
        return (AMPLITUDE * jnp.exp(exponent)).astype(jnp.bfloat16)

    def weight(self, j, offset):
        leaf = self.me * self.count + j
        total = jnp.int32(0)
        for slot in range(self.neighbours_ref.shape[1]):
            hit = (slot < self.counts_ref[j]) & (self.neighbours_ref[j, slot] == leaf + offset)
            total = total + hit.astype(jnp.int32)
        return total.astype(jnp.float32)


def local_kernel(sub_size, emb_ref, dirs_ref, basis_ref, neighbours_ref, counts_ref, out_ref):
    lv = Leaves(emb_ref, dirs_ref, neighbours_ref, counts_ref, sub_size)
    rank = basis_ref.shape[1]
    near = [nt_dot(lv.leaf_values[j], lv.block(j, lv.points[j], lv.norms[j])) for j in range(lv.count)]
    for j in range(lv.count - 1):
        pair = lv.block(j, lv.points[j + 1], lv.norms[j + 1])
        near[j] = near[j] + lv.weight(j, 1) * nt_dot(lv.leaf_values[j + 1], pair)
        near[j + 1] = near[j + 1] + lv.weight(j + 1, -1) * nn_dot(lv.leaf_values[j], pair)
    basis0 = basis_ref[0]
    factor0 = 1.0 / math.sqrt(rank * LEAF)
    scaled0 = [
        (nt_dot(lv.leaf_values[q], basis0[:, q * LEAF : (q + 1) * LEAF]) * factor0).astype(jnp.bfloat16)
        for q in range(lv.count)
    ]
    for q in range(lv.count):
        far0 = nn_dot(scaled0[q ^ 1], basis0[:, q * LEAF : (q + 1) * LEAF])
        out_ref[:, q * LEAF : (q + 1) * LEAF] = (
            RIDGE * lv.directions[:, q * LEAF : (q + 1) * LEAF] + near[q] + far0
        )


def final_kernel(sub_size, sub_bits, leaf_bits, loc_bits, *refs):
    sub_masks = 2**sub_bits - 1
    leaf_masks = 2**leaf_bits - 1
    emb_ref, dirs_ref, local_ref, pair_ref, cross_ref, basis_ref, neighbours_ref, counts_ref = refs[:8]
    round_one = refs[8 : 8 + sub_masks - 1]
    round_two = refs[8 + sub_masks - 1 : 8 + sub_masks - 1 + leaf_masks]
    out_ref = refs[8 + sub_masks - 1 + leaf_masks]
    lv = Leaves(emb_ref, dirs_ref, neighbours_ref, counts_ref, sub_size)
    rank = basis_ref.shape[1]
    nrhs = dirs_ref.shape[0]
    local_points = lv.local_points
    levels = sub_bits + leaf_bits
    lower_width = rank * sub_bits

    pair, cross = pair_ref[...], cross_ref[...]
    step = nrhs * rank * levels // LEAF
    from_pair = unpack_parts(pair, lv.width_e + nrhs, step, rank * levels)
    column_level = lax.broadcasted_iota(jnp.int32, (1, rank * levels), 1) // rank
    lower_level = column_level[:, :lower_width]
    upper_level = column_level[:, : rank * leaf_bits]
    lower = jnp.where(lower_level == 0, from_pair[:, :lower_width], 0.0)
    for mask, got_ref in enumerate(round_one, start=2):
        lower = lower + jnp.where(lower_level == mask.bit_length() - 1, got_ref[:, :lower_width], 0.0)
    upper = None
    for mask, got_ref in enumerate(round_two, start=1):
        term = jnp.where(upper_level == mask.bit_length() - 1, got_ref[...], 0.0)
        upper = term if upper is None else upper + term
    sibling = jnp.concatenate([lower, upper], axis=1)
    factor = jnp.zeros((1, rank * levels), jnp.float32)
    for bit in range(levels):
        factor = jnp.where(column_level == bit, 1.0 / math.sqrt(rank * local_points * 2**bit), factor)
    scaled = (sibling * factor).astype(jnp.bfloat16)
    stacked = basis_ref[loc_bits : loc_bits + levels].reshape(levels * rank, local_points)
    far = nn_dot(scaled, stacked)

    even = lax.axis_index("sub") % 2 == 0
    halo_pair = pair[: lv.width_e + nrhs]
    left, right = jnp.where(even, cross, halo_pair), jnp.where(even, halo_pair, cross)
    halo = {}
    for j, received, offset in ((0, left, -1), (lv.count - 1, right, 1)):
        halo_points = received[: lv.width_e, :]
        halo_float = halo_points.astype(jnp.float32)
        halo_norms = -DISTANCE_SCALE * jnp.sum(halo_float * halo_float, axis=0, keepdims=True)
        weights = lv.block(j, halo_points, halo_norms)
        term = lv.weight(j, offset) * nt_dot(received[lv.width_e :, :], weights)
        halo[j] = term if j not in halo else halo[j] + term
    for j in range(lv.count):
        total = local_ref[:, j * LEAF : (j + 1) * LEAF] + far[:, j * LEAF : (j + 1) * LEAF]
        if j in halo:
            total = total + halo[j]
        out_ref[:, j * LEAF : (j + 1) * LEAF] = total


def on_device(embeddings, directions, level_basis, neighbours, counts):
    axes = ("leaf", "sub")
    width_e = embeddings.shape[0]
    local_points = embeddings.shape[1]
    rank = level_basis.shape[1]
    nrhs = directions.shape[0]
    sub_size = lax.axis_size("sub")
    leaf_size = lax.axis_size("leaf")
    sub_bits = sub_size.bit_length() - 1
    leaf_bits = leaf_size.bit_length() - 1
    dev_bits = sub_bits + leaf_bits
    loc_bits = level_basis.shape[0] - dev_bits

    step = nrhs * rank * dev_bits // LEAF
    pair_shape = jax.ShapeDtypeStruct((width_e + nrhs + 3 * step, LEAF), jnp.bfloat16)
    cross_shape = jax.ShapeDtypeStruct((width_e + nrhs, LEAF), jnp.bfloat16)
    parts_shape = jax.ShapeDtypeStruct((nrhs, rank * dev_bits), jnp.float32)
    pair, cross, parts = pl.pallas_call(
        functools.partial(send_kernel, loc_bits),
        out_shape=(pair_shape, cross_shape, parts_shape),
        in_specs=[VMEM, VMEM, VMEM],
        out_specs=(VMEM, VMEM, VMEM),
    )(embeddings, directions, level_basis)

    ndev = sub_size * leaf_size
    from_pair = lax.ppermute(pair, axes, [(i, i ^ 1) for i in range(ndev)])
    round_one = [from_mask(parts, "sub", mask) for mask in range(2, sub_size)]
    from_cross = lax.ppermute(cross, axes, [(i, i - 1 + 2 * (i % 2)) for i in range(1, ndev - 1)])
    upper = slice(rank * sub_bits, rank * dev_bits)
    line = parts[:, upper] + unpack_parts(from_pair, width_e + nrhs, step, rank * dev_bits)[:, upper]
    for got in round_one:
        line = line + got[:, upper]
    round_two = [from_mask(line, "leaf", mask) for mask in range(1, leaf_size)]

    out = jax.ShapeDtypeStruct((nrhs, local_points), jnp.float32)
    local = pl.pallas_call(
        functools.partial(local_kernel, sub_size),
        out_shape=out,
        in_specs=[VMEM, VMEM, VMEM, SMEM, SMEM],
        out_specs=VMEM,
    )(embeddings, directions, level_basis, neighbours, counts)

    remote = round_one + round_two
    return pl.pallas_call(
        functools.partial(final_kernel, sub_size, sub_bits, leaf_bits, loc_bits),
        out_shape=out,
        in_specs=[VMEM] * 6 + [SMEM, SMEM] + [VMEM] * len(remote),
        out_specs=VMEM,
        input_output_aliases={2: 0},
    )(
        embeddings,
        directions,
        local,
        *in_vmem(from_pair, from_cross),
        level_basis,
        neighbours,
        counts,
        *in_vmem(*remote),
    )


def solution(mesh):
    placed = (
        P(None, ("groups", "leaf", "sub")),
        P(None, ("groups", "leaf", "sub")),
        P(None, None, ("groups", "leaf", "sub")),
        P(("groups", "leaf", "sub"), None),
        P(("groups", "leaf", "sub")),
    )
    return jax.shard_map(
        on_device,
        mesh=mesh,
        in_specs=placed,
        out_specs=P(None, ("groups", "leaf", "sub")),
        check_vma=False,
    )
```

```python
import functools
import math

import jax
import jax.numpy as jnp
from jax import lax
from jax.experimental import pallas as pl
from jax.experimental.pallas import tpu as pltpu
from jax.sharding import PartitionSpec as P

LEAF = 512


AMPLITUDE = 0.5
DISTANCE_SCALE = 0.125
RIDGE = 0.5

VMEM = pl.BlockSpec(memory_space=pltpu.VMEM)
SMEM = pl.BlockSpec(memory_space=pltpu.SMEM)


def from_mask(x, axis, mask):
    pairs = [(i, i ^ mask) for i in range(lax.axis_size(axis))]
    return lax.ppermute(x, axis, pairs)


def in_vmem(*arrays):
    return [pltpu.with_memory_space_constraint(a, pltpu.VMEM) for a in arrays]


def nt_dot(a, b):
    return lax.dot_general(a, b, (((1,), (1,)), ((), ())), preferred_element_type=jnp.float32)


def nn_dot(a, b):
    return lax.dot_general(a, b, (((1,), (0,)), ((), ())), preferred_element_type=jnp.float32)


def split_rows(x, width):
    groups = width // x.shape[1]
    step = x.shape[0] // groups
    return jnp.concatenate([x[g * step : (g + 1) * step] for g in range(groups)], axis=1)


def join_rows(x, columns):
    groups = x.shape[1] // columns
    return jnp.concatenate([x[:, g * columns : (g + 1) * columns] for g in range(groups)], axis=0)


def send_kernel(loc_bits, emb_ref, dirs_ref, basis_ref, pair_ref, cross_ref, parts_ref):
    width_e = emb_ref.shape[0]
    local_points = emb_ref.shape[1]
    nrhs = dirs_ref.shape[0]
    values = dirs_ref[...].astype(jnp.bfloat16)
    even = lax.axis_index("sub") % 2 == 0
    head_points, tail_points = emb_ref[:, :LEAF], emb_ref[:, local_points - LEAF :]
    head_values, tail_values = values[:, :LEAF], values[:, local_points - LEAF :]
    pair_ref[:width_e, :] = jnp.where(even, tail_points, head_points)
    pair_ref[width_e : width_e + nrhs, :] = jnp.where(even, tail_values, head_values)
    cross_ref[:width_e, :] = jnp.where(even, head_points, tail_points)
    cross_ref[width_e:, :] = jnp.where(even, head_values, tail_values)
    levels, rank = parts_ref.shape[1] // basis_ref.shape[1], basis_ref.shape[1]
    stacked = basis_ref[loc_bits : loc_bits + levels].reshape(levels * rank, local_points)
    parts = nt_dot(values, stacked)
    parts_ref[...] = parts
    rows = split_rows(parts, LEAF)
    high = rows.astype(jnp.bfloat16)
    rest = rows - high.astype(jnp.float32)
    middle = rest.astype(jnp.bfloat16)
    low = (rest - middle.astype(jnp.float32)).astype(jnp.bfloat16)
    start = width_e + nrhs
    step = rows.shape[0]
    pair_ref[start : start + step, :] = high
    pair_ref[start + step : start + 2 * step, :] = middle
    pair_ref[start + 2 * step : start + 3 * step, :] = low


def unpack_parts(pair, start, step, columns):
    pieces = pair[start : start + 3 * step].astype(jnp.float32)
    rows = (pieces[:step] + pieces[step : 2 * step]) + pieces[2 * step :]
    return join_rows(rows, columns)


class Leaves:
    def __init__(self, emb_ref, dirs_ref, neighbours_ref, counts_ref, sub_size):
        self.width_e = emb_ref.shape[0]
        self.local_points = emb_ref.shape[1]
        self.count = self.local_points // LEAF
        self.directions = dirs_ref[...]
        self.values = self.directions.astype(jnp.bfloat16)
        emb_float = emb_ref[...].astype(jnp.float32)
        row_norms = jnp.sum(emb_float * emb_float, axis=0, keepdims=True)
        emb_t = emb_float.T
        self.col_terms = -DISTANCE_SCALE * jnp.sum(emb_t * emb_t, axis=1, keepdims=True)
        self.emb_t = (emb_t * (2.0 * DISTANCE_SCALE)).astype(jnp.bfloat16)
        self.points = [emb_ref[:, j * LEAF : (j + 1) * LEAF] for j in range(self.count)]
        self.norms = [-DISTANCE_SCALE * row_norms[:, j * LEAF : (j + 1) * LEAF] for j in range(self.count)]
        self.leaf_values = [self.values[:, j * LEAF : (j + 1) * LEAF] for j in range(self.count)]
        self.neighbours_ref = neighbours_ref
        self.counts_ref = counts_ref
        self.me = lax.axis_index("leaf") * sub_size + lax.axis_index("sub")

    def block(self, j, source_points, source_terms):
        inner = nn_dot(self.emb_t[j * LEAF : (j + 1) * LEAF], source_points)
        exponent = (self.col_terms[j * LEAF : (j + 1) * LEAF] + source_terms) + inner
        return (AMPLITUDE * jnp.exp(exponent)).astype(jnp.bfloat16)

    def weight(self, j, offset):
        leaf = self.me * self.count + j
        total = jnp.int32(0)
        for slot in range(self.neighbours_ref.shape[1]):
            hit = (slot < self.counts_ref[j]) & (self.neighbours_ref[j, slot] == leaf + offset)
            total = total + hit.astype(jnp.int32)
        return total.astype(jnp.float32)


def local_kernel(sub_size, emb_ref, dirs_ref, basis_ref, neighbours_ref, counts_ref, out_ref):
    lv = Leaves(emb_ref, dirs_ref, neighbours_ref, counts_ref, sub_size)
    rank = basis_ref.shape[1]
    near = [nt_dot(lv.leaf_values[j], lv.block(j, lv.points[j], lv.norms[j])) for j in range(lv.count)]
    for j in range(lv.count - 1):
        pair = lv.block(j, lv.points[j + 1], lv.norms[j + 1])
        near[j] = near[j] + lv.weight(j, 1) * nt_dot(lv.leaf_values[j + 1], pair)
        near[j + 1] = near[j + 1] + lv.weight(j + 1, -1) * nn_dot(lv.leaf_values[j], pair)
    basis0 = basis_ref[0]
    factor0 = 1.0 / math.sqrt(rank * LEAF)
    scaled0 = [
        (nt_dot(lv.leaf_values[q], basis0[:, q * LEAF : (q + 1) * LEAF]) * factor0).astype(jnp.bfloat16)
        for q in range(lv.count)
    ]
    for q in range(lv.count):
        far0 = nn_dot(scaled0[q ^ 1], basis0[:, q * LEAF : (q + 1) * LEAF])
        out_ref[:, q * LEAF : (q + 1) * LEAF] = (
            RIDGE * lv.directions[:, q * LEAF : (q + 1) * LEAF] + near[q] + far0
        )


def final_kernel(sub_size, sub_bits, leaf_bits, loc_bits, *refs):
    sub_masks = 2**sub_bits - 1
    leaf_masks = 2**leaf_bits - 1
    emb_ref, dirs_ref, local_ref, pair_ref, cross_ref, basis_ref, neighbours_ref, counts_ref = refs[:8]
    round_one = refs[8 : 8 + sub_masks - 1]
    round_two = refs[8 + sub_masks - 1 : 8 + sub_masks - 1 + leaf_masks]
    out_ref = refs[8 + sub_masks - 1 + leaf_masks]
    lv = Leaves(emb_ref, dirs_ref, neighbours_ref, counts_ref, sub_size)
    rank = basis_ref.shape[1]
    nrhs = dirs_ref.shape[0]
    local_points = lv.local_points
    levels = sub_bits + leaf_bits
    lower_width = rank * sub_bits

    pair, cross = pair_ref[...], cross_ref[...]
    step = nrhs * rank * levels // LEAF
    from_pair = unpack_parts(pair, lv.width_e + nrhs, step, rank * levels)
    column_level = lax.broadcasted_iota(jnp.int32, (1, rank * levels), 1) // rank
    lower_level = column_level[:, :lower_width]
    upper_level = column_level[:, : rank * leaf_bits]
    lower = jnp.where(lower_level == 0, from_pair[:, :lower_width], 0.0)
    for mask, got_ref in enumerate(round_one, start=2):
        lower = lower + jnp.where(lower_level == mask.bit_length() - 1, got_ref[:, :lower_width], 0.0)
    upper = None
    for mask, got_ref in enumerate(round_two, start=1):
        term = jnp.where(upper_level == mask.bit_length() - 1, got_ref[...], 0.0)
        upper = term if upper is None else upper + term
    sibling = jnp.concatenate([lower, upper], axis=1)
    factor = jnp.zeros((1, rank * levels), jnp.float32)
    for bit in range(levels):
        factor = jnp.where(column_level == bit, 1.0 / math.sqrt(rank * local_points * 2**bit), factor)
    scaled = (sibling * factor).astype(jnp.bfloat16)
    stacked = basis_ref[loc_bits : loc_bits + levels].reshape(levels * rank, local_points)
    far = nn_dot(scaled, stacked)

    even = lax.axis_index("sub") % 2 == 0
    halo_pair = pair[: lv.width_e + nrhs]
    left, right = jnp.where(even, cross, halo_pair), jnp.where(even, halo_pair, cross)
    halo = {}
    for j, received, offset in ((0, left, -1), (lv.count - 1, right, 1)):
        halo_points = received[: lv.width_e, :]
        halo_float = halo_points.astype(jnp.float32)
        halo_norms = -DISTANCE_SCALE * jnp.sum(halo_float * halo_float, axis=0, keepdims=True)
        weights = lv.block(j, halo_points, halo_norms)
        term = lv.weight(j, offset) * nt_dot(received[lv.width_e :, :], weights)
        halo[j] = term if j not in halo else halo[j] + term
    for j in range(lv.count):
        total = local_ref[:, j * LEAF : (j + 1) * LEAF] + far[:, j * LEAF : (j + 1) * LEAF]
        if j in halo:
            total = total + halo[j]
        out_ref[:, j * LEAF : (j + 1) * LEAF] = total


def on_device(embeddings, directions, level_basis, neighbours, counts):
    axes = ("leaf", "sub")
    width_e = embeddings.shape[0]
    local_points = embeddings.shape[1]
    rank = level_basis.shape[1]
    nrhs = directions.shape[0]
    sub_size = lax.axis_size("sub")
    leaf_size = lax.axis_size("leaf")
    sub_bits = sub_size.bit_length() - 1
    leaf_bits = leaf_size.bit_length() - 1
    dev_bits = sub_bits + leaf_bits
    loc_bits = level_basis.shape[0] - dev_bits

    step = nrhs * rank * dev_bits // LEAF
    pair_shape = jax.ShapeDtypeStruct((width_e + nrhs + 3 * step, LEAF), jnp.bfloat16)
    cross_shape = jax.ShapeDtypeStruct((width_e + nrhs, LEAF), jnp.bfloat16)
    parts_shape = jax.ShapeDtypeStruct((nrhs, rank * dev_bits), jnp.float32)
    pair, cross, parts = pl.pallas_call(
        functools.partial(send_kernel, loc_bits),
        out_shape=(pair_shape, cross_shape, parts_shape),
        in_specs=[VMEM, VMEM, VMEM],
        out_specs=(VMEM, VMEM, VMEM),
    )(embeddings, directions, level_basis)

    ndev = sub_size * leaf_size
    from_pair = lax.ppermute(pair, axes, [(i, i ^ 1) for i in range(ndev)])
    round_one = [from_mask(parts, "sub", mask) for mask in range(2, sub_size)]
    from_cross = lax.ppermute(cross, axes, [(i, i - 1 + 2 * (i % 2)) for i in range(1, ndev - 1)])
    upper = slice(rank * sub_bits, rank * dev_bits)
    line = parts[:, upper] + unpack_parts(from_pair, width_e + nrhs, step, rank * dev_bits)[:, upper]
    for got in round_one:
        line = line + got[:, upper]
    round_two = [from_mask(line, "leaf", mask) for mask in range(1, leaf_size)]

    out = jax.ShapeDtypeStruct((nrhs, local_points), jnp.float32)
    local = pl.pallas_call(
        functools.partial(local_kernel, sub_size),
        out_shape=out,
        in_specs=[VMEM, VMEM, VMEM, SMEM, SMEM],
        out_specs=VMEM,
    )(*in_vmem(embeddings, directions, level_basis), neighbours, counts)

    remote = round_one + round_two
    return pl.pallas_call(
        functools.partial(final_kernel, sub_size, sub_bits, leaf_bits, loc_bits),
        out_shape=out,
        in_specs=[VMEM] * 6 + [SMEM, SMEM] + [VMEM] * len(remote),
        out_specs=VMEM,
        input_output_aliases={2: 0},
    )(
        *in_vmem(embeddings, directions, local, from_pair, from_cross, level_basis),
        neighbours,
        counts,
        *in_vmem(*remote),
    )


def solution(mesh):
    placed = (
        P(None, ("groups", "leaf", "sub")),
        P(None, ("groups", "leaf", "sub")),
        P(None, None, ("groups", "leaf", "sub")),
        P(("groups", "leaf", "sub"), None),
        P(("groups", "leaf", "sub")),
    )
    return jax.shard_map(
        on_device,
        mesh=mesh,
        in_specs=placed,
        out_specs=P(None, ("groups", "leaf", "sub")),
        check_vma=False,
    )
```

```python
import functools
import math

import jax
import jax.numpy as jnp
from jax import lax
from jax.experimental import pallas as pl
from jax.experimental.pallas import tpu as pltpu
from jax.sharding import PartitionSpec as P

LEAF = 512


AMPLITUDE = 0.5
DISTANCE_SCALE = 0.125
RIDGE = 0.5

VMEM = pl.BlockSpec(memory_space=pltpu.VMEM)
SMEM = pl.BlockSpec(memory_space=pltpu.SMEM)


def from_mask(x, axis, mask):
    pairs = [(i, i ^ mask) for i in range(lax.axis_size(axis))]
    return lax.ppermute(x, axis, pairs)


def in_vmem(*arrays):
    return [pltpu.with_memory_space_constraint(a, pltpu.VMEM) for a in arrays]


def nt_dot(a, b):
    return lax.dot_general(a, b, (((1,), (1,)), ((), ())), preferred_element_type=jnp.float32)


def nn_dot(a, b):
    return lax.dot_general(a, b, (((1,), (0,)), ((), ())), preferred_element_type=jnp.float32)


def split_rows(x, width):
    groups = width // x.shape[1]
    step = x.shape[0] // groups
    return jnp.concatenate([x[g * step : (g + 1) * step] for g in range(groups)], axis=1)


def join_rows(x, columns):
    groups = x.shape[1] // columns
    return jnp.concatenate([x[:, g * columns : (g + 1) * columns] for g in range(groups)], axis=0)


def send_kernel(loc_bits, emb_ref, dirs_ref, basis_ref, pair_ref, cross_ref, parts_ref):
    width_e = emb_ref.shape[0]
    local_points = emb_ref.shape[1]
    nrhs = dirs_ref.shape[0]
    values = dirs_ref[...].astype(jnp.bfloat16)
    even = lax.axis_index("sub") % 2 == 0
    head_points, tail_points = emb_ref[:, :LEAF], emb_ref[:, local_points - LEAF :]
    head_values, tail_values = values[:, :LEAF], values[:, local_points - LEAF :]
    pair_ref[:width_e, :] = jnp.where(even, tail_points, head_points)
    pair_ref[width_e : width_e + nrhs, :] = jnp.where(even, tail_values, head_values)
    cross_ref[:width_e, :] = jnp.where(even, head_points, tail_points)
    cross_ref[width_e:, :] = jnp.where(even, head_values, tail_values)
    levels, rank = parts_ref.shape[1] // basis_ref.shape[1], basis_ref.shape[1]
    stacked = basis_ref[loc_bits : loc_bits + levels].reshape(levels * rank, local_points)
    parts = nt_dot(values, stacked)
    parts_ref[...] = parts
    rows = split_rows(parts, LEAF)
    high = rows.astype(jnp.bfloat16)
    rest = rows - high.astype(jnp.float32)
    middle = rest.astype(jnp.bfloat16)
    low = (rest - middle.astype(jnp.float32)).astype(jnp.bfloat16)
    start = width_e + nrhs
    step = rows.shape[0]
    pair_ref[start : start + step, :] = high
    pair_ref[start + step : start + 2 * step, :] = middle
    pair_ref[start + 2 * step : start + 3 * step, :] = low


def unpack_parts(pair, start, step, columns):
    pieces = pair[start : start + 3 * step].astype(jnp.float32)
    rows = (pieces[:step] + pieces[step : 2 * step]) + pieces[2 * step :]
    return join_rows(rows, columns)


class Leaves:
    def __init__(self, emb_ref, dirs_ref, neighbours_ref, counts_ref, sub_size):
        self.width_e = emb_ref.shape[0]
        self.local_points = emb_ref.shape[1]
        self.count = self.local_points // LEAF
        self.directions = dirs_ref[...]
        self.values = self.directions.astype(jnp.bfloat16)
        emb_float = emb_ref[...].astype(jnp.float32)
        row_norms = jnp.sum(emb_float * emb_float, axis=0, keepdims=True)
        emb_t = emb_float.T
        self.col_terms = -DISTANCE_SCALE * jnp.sum(emb_t * emb_t, axis=1, keepdims=True)
        self.emb_t = (emb_t * (2.0 * DISTANCE_SCALE)).astype(jnp.bfloat16)
        self.points = [emb_ref[:, j * LEAF : (j + 1) * LEAF] for j in range(self.count)]
        self.norms = [-DISTANCE_SCALE * row_norms[:, j * LEAF : (j + 1) * LEAF] for j in range(self.count)]
        self.leaf_values = [self.values[:, j * LEAF : (j + 1) * LEAF] for j in range(self.count)]
        self.neighbours_ref = neighbours_ref
        self.counts_ref = counts_ref
        self.me = lax.axis_index("leaf") * sub_size + lax.axis_index("sub")

    def block(self, j, source_points, source_terms):
        inner = nn_dot(self.emb_t[j * LEAF : (j + 1) * LEAF], source_points)
        exponent = (self.col_terms[j * LEAF : (j + 1) * LEAF] + source_terms) + inner
        return (AMPLITUDE * jnp.exp(exponent)).astype(jnp.bfloat16)

    def weight(self, j, offset):
        leaf = self.me * self.count + j
        total = jnp.int32(0)
        for slot in range(self.neighbours_ref.shape[1]):
            hit = (slot < self.counts_ref[j]) & (self.neighbours_ref[j, slot] == leaf + offset)
            total = total + hit.astype(jnp.int32)
        return total.astype(jnp.float32)


def local_kernel(sub_size, emb_ref, dirs_ref, basis_ref, neighbours_ref, counts_ref, out_ref):
    lv = Leaves(emb_ref, dirs_ref, neighbours_ref, counts_ref, sub_size)
    rank = basis_ref.shape[1]
    near = [nt_dot(lv.leaf_values[j], lv.block(j, lv.points[j], lv.norms[j])) for j in range(lv.count)]
    for j in range(lv.count - 1):
        pair = lv.block(j, lv.points[j + 1], lv.norms[j + 1])
        near[j] = near[j] + lv.weight(j, 1) * nt_dot(lv.leaf_values[j + 1], pair)
        near[j + 1] = near[j + 1] + lv.weight(j + 1, -1) * nn_dot(lv.leaf_values[j], pair)
    basis0 = basis_ref[0]
    factor0 = 1.0 / math.sqrt(rank * LEAF)
    scaled0 = [
        (nt_dot(lv.leaf_values[q], basis0[:, q * LEAF : (q + 1) * LEAF]) * factor0).astype(jnp.bfloat16)
        for q in range(lv.count)
    ]
    for q in range(lv.count):
        far0 = nn_dot(scaled0[q ^ 1], basis0[:, q * LEAF : (q + 1) * LEAF])
        out_ref[:, q * LEAF : (q + 1) * LEAF] = (
            RIDGE * lv.directions[:, q * LEAF : (q + 1) * LEAF] + near[q] + far0
        )


def final_kernel(sub_size, sub_bits, leaf_bits, loc_bits, *refs):
    sub_masks = 2**sub_bits - 1
    leaf_masks = 2**leaf_bits - 1
    emb_ref, dirs_ref, local_ref, pair_ref, cross_ref, basis_ref, neighbours_ref, counts_ref = refs[:8]
    round_one = refs[8 : 8 + sub_masks - 1]
    round_two = refs[8 + sub_masks - 1 : 8 + sub_masks - 1 + leaf_masks]
    out_ref = refs[8 + sub_masks - 1 + leaf_masks]
    lv = Leaves(emb_ref, dirs_ref, neighbours_ref, counts_ref, sub_size)
    rank = basis_ref.shape[1]
    nrhs = dirs_ref.shape[0]
    local_points = lv.local_points
    levels = sub_bits + leaf_bits
    lower_width = rank * sub_bits

    pair, cross = pair_ref[...], cross_ref[...]
    step = nrhs * rank * levels // LEAF
    from_pair = unpack_parts(pair, lv.width_e + nrhs, step, rank * levels)
    column_level = lax.broadcasted_iota(jnp.int32, (1, rank * levels), 1) // rank
    lower_level = column_level[:, :lower_width]
    upper_level = column_level[:, : rank * leaf_bits]
    lower = jnp.where(lower_level == 0, from_pair[:, :lower_width], 0.0)
    for mask, got_ref in enumerate(round_one, start=2):
        lower = lower + jnp.where(lower_level == mask.bit_length() - 1, got_ref[:, :lower_width], 0.0)
    upper = None
    for mask, got_ref in enumerate(round_two, start=1):
        term = jnp.where(upper_level == mask.bit_length() - 1, got_ref[...], 0.0)
        upper = term if upper is None else upper + term
    sibling = jnp.concatenate([lower, upper], axis=1)
    factor = jnp.zeros((1, rank * levels), jnp.float32)
    for bit in range(levels):
        factor = jnp.where(column_level == bit, 1.0 / math.sqrt(rank * local_points * 2**bit), factor)
    scaled = (sibling * factor).astype(jnp.bfloat16)
    stacked = basis_ref[loc_bits : loc_bits + levels].reshape(levels * rank, local_points)
    far = nn_dot(scaled, stacked)

    even = lax.axis_index("sub") % 2 == 0
    halo_pair = pair[: lv.width_e + nrhs]
    left, right = jnp.where(even, cross, halo_pair), jnp.where(even, halo_pair, cross)
    halo = {}
    for j, received, offset in ((0, left, -1), (lv.count - 1, right, 1)):
        halo_points = received[: lv.width_e, :]
        halo_float = halo_points.astype(jnp.float32)
        halo_norms = -DISTANCE_SCALE * jnp.sum(halo_float * halo_float, axis=0, keepdims=True)
        weights = lv.block(j, halo_points, halo_norms)
        term = lv.weight(j, offset) * nt_dot(received[lv.width_e :, :], weights)
        halo[j] = term if j not in halo else halo[j] + term
    for j in range(lv.count):
        total = local_ref[:, j * LEAF : (j + 1) * LEAF] + far[:, j * LEAF : (j + 1) * LEAF]
        if j in halo:
            total = total + halo[j]
        out_ref[:, j * LEAF : (j + 1) * LEAF] = total


def on_device(embeddings, directions, level_basis, neighbours, counts):
    axes = ("leaf", "sub")
    width_e = embeddings.shape[0]
    local_points = embeddings.shape[1]
    rank = level_basis.shape[1]
    nrhs = directions.shape[0]
    sub_size = lax.axis_size("sub")
    leaf_size = lax.axis_size("leaf")
    sub_bits = sub_size.bit_length() - 1
    leaf_bits = leaf_size.bit_length() - 1
    dev_bits = sub_bits + leaf_bits
    loc_bits = level_basis.shape[0] - dev_bits

    step = nrhs * rank * dev_bits // LEAF
    pair_shape = jax.ShapeDtypeStruct((width_e + nrhs + 3 * step, LEAF), jnp.bfloat16)
    cross_shape = jax.ShapeDtypeStruct((width_e + nrhs, LEAF), jnp.bfloat16)
    parts_shape = jax.ShapeDtypeStruct((nrhs, rank * dev_bits), jnp.float32)
    pair, cross, parts = pl.pallas_call(
        functools.partial(send_kernel, loc_bits),
        out_shape=(pair_shape, cross_shape, parts_shape),
        in_specs=[VMEM, VMEM, VMEM],
        out_specs=(VMEM, VMEM, VMEM),
    )(embeddings, directions, level_basis)

    ndev = sub_size * leaf_size
    from_pair = lax.ppermute(pair, axes, [(i, i ^ 1) for i in range(ndev)])
    round_one = [from_mask(parts, "sub", mask) for mask in range(2, sub_size)]
    from_cross = lax.ppermute(cross, axes, [(i, i - 1 + 2 * (i % 2)) for i in range(1, ndev - 1)])
    upper = slice(rank * sub_bits, rank * dev_bits)
    line = parts[:, upper] + unpack_parts(from_pair, width_e + nrhs, step, rank * dev_bits)[:, upper]
    for got in round_one:
        line = line + got[:, upper]
    round_two = [from_mask(line, "leaf", mask) for mask in range(1, leaf_size)]

    out = jax.ShapeDtypeStruct((nrhs, local_points), jnp.float32)
    local = pl.pallas_call(
        functools.partial(local_kernel, sub_size),
        out_shape=out,
        in_specs=[VMEM, VMEM, VMEM, SMEM, SMEM],
        out_specs=VMEM,
    )(*in_vmem(embeddings, directions, level_basis), neighbours, counts)

    remote = round_one + round_two
    return pl.pallas_call(
        functools.partial(final_kernel, sub_size, sub_bits, leaf_bits, loc_bits),
        out_shape=out,
        in_specs=[VMEM] * 6 + [SMEM, SMEM] + [VMEM] * len(remote),
        out_specs=VMEM,
        input_output_aliases={2: 0},
    )(
        *in_vmem(embeddings, directions),
        local,
        *in_vmem(from_pair, from_cross, level_basis),
        neighbours,
        counts,
        *in_vmem(*remote),
    )


def solution(mesh):
    placed = (
        P(None, ("groups", "leaf", "sub")),
        P(None, ("groups", "leaf", "sub")),
        P(None, None, ("groups", "leaf", "sub")),
        P(("groups", "leaf", "sub"), None),
        P(("groups", "leaf", "sub")),
    )
    return jax.shard_map(
        on_device,
        mesh=mesh,
        in_specs=placed,
        out_specs=P(None, ("groups", "leaf", "sub")),
        check_vma=False,
    )
```

```python
import functools
import math

import jax
import jax.numpy as jnp
from jax import lax
from jax.experimental import pallas as pl
from jax.experimental.pallas import tpu as pltpu
from jax.sharding import PartitionSpec as P

LEAF = 512


AMPLITUDE = 0.5
DISTANCE_SCALE = 0.125
RIDGE = 0.5

VMEM = pl.BlockSpec(memory_space=pltpu.VMEM)
SMEM = pl.BlockSpec(memory_space=pltpu.SMEM)


def from_mask(x, axis, mask):
    pairs = [(i, i ^ mask) for i in range(lax.axis_size(axis))]
    return lax.ppermute(x, axis, pairs)


def in_vmem(*arrays):
    return [pltpu.with_memory_space_constraint(a, pltpu.VMEM) for a in arrays]


def nt_dot(a, b):
    return lax.dot_general(a, b, (((1,), (1,)), ((), ())), preferred_element_type=jnp.float32)


def nn_dot(a, b):
    return lax.dot_general(a, b, (((1,), (0,)), ((), ())), preferred_element_type=jnp.float32)


def split_rows(x, width):
    groups = width // x.shape[1]
    step = x.shape[0] // groups
    return jnp.concatenate([x[g * step : (g + 1) * step] for g in range(groups)], axis=1)


def join_rows(x, columns):
    groups = x.shape[1] // columns
    return jnp.concatenate([x[:, g * columns : (g + 1) * columns] for g in range(groups)], axis=0)


def send_kernel(loc_bits, emb_ref, dirs_ref, basis_ref, pair_ref, cross_ref, parts_ref):
    width_e = emb_ref.shape[0]
    local_points = emb_ref.shape[1]
    nrhs = dirs_ref.shape[0]
    values = dirs_ref[...].astype(jnp.bfloat16)
    even = lax.axis_index("sub") % 2 == 0
    head_points, tail_points = emb_ref[:, :LEAF], emb_ref[:, local_points - LEAF :]
    head_values, tail_values = values[:, :LEAF], values[:, local_points - LEAF :]
    pair_ref[:width_e, :] = jnp.where(even, tail_points, head_points)
    pair_ref[width_e : width_e + nrhs, :] = jnp.where(even, tail_values, head_values)
    cross_ref[:width_e, :] = jnp.where(even, head_points, tail_points)
    cross_ref[width_e:, :] = jnp.where(even, head_values, tail_values)
    levels, rank = parts_ref.shape[1] // basis_ref.shape[1], basis_ref.shape[1]
    stacked = basis_ref[loc_bits : loc_bits + levels].reshape(levels * rank, local_points)
    parts = nt_dot(values, stacked)
    parts_ref[...] = parts
    rows = split_rows(parts, LEAF)
    high = rows.astype(jnp.bfloat16)
    rest = rows - high.astype(jnp.float32)
    middle = rest.astype(jnp.bfloat16)
    low = (rest - middle.astype(jnp.float32)).astype(jnp.bfloat16)
    start = width_e + nrhs
    step = rows.shape[0]
    pair_ref[start : start + step, :] = high
    pair_ref[start + step : start + 2 * step, :] = middle
    pair_ref[start + 2 * step : start + 3 * step, :] = low


def unpack_parts(pair, start, step, columns):
    pieces = pair[start : start + 3 * step].astype(jnp.float32)
    rows = (pieces[:step] + pieces[step : 2 * step]) + pieces[2 * step :]
    return join_rows(rows, columns)


class Leaves:
    def __init__(self, emb_ref, dirs_ref, neighbours_ref, counts_ref, sub_size):
        self.width_e = emb_ref.shape[0]
        self.local_points = emb_ref.shape[1]
        self.count = self.local_points // LEAF
        self.directions = dirs_ref[...]
        self.values = self.directions.astype(jnp.bfloat16)
        emb_float = emb_ref[...].astype(jnp.float32)
        row_norms = jnp.sum(emb_float * emb_float, axis=0, keepdims=True)
        emb_t = emb_float.T
        self.col_terms = -DISTANCE_SCALE * jnp.sum(emb_t * emb_t, axis=1, keepdims=True)
        self.emb_t = (emb_t * (2.0 * DISTANCE_SCALE)).astype(jnp.bfloat16)
        self.points = [emb_ref[:, j * LEAF : (j + 1) * LEAF] for j in range(self.count)]
        self.norms = [-DISTANCE_SCALE * row_norms[:, j * LEAF : (j + 1) * LEAF] for j in range(self.count)]
        self.leaf_values = [self.values[:, j * LEAF : (j + 1) * LEAF] for j in range(self.count)]
        self.neighbours_ref = neighbours_ref
        self.counts_ref = counts_ref
        self.me = lax.axis_index("leaf") * sub_size + lax.axis_index("sub")

    def block(self, j, source_points, source_terms):
        inner = nn_dot(self.emb_t[j * LEAF : (j + 1) * LEAF], source_points)
        exponent = (self.col_terms[j * LEAF : (j + 1) * LEAF] + source_terms) + inner
        return (AMPLITUDE * jnp.exp(exponent)).astype(jnp.bfloat16)

    def weight(self, j, offset):
        leaf = self.me * self.count + j
        total = jnp.int32(0)
        for slot in range(self.neighbours_ref.shape[1]):
            hit = (slot < self.counts_ref[j]) & (self.neighbours_ref[j, slot] == leaf + offset)
            total = total + hit.astype(jnp.int32)
        return total.astype(jnp.float32)


def local_kernel(sub_size, emb_ref, dirs_ref, basis_ref, neighbours_ref, counts_ref, out_ref):
    lv = Leaves(emb_ref, dirs_ref, neighbours_ref, counts_ref, sub_size)
    rank = basis_ref.shape[1]
    near = [nt_dot(lv.leaf_values[j], lv.block(j, lv.points[j], lv.norms[j])) for j in range(lv.count)]
    for j in range(lv.count - 1):
        pair = lv.block(j, lv.points[j + 1], lv.norms[j + 1])
        near[j] = near[j] + lv.weight(j, 1) * nt_dot(lv.leaf_values[j + 1], pair)
        near[j + 1] = near[j + 1] + lv.weight(j + 1, -1) * nn_dot(lv.leaf_values[j], pair)
    basis0 = basis_ref[0]
    factor0 = 1.0 / math.sqrt(rank * LEAF)
    scaled0 = [
        (nt_dot(lv.leaf_values[q], basis0[:, q * LEAF : (q + 1) * LEAF]) * factor0).astype(jnp.bfloat16)
        for q in range(lv.count)
    ]
    for q in range(lv.count):
        far0 = nn_dot(scaled0[q ^ 1], basis0[:, q * LEAF : (q + 1) * LEAF])
        out_ref[:, q * LEAF : (q + 1) * LEAF] = (
            RIDGE * lv.directions[:, q * LEAF : (q + 1) * LEAF] + near[q] + far0
        )


def final_kernel(sub_size, sub_bits, leaf_bits, loc_bits, *refs):
    sub_masks = 2**sub_bits - 1
    leaf_masks = 2**leaf_bits - 1
    emb_ref, dirs_ref, local_ref, pair_ref, cross_ref, basis_ref, neighbours_ref, counts_ref = refs[:8]
    round_one = refs[8 : 8 + sub_masks - 1]
    round_two = refs[8 + sub_masks - 1 : 8 + sub_masks - 1 + leaf_masks]
    out_ref = refs[8 + sub_masks - 1 + leaf_masks]
    lv = Leaves(emb_ref, dirs_ref, neighbours_ref, counts_ref, sub_size)
    rank = basis_ref.shape[1]
    nrhs = dirs_ref.shape[0]
    local_points = lv.local_points
    levels = sub_bits + leaf_bits
    lower_width = rank * sub_bits

    pair, cross = pair_ref[...], cross_ref[...]
    step = nrhs * rank * levels // LEAF
    from_pair = unpack_parts(pair, lv.width_e + nrhs, step, rank * levels)
    column_level = lax.broadcasted_iota(jnp.int32, (1, rank * levels), 1) // rank
    lower_level = column_level[:, :lower_width]
    upper_level = column_level[:, : rank * leaf_bits]
    lower = jnp.where(lower_level == 0, from_pair[:, :lower_width], 0.0)
    for mask, got_ref in enumerate(round_one, start=2):
        lower = lower + jnp.where(lower_level == mask.bit_length() - 1, got_ref[:, :lower_width], 0.0)
    upper = None
    for mask, got_ref in enumerate(round_two, start=1):
        term = jnp.where(upper_level == mask.bit_length() - 1, got_ref[...], 0.0)
        upper = term if upper is None else upper + term
    sibling = jnp.concatenate([lower, upper], axis=1)
    factor = jnp.zeros((1, rank * levels), jnp.float32)
    for bit in range(levels):
        factor = jnp.where(column_level == bit, 1.0 / math.sqrt(rank * local_points * 2**bit), factor)
    scaled = (sibling * factor).astype(jnp.bfloat16)
    stacked = basis_ref[loc_bits : loc_bits + levels].reshape(levels * rank, local_points)
    far = nn_dot(scaled, stacked)

    even = lax.axis_index("sub") % 2 == 0
    halo_pair = pair[: lv.width_e + nrhs]
    left, right = jnp.where(even, cross, halo_pair), jnp.where(even, halo_pair, cross)
    halo = {}
    for j, received, offset in ((0, left, -1), (lv.count - 1, right, 1)):
        halo_points = received[: lv.width_e, :]
        halo_float = halo_points.astype(jnp.float32)
        halo_norms = -DISTANCE_SCALE * jnp.sum(halo_float * halo_float, axis=0, keepdims=True)
        weights = lv.block(j, halo_points, halo_norms)
        term = lv.weight(j, offset) * nt_dot(received[lv.width_e :, :], weights)
        halo[j] = term if j not in halo else halo[j] + term
    for j in range(lv.count):
        total = local_ref[:, j * LEAF : (j + 1) * LEAF] + far[:, j * LEAF : (j + 1) * LEAF]
        if j in halo:
            total = total + halo[j]
        out_ref[:, j * LEAF : (j + 1) * LEAF] = total


def on_device(embeddings, directions, level_basis, neighbours, counts):
    axes = ("leaf", "sub")
    width_e = embeddings.shape[0]
    local_points = embeddings.shape[1]
    rank = level_basis.shape[1]
    nrhs = directions.shape[0]
    sub_size = lax.axis_size("sub")
    leaf_size = lax.axis_size("leaf")
    sub_bits = sub_size.bit_length() - 1
    leaf_bits = leaf_size.bit_length() - 1
    dev_bits = sub_bits + leaf_bits
    loc_bits = level_basis.shape[0] - dev_bits

    step = nrhs * rank * dev_bits // LEAF
    pair_shape = jax.ShapeDtypeStruct((width_e + nrhs + 3 * step, LEAF), jnp.bfloat16)
    cross_shape = jax.ShapeDtypeStruct((width_e + nrhs, LEAF), jnp.bfloat16)
    parts_shape = jax.ShapeDtypeStruct((nrhs, rank * dev_bits), jnp.float32)
    pair, cross, parts = pl.pallas_call(
        functools.partial(send_kernel, loc_bits),
        out_shape=(pair_shape, cross_shape, parts_shape),
        in_specs=[VMEM, VMEM, VMEM],
        out_specs=(VMEM, VMEM, VMEM),
    )(embeddings, directions, level_basis)

    ndev = sub_size * leaf_size
    from_pair = lax.ppermute(pair, axes, [(i, i ^ 1) for i in range(ndev)])
    round_one = [from_mask(parts, "sub", mask) for mask in range(2, sub_size)]
    from_cross = lax.ppermute(cross, axes, [(i, i - 1 + 2 * (i % 2)) for i in range(1, ndev - 1)])
    upper = slice(rank * sub_bits, rank * dev_bits)
    line = parts[:, upper] + unpack_parts(from_pair, width_e + nrhs, step, rank * dev_bits)[:, upper]
    for got in round_one:
        line = line + got[:, upper]
    round_two = [from_mask(line, "leaf", mask) for mask in range(1, leaf_size)]

    out = jax.ShapeDtypeStruct((nrhs, local_points), jnp.float32)
    local = pl.pallas_call(
        functools.partial(local_kernel, sub_size),
        out_shape=out,
        in_specs=[VMEM, VMEM, VMEM, SMEM, SMEM],
        out_specs=VMEM,
    )(*in_vmem(embeddings, directions, level_basis), neighbours, counts)

    remote = round_one + round_two
    return pl.pallas_call(
        functools.partial(final_kernel, sub_size, sub_bits, leaf_bits, loc_bits),
        out_shape=out,
        in_specs=[VMEM] * 6 + [SMEM, SMEM] + [VMEM] * len(remote),
        out_specs=VMEM,
    )(
        *in_vmem(embeddings, directions, local, from_pair, from_cross, level_basis),
        neighbours,
        counts,
        *in_vmem(*remote),
    )


def solution(mesh):
    placed = (
        P(None, ("groups", "leaf", "sub")),
        P(None, ("groups", "leaf", "sub")),
        P(None, None, ("groups", "leaf", "sub")),
        P(("groups", "leaf", "sub"), None),
        P(("groups", "leaf", "sub")),
    )
    return jax.shard_map(
        on_device,
        mesh=mesh,
        in_specs=placed,
        out_specs=P(None, ("groups", "leaf", "sub")),
        check_vma=False,
    )
```

```python
import functools
import math

import jax
import jax.numpy as jnp
from jax import lax
from jax.experimental import pallas as pl
from jax.experimental.pallas import tpu as pltpu
from jax.sharding import PartitionSpec as P

LEAF = 512


AMPLITUDE = 0.5
DISTANCE_SCALE = 0.125
RIDGE = 0.5

VMEM = pl.BlockSpec(memory_space=pltpu.VMEM)
SMEM = pl.BlockSpec(memory_space=pltpu.SMEM)


def from_mask(x, axis, mask):
    pairs = [(i, i ^ mask) for i in range(lax.axis_size(axis))]
    return lax.ppermute(x, axis, pairs)


def in_vmem(*arrays):
    return [pltpu.with_memory_space_constraint(a, pltpu.VMEM) for a in arrays]


def nt_dot(a, b):
    return lax.dot_general(a, b, (((1,), (1,)), ((), ())), preferred_element_type=jnp.float32)


def nn_dot(a, b):
    return lax.dot_general(a, b, (((1,), (0,)), ((), ())), preferred_element_type=jnp.float32)


def split_rows(x, width):
    groups = width // x.shape[1]
    step = x.shape[0] // groups
    return jnp.concatenate([x[g * step : (g + 1) * step] for g in range(groups)], axis=1)


def join_rows(x, columns):
    groups = x.shape[1] // columns
    return jnp.concatenate([x[:, g * columns : (g + 1) * columns] for g in range(groups)], axis=0)


def send_kernel(loc_bits, emb_ref, dirs_ref, basis_ref, pair_ref, cross_ref, parts_ref):
    width_e = emb_ref.shape[0]
    local_points = emb_ref.shape[1]
    nrhs = dirs_ref.shape[0]
    values = dirs_ref[...].astype(jnp.bfloat16)
    even = lax.axis_index("sub") % 2 == 0
    head_points, tail_points = emb_ref[:, :LEAF], emb_ref[:, local_points - LEAF :]
    head_values, tail_values = values[:, :LEAF], values[:, local_points - LEAF :]
    pair_ref[:width_e, :] = jnp.where(even, tail_points, head_points)
    pair_ref[width_e : width_e + nrhs, :] = jnp.where(even, tail_values, head_values)
    cross_ref[:width_e, :] = jnp.where(even, head_points, tail_points)
    cross_ref[width_e:, :] = jnp.where(even, head_values, tail_values)
    levels, rank = parts_ref.shape[1] // basis_ref.shape[1], basis_ref.shape[1]
    stacked = basis_ref[loc_bits : loc_bits + levels].reshape(levels * rank, local_points)
    parts = nt_dot(values, stacked)
    parts_ref[...] = parts
    rows = split_rows(parts, LEAF)
    high = rows.astype(jnp.bfloat16)
    rest = rows - high.astype(jnp.float32)
    middle = rest.astype(jnp.bfloat16)
    low = (rest - middle.astype(jnp.float32)).astype(jnp.bfloat16)
    start = width_e + nrhs
    step = rows.shape[0]
    pair_ref[start : start + step, :] = high
    pair_ref[start + step : start + 2 * step, :] = middle
    pair_ref[start + 2 * step : start + 3 * step, :] = low


def unpack_parts(pair, start, step, columns):
    pieces = pair[start : start + 3 * step].astype(jnp.float32)
    rows = (pieces[:step] + pieces[step : 2 * step]) + pieces[2 * step :]
    return join_rows(rows, columns)


class Leaves:
    def __init__(self, emb_ref, dirs_ref, neighbours_ref, counts_ref, sub_size):
        self.width_e = emb_ref.shape[0]
        self.local_points = emb_ref.shape[1]
        self.count = self.local_points // LEAF
        self.directions = dirs_ref[...]
        self.values = self.directions.astype(jnp.bfloat16)
        emb_float = emb_ref[...].astype(jnp.float32)
        row_norms = jnp.sum(emb_float * emb_float, axis=0, keepdims=True)
        emb_t = emb_float.T
        self.col_terms = -DISTANCE_SCALE * jnp.sum(emb_t * emb_t, axis=1, keepdims=True)
        self.emb_t = (emb_t * (2.0 * DISTANCE_SCALE)).astype(jnp.bfloat16)
        self.points = [emb_ref[:, j * LEAF : (j + 1) * LEAF] for j in range(self.count)]
        self.norms = [-DISTANCE_SCALE * row_norms[:, j * LEAF : (j + 1) * LEAF] for j in range(self.count)]
        self.leaf_values = [self.values[:, j * LEAF : (j + 1) * LEAF] for j in range(self.count)]
        self.neighbours_ref = neighbours_ref
        self.counts_ref = counts_ref
        self.me = lax.axis_index("leaf") * sub_size + lax.axis_index("sub")

    def block(self, j, source_points, source_terms):
        inner = nn_dot(self.emb_t[j * LEAF : (j + 1) * LEAF], source_points)
        exponent = (self.col_terms[j * LEAF : (j + 1) * LEAF] + source_terms) + inner
        return (AMPLITUDE * jnp.exp(exponent)).astype(jnp.bfloat16)

    def weight(self, j, offset):
        leaf = self.me * self.count + j
        total = jnp.int32(0)
        for slot in range(self.neighbours_ref.shape[1]):
            hit = (slot < self.counts_ref[j]) & (self.neighbours_ref[j, slot] == leaf + offset)
            total = total + hit.astype(jnp.int32)
        return total.astype(jnp.float32)


def local_kernel(sub_size, emb_ref, dirs_ref, basis_ref, neighbours_ref, counts_ref, out_ref):
    lv = Leaves(emb_ref, dirs_ref, neighbours_ref, counts_ref, sub_size)
    rank = basis_ref.shape[1]
    near = [nt_dot(lv.leaf_values[j], lv.block(j, lv.points[j], lv.norms[j])) for j in range(lv.count)]
    for j in range(lv.count - 1):
        pair = lv.block(j, lv.points[j + 1], lv.norms[j + 1])
        near[j] = near[j] + lv.weight(j, 1) * nt_dot(lv.leaf_values[j + 1], pair)
        near[j + 1] = near[j + 1] + lv.weight(j + 1, -1) * nn_dot(lv.leaf_values[j], pair)
    basis0 = basis_ref[0]
    factor0 = 1.0 / math.sqrt(rank * LEAF)
    scaled0 = [
        (nt_dot(lv.leaf_values[q], basis0[:, q * LEAF : (q + 1) * LEAF]) * factor0).astype(jnp.bfloat16)
        for q in range(lv.count)
    ]
    for q in range(lv.count):
        far0 = nn_dot(scaled0[q ^ 1], basis0[:, q * LEAF : (q + 1) * LEAF])
        out_ref[:, q * LEAF : (q + 1) * LEAF] = (
            RIDGE * lv.directions[:, q * LEAF : (q + 1) * LEAF] + near[q] + far0
        )


def final_kernel(sub_size, sub_bits, leaf_bits, loc_bits, *refs):
    sub_masks = 2**sub_bits - 1
    leaf_masks = 2**leaf_bits - 1
    emb_ref, dirs_ref, local_ref, pair_ref, cross_ref, basis_ref, neighbours_ref, counts_ref = refs[:8]
    round_one = refs[8 : 8 + sub_masks - 1]
    round_two = refs[8 + sub_masks - 1 : 8 + sub_masks - 1 + leaf_masks]
    out_ref = refs[8 + sub_masks - 1 + leaf_masks]
    lv = Leaves(emb_ref, dirs_ref, neighbours_ref, counts_ref, sub_size)
    rank = basis_ref.shape[1]
    nrhs = dirs_ref.shape[0]
    local_points = lv.local_points
    levels = sub_bits + leaf_bits
    lower_width = rank * sub_bits

    pair, cross = pair_ref[...], cross_ref[...]
    step = nrhs * rank * levels // LEAF
    from_pair = unpack_parts(pair, lv.width_e + nrhs, step, rank * levels)
    column_level = lax.broadcasted_iota(jnp.int32, (1, rank * levels), 1) // rank
    lower_level = column_level[:, :lower_width]
    upper_level = column_level[:, : rank * leaf_bits]
    lower = jnp.where(lower_level == 0, from_pair[:, :lower_width], 0.0)
    for mask, got_ref in enumerate(round_one, start=2):
        lower = lower + jnp.where(lower_level == mask.bit_length() - 1, got_ref[:, :lower_width], 0.0)
    upper = None
    for mask, got_ref in enumerate(round_two, start=1):
        term = jnp.where(upper_level == mask.bit_length() - 1, got_ref[...], 0.0)
        upper = term if upper is None else upper + term
    sibling = jnp.concatenate([lower, upper], axis=1)
    factor = jnp.zeros((1, rank * levels), jnp.float32)
    for bit in range(levels):
        factor = jnp.where(column_level == bit, 1.0 / math.sqrt(rank * local_points * 2**bit), factor)
    scaled = (sibling * factor).astype(jnp.bfloat16)
    stacked = basis_ref[loc_bits : loc_bits + levels].reshape(levels * rank, local_points)
    far = nn_dot(scaled, stacked)

    even = lax.axis_index("sub") % 2 == 0
    halo_pair = pair[: lv.width_e + nrhs]
    left, right = jnp.where(even, cross, halo_pair), jnp.where(even, halo_pair, cross)
    halo = {}
    for j, received, offset in ((0, left, -1), (lv.count - 1, right, 1)):
        halo_points = received[: lv.width_e, :]
        halo_float = halo_points.astype(jnp.float32)
        halo_norms = -DISTANCE_SCALE * jnp.sum(halo_float * halo_float, axis=0, keepdims=True)
        weights = lv.block(j, halo_points, halo_norms)
        term = lv.weight(j, offset) * nt_dot(received[lv.width_e :, :], weights)
        halo[j] = term if j not in halo else halo[j] + term
    for j in range(lv.count):
        total = local_ref[:, j * LEAF : (j + 1) * LEAF] + far[:, j * LEAF : (j + 1) * LEAF]
        if j in halo:
            total = total + halo[j]
        out_ref[:, j * LEAF : (j + 1) * LEAF] = total


def on_device(embeddings, directions, level_basis, neighbours, counts):
    axes = ("leaf", "sub")
    width_e = embeddings.shape[0]
    local_points = embeddings.shape[1]
    rank = level_basis.shape[1]
    nrhs = directions.shape[0]
    sub_size = lax.axis_size("sub")
    leaf_size = lax.axis_size("leaf")
    sub_bits = sub_size.bit_length() - 1
    leaf_bits = leaf_size.bit_length() - 1
    dev_bits = sub_bits + leaf_bits
    loc_bits = level_basis.shape[0] - dev_bits

    step = nrhs * rank * dev_bits // LEAF
    pair_shape = jax.ShapeDtypeStruct((width_e + nrhs + 3 * step, LEAF), jnp.bfloat16)
    cross_shape = jax.ShapeDtypeStruct((width_e + nrhs, LEAF), jnp.bfloat16)
    parts_shape = jax.ShapeDtypeStruct((nrhs, rank * dev_bits), jnp.float32)
    pair, cross, parts = pl.pallas_call(
        functools.partial(send_kernel, loc_bits),
        out_shape=(pair_shape, cross_shape, parts_shape),
        in_specs=[VMEM, VMEM, VMEM],
        out_specs=(VMEM, VMEM, VMEM),
    )(*in_vmem(embeddings, directions, level_basis))

    ndev = sub_size * leaf_size
    from_pair = lax.ppermute(pair, axes, [(i, i ^ 1) for i in range(ndev)])
    round_one = [from_mask(parts, "sub", mask) for mask in range(2, sub_size)]
    from_cross = lax.ppermute(cross, axes, [(i, i - 1 + 2 * (i % 2)) for i in range(1, ndev - 1)])
    upper = slice(rank * sub_bits, rank * dev_bits)
    line = parts[:, upper] + unpack_parts(from_pair, width_e + nrhs, step, rank * dev_bits)[:, upper]
    for got in round_one:
        line = line + got[:, upper]
    round_two = [from_mask(line, "leaf", mask) for mask in range(1, leaf_size)]

    out = jax.ShapeDtypeStruct((nrhs, local_points), jnp.float32)
    local = pl.pallas_call(
        functools.partial(local_kernel, sub_size),
        out_shape=out,
        in_specs=[VMEM, VMEM, VMEM, SMEM, SMEM],
        out_specs=VMEM,
    )(*in_vmem(embeddings, directions, level_basis), neighbours, counts)

    remote = round_one + round_two
    return pl.pallas_call(
        functools.partial(final_kernel, sub_size, sub_bits, leaf_bits, loc_bits),
        out_shape=out,
        in_specs=[VMEM] * 6 + [SMEM, SMEM] + [VMEM] * len(remote),
        out_specs=VMEM,
        input_output_aliases={2: 0},
    )(
        *in_vmem(embeddings, directions, local, from_pair, from_cross, level_basis),
        neighbours,
        counts,
        *in_vmem(*remote),
    )


def solution(mesh):
    placed = (
        P(None, ("groups", "leaf", "sub")),
        P(None, ("groups", "leaf", "sub")),
        P(None, None, ("groups", "leaf", "sub")),
        P(("groups", "leaf", "sub"), None),
        P(("groups", "leaf", "sub")),
    )
    return jax.shard_map(
        on_device,
        mesh=mesh,
        in_specs=placed,
        out_specs=P(None, ("groups", "leaf", "sub")),
        check_vma=False,
    )
```

```python
import functools
import math

import jax
import jax.numpy as jnp
from jax import lax
from jax.experimental import pallas as pl
from jax.experimental.pallas import tpu as pltpu
from jax.sharding import PartitionSpec as P

LEAF = 512


AMPLITUDE = 0.5
DISTANCE_SCALE = 0.125
RIDGE = 0.5

VMEM = pl.BlockSpec(memory_space=pltpu.VMEM)
SMEM = pl.BlockSpec(memory_space=pltpu.SMEM)


def from_mask(x, axis, mask):
    pairs = [(i, i ^ mask) for i in range(lax.axis_size(axis))]
    return lax.ppermute(x, axis, pairs)


def in_vmem(*arrays):
    return [pltpu.with_memory_space_constraint(a, pltpu.VMEM) for a in arrays]


def nt_dot(a, b):
    return lax.dot_general(a, b, (((1,), (1,)), ((), ())), preferred_element_type=jnp.float32)


def nn_dot(a, b):
    return lax.dot_general(a, b, (((1,), (0,)), ((), ())), preferred_element_type=jnp.float32)


def split_rows(x, width):
    groups = width // x.shape[1]
    step = x.shape[0] // groups
    return jnp.concatenate([x[g * step : (g + 1) * step] for g in range(groups)], axis=1)


def join_rows(x, columns):
    groups = x.shape[1] // columns
    return jnp.concatenate([x[:, g * columns : (g + 1) * columns] for g in range(groups)], axis=0)


def send_kernel(loc_bits, emb_ref, dirs_ref, basis_ref, pair_ref, cross_ref, parts_ref, upper_ref, sem):
    levels = upper_ref.shape[0]
    fetch = pltpu.make_async_copy(basis_ref.at[pl.ds(loc_bits, levels)], upper_ref, sem)
    fetch.start()
    width_e = emb_ref.shape[0]
    local_points = emb_ref.shape[1]
    nrhs = dirs_ref.shape[0]
    values = dirs_ref[...].astype(jnp.bfloat16)
    even = lax.axis_index("sub") % 2 == 0
    head_points, tail_points = emb_ref[:, :LEAF], emb_ref[:, local_points - LEAF :]
    head_values, tail_values = values[:, :LEAF], values[:, local_points - LEAF :]
    pair_ref[:width_e, :] = jnp.where(even, tail_points, head_points)
    pair_ref[width_e : width_e + nrhs, :] = jnp.where(even, tail_values, head_values)
    cross_ref[:width_e, :] = jnp.where(even, head_points, tail_points)
    cross_ref[width_e:, :] = jnp.where(even, head_values, tail_values)
    rank = upper_ref.shape[1]
    fetch.wait()
    stacked = upper_ref[...].reshape(levels * rank, local_points)
    parts = nt_dot(values, stacked)
    parts_ref[...] = parts
    rows = split_rows(parts, LEAF)
    high = rows.astype(jnp.bfloat16)
    rest = rows - high.astype(jnp.float32)
    middle = rest.astype(jnp.bfloat16)
    low = (rest - middle.astype(jnp.float32)).astype(jnp.bfloat16)
    start = width_e + nrhs
    step = rows.shape[0]
    pair_ref[start : start + step, :] = high
    pair_ref[start + step : start + 2 * step, :] = middle
    pair_ref[start + 2 * step : start + 3 * step, :] = low


def unpack_parts(pair, start, step, columns):
    pieces = pair[start : start + 3 * step].astype(jnp.float32)
    rows = (pieces[:step] + pieces[step : 2 * step]) + pieces[2 * step :]
    return join_rows(rows, columns)


class Leaves:
    def __init__(self, emb_ref, dirs_ref, neighbours_ref, counts_ref, sub_size):
        self.width_e = emb_ref.shape[0]
        self.local_points = emb_ref.shape[1]
        self.count = self.local_points // LEAF
        self.directions = dirs_ref[...]
        self.values = self.directions.astype(jnp.bfloat16)
        emb_float = emb_ref[...].astype(jnp.float32)
        row_norms = jnp.sum(emb_float * emb_float, axis=0, keepdims=True)
        emb_t = emb_float.T
        self.col_terms = -DISTANCE_SCALE * jnp.sum(emb_t * emb_t, axis=1, keepdims=True)
        self.emb_t = (emb_t * (2.0 * DISTANCE_SCALE)).astype(jnp.bfloat16)
        self.points = [emb_ref[:, j * LEAF : (j + 1) * LEAF] for j in range(self.count)]
        self.norms = [-DISTANCE_SCALE * row_norms[:, j * LEAF : (j + 1) * LEAF] for j in range(self.count)]
        self.leaf_values = [self.values[:, j * LEAF : (j + 1) * LEAF] for j in range(self.count)]
        self.neighbours_ref = neighbours_ref
        self.counts_ref = counts_ref
        self.me = lax.axis_index("leaf") * sub_size + lax.axis_index("sub")

    def block(self, j, source_points, source_terms):
        inner = nn_dot(self.emb_t[j * LEAF : (j + 1) * LEAF], source_points)
        exponent = (self.col_terms[j * LEAF : (j + 1) * LEAF] + source_terms) + inner
        return (AMPLITUDE * jnp.exp(exponent)).astype(jnp.bfloat16)

    def weight(self, j, offset):
        leaf = self.me * self.count + j
        total = jnp.int32(0)
        for slot in range(self.neighbours_ref.shape[1]):
            hit = (slot < self.counts_ref[j]) & (self.neighbours_ref[j, slot] == leaf + offset)
            total = total + hit.astype(jnp.int32)
        return total.astype(jnp.float32)


def local_kernel(sub_size, emb_ref, dirs_ref, basis_ref, neighbours_ref, counts_ref, out_ref):
    lv = Leaves(emb_ref, dirs_ref, neighbours_ref, counts_ref, sub_size)
    rank = basis_ref.shape[1]
    near = [nt_dot(lv.leaf_values[j], lv.block(j, lv.points[j], lv.norms[j])) for j in range(lv.count)]
    for j in range(lv.count - 1):
        pair = lv.block(j, lv.points[j + 1], lv.norms[j + 1])
        near[j] = near[j] + lv.weight(j, 1) * nt_dot(lv.leaf_values[j + 1], pair)
        near[j + 1] = near[j + 1] + lv.weight(j + 1, -1) * nn_dot(lv.leaf_values[j], pair)
    basis0 = basis_ref[0]
    factor0 = 1.0 / math.sqrt(rank * LEAF)
    scaled0 = [
        (nt_dot(lv.leaf_values[q], basis0[:, q * LEAF : (q + 1) * LEAF]) * factor0).astype(jnp.bfloat16)
        for q in range(lv.count)
    ]
    for q in range(lv.count):
        far0 = nn_dot(scaled0[q ^ 1], basis0[:, q * LEAF : (q + 1) * LEAF])
        out_ref[:, q * LEAF : (q + 1) * LEAF] = (
            RIDGE * lv.directions[:, q * LEAF : (q + 1) * LEAF] + near[q] + far0
        )


def final_kernel(sub_size, sub_bits, leaf_bits, loc_bits, *refs):
    sub_masks = 2**sub_bits - 1
    leaf_masks = 2**leaf_bits - 1
    emb_ref, dirs_ref, local_ref, pair_ref, cross_ref, basis_ref, neighbours_ref, counts_ref = refs[:8]
    round_one = refs[8 : 8 + sub_masks - 1]
    round_two = refs[8 + sub_masks - 1 : 8 + sub_masks - 1 + leaf_masks]
    out_ref = refs[8 + sub_masks - 1 + leaf_masks]
    lv = Leaves(emb_ref, dirs_ref, neighbours_ref, counts_ref, sub_size)
    rank = basis_ref.shape[1]
    nrhs = dirs_ref.shape[0]
    local_points = lv.local_points
    levels = sub_bits + leaf_bits
    lower_width = rank * sub_bits

    pair, cross = pair_ref[...], cross_ref[...]
    step = nrhs * rank * levels // LEAF
    from_pair = unpack_parts(pair, lv.width_e + nrhs, step, rank * levels)
    column_level = lax.broadcasted_iota(jnp.int32, (1, rank * levels), 1) // rank
    lower_level = column_level[:, :lower_width]
    upper_level = column_level[:, : rank * leaf_bits]
    lower = jnp.where(lower_level == 0, from_pair[:, :lower_width], 0.0)
    for mask, got_ref in enumerate(round_one, start=2):
        lower = lower + jnp.where(lower_level == mask.bit_length() - 1, got_ref[:, :lower_width], 0.0)
    upper = None
    for mask, got_ref in enumerate(round_two, start=1):
        term = jnp.where(upper_level == mask.bit_length() - 1, got_ref[...], 0.0)
        upper = term if upper is None else upper + term
    sibling = jnp.concatenate([lower, upper], axis=1)
    factor = jnp.zeros((1, rank * levels), jnp.float32)
    for bit in range(levels):
        factor = jnp.where(column_level == bit, 1.0 / math.sqrt(rank * local_points * 2**bit), factor)
    scaled = (sibling * factor).astype(jnp.bfloat16)
    stacked = basis_ref[loc_bits : loc_bits + levels].reshape(levels * rank, local_points)
    far = nn_dot(scaled, stacked)

    even = lax.axis_index("sub") % 2 == 0
    halo_pair = pair[: lv.width_e + nrhs]
    left, right = jnp.where(even, cross, halo_pair), jnp.where(even, halo_pair, cross)
    halo = {}
    for j, received, offset in ((0, left, -1), (lv.count - 1, right, 1)):
        halo_points = received[: lv.width_e, :]
        halo_float = halo_points.astype(jnp.float32)
        halo_norms = -DISTANCE_SCALE * jnp.sum(halo_float * halo_float, axis=0, keepdims=True)
        weights = lv.block(j, halo_points, halo_norms)
        term = lv.weight(j, offset) * nt_dot(received[lv.width_e :, :], weights)
        halo[j] = term if j not in halo else halo[j] + term
    for j in range(lv.count):
        total = local_ref[:, j * LEAF : (j + 1) * LEAF] + far[:, j * LEAF : (j + 1) * LEAF]
        if j in halo:
            total = total + halo[j]
        out_ref[:, j * LEAF : (j + 1) * LEAF] = total


def on_device(embeddings, directions, level_basis, neighbours, counts):
    axes = ("leaf", "sub")
    width_e = embeddings.shape[0]
    local_points = embeddings.shape[1]
    rank = level_basis.shape[1]
    nrhs = directions.shape[0]
    sub_size = lax.axis_size("sub")
    leaf_size = lax.axis_size("leaf")
    sub_bits = sub_size.bit_length() - 1
    leaf_bits = leaf_size.bit_length() - 1
    dev_bits = sub_bits + leaf_bits
    loc_bits = level_basis.shape[0] - dev_bits

    step = nrhs * rank * dev_bits // LEAF
    pair_shape = jax.ShapeDtypeStruct((width_e + nrhs + 3 * step, LEAF), jnp.bfloat16)
    cross_shape = jax.ShapeDtypeStruct((width_e + nrhs, LEAF), jnp.bfloat16)
    parts_shape = jax.ShapeDtypeStruct((nrhs, rank * dev_bits), jnp.float32)
    pair, cross, parts = pl.pallas_call(
        functools.partial(send_kernel, loc_bits),
        out_shape=(pair_shape, cross_shape, parts_shape),
        in_specs=[VMEM, VMEM, pl.BlockSpec(memory_space=pl.ANY)],
        out_specs=(VMEM, VMEM, VMEM),
        scratch_shapes=[
            pltpu.VMEM((dev_bits, rank, local_points), level_basis.dtype),
            pltpu.SemaphoreType.DMA(()),
        ],
    )(embeddings, directions, level_basis)

    ndev = sub_size * leaf_size
    from_pair = lax.ppermute(pair, axes, [(i, i ^ 1) for i in range(ndev)])
    round_one = [from_mask(parts, "sub", mask) for mask in range(2, sub_size)]
    from_cross = lax.ppermute(cross, axes, [(i, i - 1 + 2 * (i % 2)) for i in range(1, ndev - 1)])
    upper = slice(rank * sub_bits, rank * dev_bits)
    line = parts[:, upper] + unpack_parts(from_pair, width_e + nrhs, step, rank * dev_bits)[:, upper]
    for got in round_one:
        line = line + got[:, upper]
    round_two = [from_mask(line, "leaf", mask) for mask in range(1, leaf_size)]

    out = jax.ShapeDtypeStruct((nrhs, local_points), jnp.float32)
    local = pl.pallas_call(
        functools.partial(local_kernel, sub_size),
        out_shape=out,
        in_specs=[VMEM, VMEM, VMEM, SMEM, SMEM],
        out_specs=VMEM,
    )(*in_vmem(embeddings, directions, level_basis), neighbours, counts)

    remote = round_one + round_two
    return pl.pallas_call(
        functools.partial(final_kernel, sub_size, sub_bits, leaf_bits, loc_bits),
        out_shape=out,
        in_specs=[VMEM] * 6 + [SMEM, SMEM] + [VMEM] * len(remote),
        out_specs=VMEM,
        input_output_aliases={2: 0},
    )(
        *in_vmem(embeddings, directions, local, from_pair, from_cross, level_basis),
        neighbours,
        counts,
        *in_vmem(*remote),
    )


def solution(mesh):
    placed = (
        P(None, ("groups", "leaf", "sub")),
        P(None, ("groups", "leaf", "sub")),
        P(None, None, ("groups", "leaf", "sub")),
        P(("groups", "leaf", "sub"), None),
        P(("groups", "leaf", "sub")),
    )
    return jax.shard_map(
        on_device,
        mesh=mesh,
        in_specs=placed,
        out_specs=P(None, ("groups", "leaf", "sub")),
        check_vma=False,
    )
```

```python
import functools
import math

import jax
import jax.numpy as jnp
from jax import lax
from jax.experimental import pallas as pl
from jax.experimental.pallas import tpu as pltpu
from jax.sharding import PartitionSpec as P

LEAF = 512


AMPLITUDE = 0.5
DISTANCE_SCALE = 0.125
RIDGE = 0.5

VMEM = pl.BlockSpec(memory_space=pltpu.VMEM)
SMEM = pl.BlockSpec(memory_space=pltpu.SMEM)


def from_mask(x, axis, mask):
    pairs = [(i, i ^ mask) for i in range(lax.axis_size(axis))]
    return lax.ppermute(x, axis, pairs)


def in_vmem(*arrays):
    return [pltpu.with_memory_space_constraint(a, pltpu.VMEM) for a in arrays]


def nt_dot(a, b):
    return lax.dot_general(a, b, (((1,), (1,)), ((), ())), preferred_element_type=jnp.float32)


def nn_dot(a, b):
    return lax.dot_general(a, b, (((1,), (0,)), ((), ())), preferred_element_type=jnp.float32)


def split_rows(x, width):
    groups = width // x.shape[1]
    step = x.shape[0] // groups
    return jnp.concatenate([x[g * step : (g + 1) * step] for g in range(groups)], axis=1)


def join_rows(x, columns):
    groups = x.shape[1] // columns
    return jnp.concatenate([x[:, g * columns : (g + 1) * columns] for g in range(groups)], axis=0)


def send_kernel(loc_bits, emb_ref, dirs_ref, basis_ref, pair_ref, cross_ref, parts_ref):
    width_e = emb_ref.shape[0]
    local_points = emb_ref.shape[1]
    nrhs = dirs_ref.shape[0]
    values = dirs_ref[...].astype(jnp.bfloat16)
    even = lax.axis_index("sub") % 2 == 0
    head_points, tail_points = emb_ref[:, :LEAF], emb_ref[:, local_points - LEAF :]
    head_values, tail_values = values[:, :LEAF], values[:, local_points - LEAF :]
    pair_ref[:width_e, :] = jnp.where(even, tail_points, head_points)
    pair_ref[width_e : width_e + nrhs, :] = jnp.where(even, tail_values, head_values)
    cross_ref[:width_e, :] = jnp.where(even, head_points, tail_points)
    cross_ref[width_e:, :] = jnp.where(even, head_values, tail_values)
    levels, rank = parts_ref.shape[1] // basis_ref.shape[1], basis_ref.shape[1]
    stacked = basis_ref[loc_bits : loc_bits + levels].reshape(levels * rank, local_points)
    parts = nt_dot(values, stacked)
    parts_ref[...] = parts
    rows = split_rows(parts, LEAF)
    high = rows.astype(jnp.bfloat16)
    rest = rows - high.astype(jnp.float32)
    middle = rest.astype(jnp.bfloat16)
    low = (rest - middle.astype(jnp.float32)).astype(jnp.bfloat16)
    start = width_e + nrhs
    step = rows.shape[0]
    pair_ref[start : start + step, :] = high
    pair_ref[start + step : start + 2 * step, :] = middle
    pair_ref[start + 2 * step : start + 3 * step, :] = low


def unpack_parts(pair, start, step, columns):
    pieces = pair[start : start + 3 * step].astype(jnp.float32)
    rows = (pieces[:step] + pieces[step : 2 * step]) + pieces[2 * step :]
    return join_rows(rows, columns)


class Leaves:
    def __init__(self, emb_ref, dirs_ref, neighbours_ref, counts_ref, sub_size):
        self.width_e = emb_ref.shape[0]
        self.local_points = emb_ref.shape[1]
        self.count = self.local_points // LEAF
        self.directions = dirs_ref[...]
        self.values = self.directions.astype(jnp.bfloat16)
        emb_float = emb_ref[...].astype(jnp.float32)
        row_norms = jnp.sum(emb_float * emb_float, axis=0, keepdims=True)
        emb_t = emb_float.T
        self.col_terms = -DISTANCE_SCALE * jnp.sum(emb_t * emb_t, axis=1, keepdims=True)
        self.emb_t = (emb_t * (2.0 * DISTANCE_SCALE)).astype(jnp.bfloat16)
        self.points = [emb_ref[:, j * LEAF : (j + 1) * LEAF] for j in range(self.count)]
        self.norms = [-DISTANCE_SCALE * row_norms[:, j * LEAF : (j + 1) * LEAF] for j in range(self.count)]
        self.leaf_values = [self.values[:, j * LEAF : (j + 1) * LEAF] for j in range(self.count)]
        self.neighbours_ref = neighbours_ref
        self.counts_ref = counts_ref
        self.me = lax.axis_index("leaf") * sub_size + lax.axis_index("sub")

    def block(self, j, source_points, source_terms):
        inner = nn_dot(self.emb_t[j * LEAF : (j + 1) * LEAF], source_points)
        exponent = (self.col_terms[j * LEAF : (j + 1) * LEAF] + source_terms) + inner
        return (AMPLITUDE * jnp.exp(exponent)).astype(jnp.bfloat16)

    def weight(self, j, offset):
        leaf = self.me * self.count + j
        total = jnp.int32(0)
        for slot in range(self.neighbours_ref.shape[1]):
            hit = (slot < self.counts_ref[j]) & (self.neighbours_ref[j, slot] == leaf + offset)
            total = total + hit.astype(jnp.int32)
        return total.astype(jnp.float32)


def local_kernel(sub_size, emb_ref, dirs_ref, basis_ref, pair_ref, cross_ref, neighbours_ref, counts_ref, out_ref):
    lv = Leaves(emb_ref, dirs_ref, neighbours_ref, counts_ref, sub_size)
    rank = basis_ref.shape[1]
    nrhs = dirs_ref.shape[0]
    near = [nt_dot(lv.leaf_values[j], lv.block(j, lv.points[j], lv.norms[j])) for j in range(lv.count)]
    for j in range(lv.count - 1):
        pair = lv.block(j, lv.points[j + 1], lv.norms[j + 1])
        near[j] = near[j] + lv.weight(j, 1) * nt_dot(lv.leaf_values[j + 1], pair)
        near[j + 1] = near[j + 1] + lv.weight(j + 1, -1) * nn_dot(lv.leaf_values[j], pair)
    basis0 = basis_ref[0]
    factor0 = 1.0 / math.sqrt(rank * LEAF)
    scaled0 = [
        (nt_dot(lv.leaf_values[q], basis0[:, q * LEAF : (q + 1) * LEAF]) * factor0).astype(jnp.bfloat16)
        for q in range(lv.count)
    ]
    even = lax.axis_index("sub") % 2 == 0
    halo_pair = pair_ref[: lv.width_e + nrhs, :]
    cross = cross_ref[...]
    left, right = jnp.where(even, cross, halo_pair), jnp.where(even, halo_pair, cross)
    for j, received, offset in ((0, left, -1), (lv.count - 1, right, 1)):
        halo_points = received[: lv.width_e, :]
        halo_float = halo_points.astype(jnp.float32)
        halo_norms = -DISTANCE_SCALE * jnp.sum(halo_float * halo_float, axis=0, keepdims=True)
        weights = lv.block(j, halo_points, halo_norms)
        near[j] = near[j] + lv.weight(j, offset) * nt_dot(received[lv.width_e :, :], weights)
    for q in range(lv.count):
        far0 = nn_dot(scaled0[q ^ 1], basis0[:, q * LEAF : (q + 1) * LEAF])
        out_ref[:, q * LEAF : (q + 1) * LEAF] = (
            RIDGE * lv.directions[:, q * LEAF : (q + 1) * LEAF] + near[q] + far0
        )


def final_kernel(sub_size, sub_bits, leaf_bits, loc_bits, *refs):
    sub_masks = 2**sub_bits - 1
    leaf_masks = 2**leaf_bits - 1
    emb_ref, dirs_ref, local_ref, pair_ref, cross_ref, basis_ref, neighbours_ref, counts_ref = refs[:8]
    round_one = refs[8 : 8 + sub_masks - 1]
    round_two = refs[8 + sub_masks - 1 : 8 + sub_masks - 1 + leaf_masks]
    out_ref = refs[8 + sub_masks - 1 + leaf_masks]
    rank = basis_ref.shape[1]
    nrhs, local_points = local_ref.shape
    width_e = emb_ref.shape[0]
    levels = sub_bits + leaf_bits
    lower_width = rank * sub_bits

    step = nrhs * rank * levels // LEAF
    from_pair = unpack_parts(pair_ref[...], width_e + nrhs, step, rank * levels)
    column_level = lax.broadcasted_iota(jnp.int32, (1, rank * levels), 1) // rank
    lower_level = column_level[:, :lower_width]
    upper_level = column_level[:, : rank * leaf_bits]
    lower = jnp.where(lower_level == 0, from_pair[:, :lower_width], 0.0)
    for mask, got_ref in enumerate(round_one, start=2):
        lower = lower + jnp.where(lower_level == mask.bit_length() - 1, got_ref[:, :lower_width], 0.0)
    upper = None
    for mask, got_ref in enumerate(round_two, start=1):
        term = jnp.where(upper_level == mask.bit_length() - 1, got_ref[...], 0.0)
        upper = term if upper is None else upper + term
    sibling = jnp.concatenate([lower, upper], axis=1)
    factor = jnp.zeros((1, rank * levels), jnp.float32)
    for bit in range(levels):
        factor = jnp.where(column_level == bit, 1.0 / math.sqrt(rank * local_points * 2**bit), factor)
    scaled = (sibling * factor).astype(jnp.bfloat16)
    stacked = basis_ref[loc_bits : loc_bits + levels].reshape(levels * rank, local_points)
    far = nn_dot(scaled, stacked)

    out_ref[...] = local_ref[...] + far


def on_device(embeddings, directions, level_basis, neighbours, counts):
    axes = ("leaf", "sub")
    width_e = embeddings.shape[0]
    local_points = embeddings.shape[1]
    rank = level_basis.shape[1]
    nrhs = directions.shape[0]
    sub_size = lax.axis_size("sub")
    leaf_size = lax.axis_size("leaf")
    sub_bits = sub_size.bit_length() - 1
    leaf_bits = leaf_size.bit_length() - 1
    dev_bits = sub_bits + leaf_bits
    loc_bits = level_basis.shape[0] - dev_bits

    step = nrhs * rank * dev_bits // LEAF
    pair_shape = jax.ShapeDtypeStruct((width_e + nrhs + 3 * step, LEAF), jnp.bfloat16)
    cross_shape = jax.ShapeDtypeStruct((width_e + nrhs, LEAF), jnp.bfloat16)
    parts_shape = jax.ShapeDtypeStruct((nrhs, rank * dev_bits), jnp.float32)
    pair, cross, parts = pl.pallas_call(
        functools.partial(send_kernel, loc_bits),
        out_shape=(pair_shape, cross_shape, parts_shape),
        in_specs=[VMEM, VMEM, VMEM],
        out_specs=(VMEM, VMEM, VMEM),
    )(embeddings, directions, level_basis)

    ndev = sub_size * leaf_size
    from_pair = lax.ppermute(pair, axes, [(i, i ^ 1) for i in range(ndev)])
    round_one = [from_mask(parts, "sub", mask) for mask in range(2, sub_size)]
    from_cross = lax.ppermute(cross, axes, [(i, i - 1 + 2 * (i % 2)) for i in range(1, ndev - 1)])
    upper = slice(rank * sub_bits, rank * dev_bits)
    line = parts[:, upper] + unpack_parts(from_pair, width_e + nrhs, step, rank * dev_bits)[:, upper]
    for got in round_one:
        line = line + got[:, upper]
    round_two = [from_mask(line, "leaf", mask) for mask in range(1, leaf_size)]

    out = jax.ShapeDtypeStruct((nrhs, local_points), jnp.float32)
    local = pl.pallas_call(
        functools.partial(local_kernel, sub_size),
        out_shape=out,
        in_specs=[VMEM] * 5 + [SMEM, SMEM],
        out_specs=VMEM,
    )(*in_vmem(embeddings, directions, level_basis, from_pair, from_cross), neighbours, counts)

    remote = round_one + round_two
    return pl.pallas_call(
        functools.partial(final_kernel, sub_size, sub_bits, leaf_bits, loc_bits),
        out_shape=out,
        in_specs=[VMEM] * 6 + [SMEM, SMEM] + [VMEM] * len(remote),
        out_specs=VMEM,
        input_output_aliases={2: 0},
    )(
        *in_vmem(embeddings, directions, local, from_pair, from_cross, level_basis),
        neighbours,
        counts,
        *in_vmem(*remote),
    )


def solution(mesh):
    placed = (
        P(None, ("groups", "leaf", "sub")),
        P(None, ("groups", "leaf", "sub")),
        P(None, None, ("groups", "leaf", "sub")),
        P(("groups", "leaf", "sub"), None),
        P(("groups", "leaf", "sub")),
    )
    return jax.shard_map(
        on_device,
        mesh=mesh,
        in_specs=placed,
        out_specs=P(None, ("groups", "leaf", "sub")),
        check_vma=False,
    )
```

```python
import functools
import math

import jax
import jax.numpy as jnp
from jax import lax
from jax.experimental import pallas as pl
from jax.experimental.pallas import tpu as pltpu
from jax.sharding import PartitionSpec as P

LEAF = 512


AMPLITUDE = 0.5
DISTANCE_SCALE = 0.125
RIDGE = 0.5

VMEM = pl.BlockSpec(memory_space=pltpu.VMEM)
SMEM = pl.BlockSpec(memory_space=pltpu.SMEM)


def from_mask(x, axis, mask):
    pairs = [(i, i ^ mask) for i in range(lax.axis_size(axis))]
    return lax.ppermute(x, axis, pairs)


def in_vmem(*arrays):
    return [pltpu.with_memory_space_constraint(a, pltpu.VMEM) for a in arrays]


def nt_dot(a, b):
    return lax.dot_general(a, b, (((1,), (1,)), ((), ())), preferred_element_type=jnp.float32)


def nn_dot(a, b):
    return lax.dot_general(a, b, (((1,), (0,)), ((), ())), preferred_element_type=jnp.float32)


def split_rows(x, width):
    groups = width // x.shape[1]
    step = x.shape[0] // groups
    return jnp.concatenate([x[g * step : (g + 1) * step] for g in range(groups)], axis=1)


def join_rows(x, columns):
    groups = x.shape[1] // columns
    return jnp.concatenate([x[:, g * columns : (g + 1) * columns] for g in range(groups)], axis=0)


def send_kernel(loc_bits, emb_ref, dirs_ref, basis_ref, pair_ref, cross_ref, parts_ref):
    width_e = emb_ref.shape[0]
    local_points = emb_ref.shape[1]
    nrhs = dirs_ref.shape[0]
    values = dirs_ref[...].astype(jnp.bfloat16)
    even = lax.axis_index("sub") % 2 == 0
    head_points, tail_points = emb_ref[:, :LEAF], emb_ref[:, local_points - LEAF :]
    head_values, tail_values = values[:, :LEAF], values[:, local_points - LEAF :]
    pair_ref[:width_e, :] = jnp.where(even, tail_points, head_points)
    pair_ref[width_e : width_e + nrhs, :] = jnp.where(even, tail_values, head_values)
    cross_ref[:width_e, :] = jnp.where(even, head_points, tail_points)
    cross_ref[width_e:, :] = jnp.where(even, head_values, tail_values)
    levels, rank = parts_ref.shape[1] // basis_ref.shape[1], basis_ref.shape[1]
    stacked = basis_ref[loc_bits : loc_bits + levels].reshape(levels * rank, local_points)
    parts = nt_dot(values, stacked)
    parts_ref[...] = parts
    rows = split_rows(parts, LEAF)
    high = rows.astype(jnp.bfloat16)
    rest = rows - high.astype(jnp.float32)
    middle = rest.astype(jnp.bfloat16)
    low = (rest - middle.astype(jnp.float32)).astype(jnp.bfloat16)
    start = width_e + nrhs
    step = rows.shape[0]
    pair_ref[start : start + step, :] = high
    pair_ref[start + step : start + 2 * step, :] = middle
    pair_ref[start + 2 * step : start + 3 * step, :] = low


def unpack_parts(pair, start, step, columns):
    pieces = pair[start : start + 3 * step].astype(jnp.float32)
    rows = (pieces[:step] + pieces[step : 2 * step]) + pieces[2 * step :]
    return join_rows(rows, columns)


class Leaves:
    def __init__(self, emb_ref, dirs_ref, neighbours_ref, counts_ref, sub_size):
        self.width_e = emb_ref.shape[0]
        self.local_points = emb_ref.shape[1]
        self.count = self.local_points // LEAF
        self.directions = dirs_ref[...]
        self.values = self.directions.astype(jnp.bfloat16)
        emb_float = emb_ref[...].astype(jnp.float32)
        row_norms = jnp.sum(emb_float * emb_float, axis=0, keepdims=True)
        emb_t = emb_float.T
        self.col_terms = -DISTANCE_SCALE * jnp.sum(emb_t * emb_t, axis=1, keepdims=True)
        self.emb_t = (emb_t * (2.0 * DISTANCE_SCALE)).astype(jnp.bfloat16)
        self.points = [emb_ref[:, j * LEAF : (j + 1) * LEAF] for j in range(self.count)]
        self.norms = [-DISTANCE_SCALE * row_norms[:, j * LEAF : (j + 1) * LEAF] for j in range(self.count)]
        self.leaf_values = [self.values[:, j * LEAF : (j + 1) * LEAF] for j in range(self.count)]
        self.neighbours_ref = neighbours_ref
        self.counts_ref = counts_ref
        self.me = lax.axis_index("leaf") * sub_size + lax.axis_index("sub")

    def block(self, j, source_points, source_terms):
        inner = nn_dot(self.emb_t[j * LEAF : (j + 1) * LEAF], source_points)
        exponent = (self.col_terms[j * LEAF : (j + 1) * LEAF] + source_terms) + inner
        return (AMPLITUDE * jnp.exp(exponent)).astype(jnp.bfloat16)

    def weight(self, j, offset):
        leaf = self.me * self.count + j
        total = jnp.int32(0)
        for slot in range(self.neighbours_ref.shape[1]):
            hit = (slot < self.counts_ref[j]) & (self.neighbours_ref[j, slot] == leaf + offset)
            total = total + hit.astype(jnp.int32)
        return total.astype(jnp.float32)


def local_kernel(sub_size, emb_ref, dirs_ref, basis_ref, neighbours_ref, counts_ref, out_ref):
    lv = Leaves(emb_ref, dirs_ref, neighbours_ref, counts_ref, sub_size)
    rank = basis_ref.shape[1]
    near = [nt_dot(lv.leaf_values[j], lv.block(j, lv.points[j], lv.norms[j])) for j in range(lv.count)]
    for j in range(lv.count - 1):
        pair = lv.block(j, lv.points[j + 1], lv.norms[j + 1])
        near[j] = near[j] + lv.weight(j, 1) * nt_dot(lv.leaf_values[j + 1], pair)
        near[j + 1] = near[j + 1] + lv.weight(j + 1, -1) * nn_dot(lv.leaf_values[j], pair)
    basis0 = basis_ref[0]
    factor0 = 1.0 / math.sqrt(rank * LEAF)
    scaled0 = [
        (nt_dot(lv.leaf_values[q], basis0[:, q * LEAF : (q + 1) * LEAF]) * factor0).astype(jnp.bfloat16)
        for q in range(lv.count)
    ]
    for q in range(lv.count):
        far0 = nn_dot(scaled0[q ^ 1], basis0[:, q * LEAF : (q + 1) * LEAF])
        out_ref[:, q * LEAF : (q + 1) * LEAF] = (
            RIDGE * lv.directions[:, q * LEAF : (q + 1) * LEAF] + near[q] + far0
        )


def final_kernel(sub_size, sub_bits, leaf_bits, loc_bits, *refs):
    sub_masks = 2**sub_bits - 1
    leaf_masks = 2**leaf_bits - 1
    emb_ref, dirs_ref, local_ref, pair_ref, cross_ref, basis_ref, neighbours_ref, counts_ref = refs[:8]
    round_one = refs[8 : 8 + sub_masks - 1]
    round_two = refs[8 + sub_masks - 1 : 8 + sub_masks - 1 + leaf_masks]
    out_ref = refs[8 + sub_masks - 1 + leaf_masks]
    lv = Leaves(emb_ref, dirs_ref, neighbours_ref, counts_ref, sub_size)
    rank = basis_ref.shape[1]
    nrhs = dirs_ref.shape[0]
    local_points = lv.local_points
    levels = sub_bits + leaf_bits
    lower_width = rank * sub_bits

    pair, cross = pair_ref[...], cross_ref[...]
    step = nrhs * rank * levels // LEAF
    from_pair = unpack_parts(pair, lv.width_e + nrhs, step, rank * levels)
    column_level = lax.broadcasted_iota(jnp.int32, (1, rank * levels), 1) // rank
    lower_level = column_level[:, :lower_width]
    upper_level = column_level[:, : rank * leaf_bits]
    lower = jnp.where(lower_level == 0, from_pair[:, :lower_width], 0.0)
    for mask, got_ref in enumerate(round_one, start=2):
        lower = lower + jnp.where(lower_level == mask.bit_length() - 1, got_ref[:, :lower_width], 0.0)
    upper = None
    for mask, got_ref in enumerate(round_two, start=1):
        term = jnp.where(upper_level == mask.bit_length() - 1, got_ref[...], 0.0)
        upper = term if upper is None else upper + term
    sibling = jnp.concatenate([lower, upper], axis=1)
    factor = jnp.zeros((1, rank * levels), jnp.float32)
    for bit in range(levels):
        factor = jnp.where(column_level == bit, 1.0 / math.sqrt(rank * local_points * 2**bit), factor)
    scaled = (sibling * factor).astype(jnp.bfloat16)
    stacked = basis_ref[loc_bits : loc_bits + levels].reshape(levels * rank, local_points)
    far = nn_dot(scaled, stacked)

    even = lax.axis_index("sub") % 2 == 0
    halo_pair = pair[: lv.width_e + nrhs]
    left, right = jnp.where(even, cross, halo_pair), jnp.where(even, halo_pair, cross)
    halo = {}
    for j, received, offset in ((0, left, -1), (lv.count - 1, right, 1)):
        halo_points = received[: lv.width_e, :]
        halo_float = halo_points.astype(jnp.float32)
        halo_norms = -DISTANCE_SCALE * jnp.sum(halo_float * halo_float, axis=0, keepdims=True)
        weights = lv.block(j, halo_points, halo_norms)
        term = lv.weight(j, offset) * nt_dot(received[lv.width_e :, :], weights)
        halo[j] = term if j not in halo else halo[j] + term
    for j in range(lv.count):
        total = local_ref[:, j * LEAF : (j + 1) * LEAF] + far[:, j * LEAF : (j + 1) * LEAF]
        if j in halo:
            total = total + halo[j]
        out_ref[:, j * LEAF : (j + 1) * LEAF] = total


def on_device(embeddings, directions, level_basis, neighbours, counts):
    axes = ("leaf", "sub")
    width_e = embeddings.shape[0]
    local_points = embeddings.shape[1]
    rank = level_basis.shape[1]
    nrhs = directions.shape[0]
    sub_size = lax.axis_size("sub")
    leaf_size = lax.axis_size("leaf")
    sub_bits = sub_size.bit_length() - 1
    leaf_bits = leaf_size.bit_length() - 1
    dev_bits = sub_bits + leaf_bits
    loc_bits = level_basis.shape[0] - dev_bits

    step = nrhs * rank * dev_bits // LEAF
    pair_shape = jax.ShapeDtypeStruct((width_e + nrhs + 3 * step, LEAF), jnp.bfloat16)
    cross_shape = jax.ShapeDtypeStruct((width_e + nrhs, LEAF), jnp.bfloat16)
    parts_shape = jax.ShapeDtypeStruct((nrhs, rank * dev_bits), jnp.float32)
    pair, cross, parts = pl.pallas_call(
        functools.partial(send_kernel, loc_bits),
        out_shape=(pair_shape, cross_shape, parts_shape),
        in_specs=[VMEM, VMEM, VMEM],
        out_specs=(VMEM, VMEM, VMEM),
    )(embeddings, directions, level_basis)

    ndev = sub_size * leaf_size
    from_pair = lax.ppermute(pair, axes, [(i, i ^ 1) for i in range(ndev)])
    round_one = [from_mask(parts, "sub", mask) for mask in range(2, sub_size)]
    from_cross = lax.ppermute(cross, axes, [(i, i - 1 + 2 * (i % 2)) for i in range(1, ndev - 1)])
    upper = slice(rank * sub_bits, rank * dev_bits)
    line = parts[:, upper] + unpack_parts(from_pair, width_e + nrhs, step, rank * dev_bits)[:, upper]
    for got in round_one:
        line = line + got[:, upper]
    round_two = [from_mask(line, "leaf", mask) for mask in range(1, leaf_size)]

    out = jax.ShapeDtypeStruct((nrhs, local_points), jnp.float32)
    local = pl.pallas_call(
        functools.partial(local_kernel, sub_size),
        out_shape=out,
        in_specs=[VMEM, VMEM, VMEM, SMEM, SMEM],
        out_specs=VMEM,
        input_output_aliases={1: 0},
    )(*in_vmem(embeddings, directions, level_basis), neighbours, counts)

    remote = round_one + round_two
    return pl.pallas_call(
        functools.partial(final_kernel, sub_size, sub_bits, leaf_bits, loc_bits),
        out_shape=out,
        in_specs=[VMEM] * 6 + [SMEM, SMEM] + [VMEM] * len(remote),
        out_specs=VMEM,
    )(
        *in_vmem(embeddings, local, local, from_pair, from_cross, level_basis),
        neighbours,
        counts,
        *in_vmem(*remote),
    )


def solution(mesh):
    placed = (
        P(None, ("groups", "leaf", "sub")),
        P(None, ("groups", "leaf", "sub")),
        P(None, None, ("groups", "leaf", "sub")),
        P(("groups", "leaf", "sub"), None),
        P(("groups", "leaf", "sub")),
    )
    return jax.shard_map(
        on_device,
        mesh=mesh,
        in_specs=placed,
        out_specs=P(None, ("groups", "leaf", "sub")),
        check_vma=False,
    )
```

```python
import functools
import math

import jax
import jax.numpy as jnp
from jax import lax
from jax.experimental import pallas as pl
from jax.experimental.pallas import tpu as pltpu
from jax.sharding import PartitionSpec as P

LEAF = 512


AMPLITUDE = 0.5
DISTANCE_SCALE = 0.125
RIDGE = 0.5

VMEM = pl.BlockSpec(memory_space=pltpu.VMEM)
SMEM = pl.BlockSpec(memory_space=pltpu.SMEM)


def from_mask(x, axis, mask):
    pairs = [(i, i ^ mask) for i in range(lax.axis_size(axis))]
    return lax.ppermute(x, axis, pairs)


def in_vmem(*arrays):
    return [pltpu.with_memory_space_constraint(a, pltpu.VMEM) for a in arrays]


def nt_dot(a, b):
    return lax.dot_general(a, b, (((1,), (1,)), ((), ())), preferred_element_type=jnp.float32)


def nn_dot(a, b):
    return lax.dot_general(a, b, (((1,), (0,)), ((), ())), preferred_element_type=jnp.float32)


def split_rows(x, width):
    groups = width // x.shape[1]
    step = x.shape[0] // groups
    return jnp.concatenate([x[g * step : (g + 1) * step] for g in range(groups)], axis=1)


def join_rows(x, columns):
    groups = x.shape[1] // columns
    return jnp.concatenate([x[:, g * columns : (g + 1) * columns] for g in range(groups)], axis=0)


def send_kernel(loc_bits, emb_ref, dirs_ref, basis_ref, pair_ref, cross_ref, parts_ref):
    width_e = emb_ref.shape[0]
    local_points = emb_ref.shape[1]
    nrhs = dirs_ref.shape[0]
    values = dirs_ref[...].astype(jnp.bfloat16)
    even = lax.axis_index("sub") % 2 == 0
    head_points, tail_points = emb_ref[:, :LEAF], emb_ref[:, local_points - LEAF :]
    head_values, tail_values = values[:, :LEAF], values[:, local_points - LEAF :]
    pair_ref[:width_e, :] = jnp.where(even, tail_points, head_points)
    pair_ref[width_e : width_e + nrhs, :] = jnp.where(even, tail_values, head_values)
    cross_ref[:width_e, :] = jnp.where(even, head_points, tail_points)
    cross_ref[width_e:, :] = jnp.where(even, head_values, tail_values)
    levels, rank = parts_ref.shape[1] // basis_ref.shape[1], basis_ref.shape[1]
    stacked = basis_ref[loc_bits : loc_bits + levels].reshape(levels * rank, local_points)
    parts = nt_dot(values, stacked)
    parts_ref[...] = parts
    rows = split_rows(parts, LEAF)
    high = rows.astype(jnp.bfloat16)
    rest = rows - high.astype(jnp.float32)
    middle = rest.astype(jnp.bfloat16)
    low = (rest - middle.astype(jnp.float32)).astype(jnp.bfloat16)
    start = width_e + nrhs
    step = rows.shape[0]
    pair_ref[start : start + step, :] = high
    pair_ref[start + step : start + 2 * step, :] = middle
    pair_ref[start + 2 * step : start + 3 * step, :] = low


def unpack_parts(pair, start, step, columns):
    pieces = pair[start : start + 3 * step].astype(jnp.float32)
    rows = (pieces[:step] + pieces[step : 2 * step]) + pieces[2 * step :]
    return join_rows(rows, columns)


class Leaves:
    def __init__(self, emb_ref, dirs_ref, neighbours_ref, counts_ref, sub_size):
        self.width_e = emb_ref.shape[0]
        self.local_points = emb_ref.shape[1]
        self.count = self.local_points // LEAF
        self.directions = dirs_ref[...]
        self.values = self.directions.astype(jnp.bfloat16)
        emb_float = emb_ref[...].astype(jnp.float32)
        row_norms = jnp.sum(emb_float * emb_float, axis=0, keepdims=True)
        emb_t = emb_float.T
        self.col_terms = -DISTANCE_SCALE * jnp.sum(emb_t * emb_t, axis=1, keepdims=True)
        self.emb_t = (emb_t * (2.0 * DISTANCE_SCALE)).astype(jnp.bfloat16)
        self.points = [emb_ref[:, j * LEAF : (j + 1) * LEAF] for j in range(self.count)]
        self.norms = [-DISTANCE_SCALE * row_norms[:, j * LEAF : (j + 1) * LEAF] for j in range(self.count)]
        self.leaf_values = [self.values[:, j * LEAF : (j + 1) * LEAF] for j in range(self.count)]
        self.neighbours_ref = neighbours_ref
        self.counts_ref = counts_ref
        self.me = lax.axis_index("leaf") * sub_size + lax.axis_index("sub")

    def block(self, j, source_points, source_terms):
        inner = nn_dot(self.emb_t[j * LEAF : (j + 1) * LEAF], source_points)
        exponent = (self.col_terms[j * LEAF : (j + 1) * LEAF] + source_terms) + inner
        return (AMPLITUDE * jnp.exp(exponent)).astype(jnp.bfloat16)

    def weight(self, j, offset):
        leaf = self.me * self.count + j
        total = jnp.int32(0)
        for slot in range(self.neighbours_ref.shape[1]):
            hit = (slot < self.counts_ref[j]) & (self.neighbours_ref[j, slot] == leaf + offset)
            total = total + hit.astype(jnp.int32)
        return total.astype(jnp.float32)


def local_kernel(sub_size, emb_ref, dirs_ref, basis_ref, neighbours_ref, counts_ref, place_ref, out_ref):
    lv = Leaves(emb_ref, dirs_ref, neighbours_ref, counts_ref, sub_size)
    rank = basis_ref.shape[1]
    near = [nt_dot(lv.leaf_values[j], lv.block(j, lv.points[j], lv.norms[j])) for j in range(lv.count)]
    for j in range(lv.count - 1):
        pair = lv.block(j, lv.points[j + 1], lv.norms[j + 1])
        near[j] = near[j] + lv.weight(j, 1) * nt_dot(lv.leaf_values[j + 1], pair)
        near[j + 1] = near[j + 1] + lv.weight(j + 1, -1) * nn_dot(lv.leaf_values[j], pair)
    basis0 = basis_ref[0]
    factor0 = 1.0 / math.sqrt(rank * LEAF)
    scaled0 = [
        (nt_dot(lv.leaf_values[q], basis0[:, q * LEAF : (q + 1) * LEAF]) * factor0).astype(jnp.bfloat16)
        for q in range(lv.count)
    ]
    for q in range(lv.count):
        far0 = nn_dot(scaled0[q ^ 1], basis0[:, q * LEAF : (q + 1) * LEAF])
        out_ref[:, q * LEAF : (q + 1) * LEAF] = (
            RIDGE * lv.directions[:, q * LEAF : (q + 1) * LEAF] + near[q] + far0
        )


def final_kernel(sub_size, sub_bits, leaf_bits, loc_bits, *refs):
    sub_masks = 2**sub_bits - 1
    leaf_masks = 2**leaf_bits - 1
    emb_ref, dirs_ref, local_ref, pair_ref, cross_ref, basis_ref, neighbours_ref, counts_ref = refs[:8]
    round_one = refs[8 : 8 + sub_masks - 1]
    round_two = refs[8 + sub_masks - 1 : 8 + sub_masks - 1 + leaf_masks]
    out_ref = refs[8 + sub_masks - 1 + leaf_masks]
    lv = Leaves(emb_ref, dirs_ref, neighbours_ref, counts_ref, sub_size)
    rank = basis_ref.shape[1]
    nrhs = dirs_ref.shape[0]
    local_points = lv.local_points
    levels = sub_bits + leaf_bits
    lower_width = rank * sub_bits

    pair, cross = pair_ref[...], cross_ref[...]
    step = nrhs * rank * levels // LEAF
    from_pair = unpack_parts(pair, lv.width_e + nrhs, step, rank * levels)
    column_level = lax.broadcasted_iota(jnp.int32, (1, rank * levels), 1) // rank
    lower_level = column_level[:, :lower_width]
    upper_level = column_level[:, : rank * leaf_bits]
    lower = jnp.where(lower_level == 0, from_pair[:, :lower_width], 0.0)
    for mask, got_ref in enumerate(round_one, start=2):
        lower = lower + jnp.where(lower_level == mask.bit_length() - 1, got_ref[:, :lower_width], 0.0)
    upper = None
    for mask, got_ref in enumerate(round_two, start=1):
        term = jnp.where(upper_level == mask.bit_length() - 1, got_ref[...], 0.0)
        upper = term if upper is None else upper + term
    sibling = jnp.concatenate([lower, upper], axis=1)
    factor = jnp.zeros((1, rank * levels), jnp.float32)
    for bit in range(levels):
        factor = jnp.where(column_level == bit, 1.0 / math.sqrt(rank * local_points * 2**bit), factor)
    scaled = (sibling * factor).astype(jnp.bfloat16)
    stacked = basis_ref[loc_bits : loc_bits + levels].reshape(levels * rank, local_points)
    far = nn_dot(scaled, stacked)

    even = lax.axis_index("sub") % 2 == 0
    halo_pair = pair[: lv.width_e + nrhs]
    left, right = jnp.where(even, cross, halo_pair), jnp.where(even, halo_pair, cross)
    halo = {}
    for j, received, offset in ((0, left, -1), (lv.count - 1, right, 1)):
        halo_points = received[: lv.width_e, :]
        halo_float = halo_points.astype(jnp.float32)
        halo_norms = -DISTANCE_SCALE * jnp.sum(halo_float * halo_float, axis=0, keepdims=True)
        weights = lv.block(j, halo_points, halo_norms)
        term = lv.weight(j, offset) * nt_dot(received[lv.width_e :, :], weights)
        halo[j] = term if j not in halo else halo[j] + term
    for j in range(lv.count):
        total = local_ref[:, j * LEAF : (j + 1) * LEAF] + far[:, j * LEAF : (j + 1) * LEAF]
        if j in halo:
            total = total + halo[j]
        out_ref[:, j * LEAF : (j + 1) * LEAF] = total


def on_device(embeddings, directions, level_basis, neighbours, counts):
    axes = ("leaf", "sub")
    width_e = embeddings.shape[0]
    local_points = embeddings.shape[1]
    rank = level_basis.shape[1]
    nrhs = directions.shape[0]
    sub_size = lax.axis_size("sub")
    leaf_size = lax.axis_size("leaf")
    sub_bits = sub_size.bit_length() - 1
    leaf_bits = leaf_size.bit_length() - 1
    dev_bits = sub_bits + leaf_bits
    loc_bits = level_basis.shape[0] - dev_bits

    step = nrhs * rank * dev_bits // LEAF
    pair_shape = jax.ShapeDtypeStruct((width_e + nrhs + 3 * step, LEAF), jnp.bfloat16)
    cross_shape = jax.ShapeDtypeStruct((width_e + nrhs, LEAF), jnp.bfloat16)
    parts_shape = jax.ShapeDtypeStruct((nrhs, rank * dev_bits), jnp.float32)
    pair, cross, parts = pl.pallas_call(
        functools.partial(send_kernel, loc_bits),
        out_shape=(pair_shape, cross_shape, parts_shape),
        in_specs=[VMEM, VMEM, VMEM],
        out_specs=(VMEM, VMEM, VMEM),
    )(embeddings, directions, level_basis)

    ndev = sub_size * leaf_size
    from_pair = lax.ppermute(pair, axes, [(i, i ^ 1) for i in range(ndev)])
    round_one = [from_mask(parts, "sub", mask) for mask in range(2, sub_size)]
    from_cross = lax.ppermute(cross, axes, [(i, i - 1 + 2 * (i % 2)) for i in range(1, ndev - 1)])
    upper = slice(rank * sub_bits, rank * dev_bits)
    line = parts[:, upper] + unpack_parts(from_pair, width_e + nrhs, step, rank * dev_bits)[:, upper]
    for got in round_one:
        line = line + got[:, upper]
    round_two = [from_mask(line, "leaf", mask) for mask in range(1, leaf_size)]

    out = jax.ShapeDtypeStruct((nrhs, local_points), jnp.float32)
    local = pl.pallas_call(
        functools.partial(local_kernel, sub_size),
        out_shape=out,
        in_specs=[VMEM, VMEM, VMEM, SMEM, SMEM, VMEM],
        out_specs=VMEM,
        input_output_aliases={5: 0},
    )(*in_vmem(embeddings, directions, level_basis), neighbours, counts, *in_vmem(jnp.zeros(out.shape, out.dtype)))

    remote = round_one + round_two
    return pl.pallas_call(
        functools.partial(final_kernel, sub_size, sub_bits, leaf_bits, loc_bits),
        out_shape=out,
        in_specs=[VMEM] * 6 + [SMEM, SMEM] + [VMEM] * len(remote),
        out_specs=VMEM,
    )(
        *in_vmem(embeddings, directions, local, from_pair, from_cross, level_basis),
        neighbours,
        counts,
        *in_vmem(*remote),
    )


def solution(mesh):
    placed = (
        P(None, ("groups", "leaf", "sub")),
        P(None, ("groups", "leaf", "sub")),
        P(None, None, ("groups", "leaf", "sub")),
        P(("groups", "leaf", "sub"), None),
        P(("groups", "leaf", "sub")),
    )
    return jax.shard_map(
        on_device,
        mesh=mesh,
        in_specs=placed,
        out_specs=P(None, ("groups", "leaf", "sub")),
        check_vma=False,
    )
```

```python
import functools
import math

import jax
import jax.numpy as jnp
from jax import lax
from jax.experimental import pallas as pl
from jax.experimental.pallas import tpu as pltpu
from jax.sharding import PartitionSpec as P

LEAF = 512


AMPLITUDE = 0.5
DISTANCE_SCALE = 0.125
RIDGE = 0.5

VMEM = pl.BlockSpec(memory_space=pltpu.VMEM)
SMEM = pl.BlockSpec(memory_space=pltpu.SMEM)


def from_mask(x, axis, mask):
    pairs = [(i, i ^ mask) for i in range(lax.axis_size(axis))]
    return lax.ppermute(x, axis, pairs)


def in_vmem(*arrays):
    return [pltpu.with_memory_space_constraint(a, pltpu.VMEM) for a in arrays]


def nt_dot(a, b):
    return lax.dot_general(a, b, (((1,), (1,)), ((), ())), preferred_element_type=jnp.float32)


def nn_dot(a, b):
    return lax.dot_general(a, b, (((1,), (0,)), ((), ())), preferred_element_type=jnp.float32)


def split_rows(x, width):
    groups = width // x.shape[1]
    step = x.shape[0] // groups
    return jnp.concatenate([x[g * step : (g + 1) * step] for g in range(groups)], axis=1)


def join_rows(x, columns):
    groups = x.shape[1] // columns
    return jnp.concatenate([x[:, g * columns : (g + 1) * columns] for g in range(groups)], axis=0)


def send_kernel(loc_bits, emb_ref, dirs_ref, basis_ref, pair_ref, cross_ref, parts_ref):
    width_e = emb_ref.shape[0]
    local_points = emb_ref.shape[1]
    nrhs = dirs_ref.shape[0]
    values = dirs_ref[...].astype(jnp.bfloat16)
    even = lax.axis_index("sub") % 2 == 0
    head_points, tail_points = emb_ref[:, :LEAF], emb_ref[:, local_points - LEAF :]
    head_values, tail_values = values[:, :LEAF], values[:, local_points - LEAF :]
    pair_ref[:width_e, :] = jnp.where(even, tail_points, head_points)
    pair_ref[width_e : width_e + nrhs, :] = jnp.where(even, tail_values, head_values)
    cross_ref[:width_e, :] = jnp.where(even, head_points, tail_points)
    cross_ref[width_e:, :] = jnp.where(even, head_values, tail_values)
    levels, rank = parts_ref.shape[1] // basis_ref.shape[1], basis_ref.shape[1]
    stacked = basis_ref[loc_bits : loc_bits + levels].reshape(levels * rank, local_points)
    parts = nt_dot(values, stacked)
    parts_ref[...] = parts
    rows = split_rows(parts, LEAF)
    high = rows.astype(jnp.bfloat16)
    rest = rows - high.astype(jnp.float32)
    middle = rest.astype(jnp.bfloat16)
    low = (rest - middle.astype(jnp.float32)).astype(jnp.bfloat16)
    start = width_e + nrhs
    step = rows.shape[0]
    pair_ref[start : start + step, :] = high
    pair_ref[start + step : start + 2 * step, :] = middle
    pair_ref[start + 2 * step : start + 3 * step, :] = low


def unpack_parts(pair, start, step, columns):
    pieces = pair[start : start + 3 * step].astype(jnp.float32)
    rows = (pieces[:step] + pieces[step : 2 * step]) + pieces[2 * step :]
    return join_rows(rows, columns)


class Leaves:
    def __init__(self, emb_ref, dirs_ref, neighbours_ref, counts_ref, sub_size):
        self.width_e = emb_ref.shape[0]
        self.local_points = emb_ref.shape[1]
        self.count = self.local_points // LEAF
        self.directions = dirs_ref[...]
        self.values = self.directions.astype(jnp.bfloat16)
        emb_float = emb_ref[...].astype(jnp.float32)
        row_norms = jnp.sum(emb_float * emb_float, axis=0, keepdims=True)
        emb_t = emb_float.T
        self.col_terms = -DISTANCE_SCALE * jnp.sum(emb_t * emb_t, axis=1, keepdims=True)
        self.emb_t = (emb_t * (2.0 * DISTANCE_SCALE)).astype(jnp.bfloat16)
        self.points = [emb_ref[:, j * LEAF : (j + 1) * LEAF] for j in range(self.count)]
        self.norms = [-DISTANCE_SCALE * row_norms[:, j * LEAF : (j + 1) * LEAF] for j in range(self.count)]
        self.leaf_values = [self.values[:, j * LEAF : (j + 1) * LEAF] for j in range(self.count)]
        self.neighbours_ref = neighbours_ref
        self.counts_ref = counts_ref
        self.me = lax.axis_index("leaf") * sub_size + lax.axis_index("sub")

    def block(self, j, source_points, source_terms):
        inner = nn_dot(self.emb_t[j * LEAF : (j + 1) * LEAF], source_points)
        exponent = (self.col_terms[j * LEAF : (j + 1) * LEAF] + source_terms) + inner
        return (AMPLITUDE * jnp.exp(exponent)).astype(jnp.bfloat16)

    def weight(self, j, offset):
        leaf = self.me * self.count + j
        total = jnp.int32(0)
        for slot in range(self.neighbours_ref.shape[1]):
            hit = (slot < self.counts_ref[j]) & (self.neighbours_ref[j, slot] == leaf + offset)
            total = total + hit.astype(jnp.int32)
        return total.astype(jnp.float32)


def local_kernel(sub_size, emb_ref, dirs_ref, basis_ref, neighbours_ref, counts_ref, out_ref):
    lv = Leaves(emb_ref, dirs_ref, neighbours_ref, counts_ref, sub_size)
    rank = basis_ref.shape[1]
    near = [nt_dot(lv.leaf_values[j], lv.block(j, lv.points[j], lv.norms[j])) for j in range(lv.count)]
    for j in range(lv.count - 1):
        pair = lv.block(j, lv.points[j + 1], lv.norms[j + 1])
        near[j] = near[j] + lv.weight(j, 1) * nt_dot(lv.leaf_values[j + 1], pair)
        near[j + 1] = near[j + 1] + lv.weight(j + 1, -1) * nn_dot(lv.leaf_values[j], pair)
    basis0 = basis_ref[0]
    factor0 = 1.0 / math.sqrt(rank * LEAF)
    scaled0 = [
        (nt_dot(lv.leaf_values[q], basis0[:, q * LEAF : (q + 1) * LEAF]) * factor0).astype(jnp.bfloat16)
        for q in range(lv.count)
    ]
    for q in range(lv.count):
        far0 = nn_dot(scaled0[q ^ 1], basis0[:, q * LEAF : (q + 1) * LEAF])
        out_ref[:, q * LEAF : (q + 1) * LEAF] = (
            RIDGE * lv.directions[:, q * LEAF : (q + 1) * LEAF] + near[q] + far0
        )


def final_kernel(sub_size, sub_bits, leaf_bits, loc_bits, *refs):
    sub_masks = 2**sub_bits - 1
    leaf_masks = 2**leaf_bits - 1
    emb_ref, dirs_ref, local_ref, pair_ref, cross_ref, basis_ref, neighbours_ref, counts_ref = refs[:8]
    round_one = refs[8 : 8 + sub_masks - 1]
    round_two = refs[8 + sub_masks - 1 : 8 + sub_masks - 1 + leaf_masks]
    out_ref = refs[8 + sub_masks - 1 + leaf_masks]
    lv = Leaves(emb_ref, dirs_ref, neighbours_ref, counts_ref, sub_size)
    rank = basis_ref.shape[1]
    nrhs = dirs_ref.shape[0]
    local_points = lv.local_points
    levels = sub_bits + leaf_bits
    lower_width = rank * sub_bits

    pair, cross = pair_ref[...], cross_ref[...]
    step = nrhs * rank * levels // LEAF
    from_pair = unpack_parts(pair, lv.width_e + nrhs, step, rank * levels)
    column_level = lax.broadcasted_iota(jnp.int32, (1, rank * levels), 1) // rank
    lower_level = column_level[:, :lower_width]
    upper_level = column_level[:, : rank * leaf_bits]
    lower = jnp.where(lower_level == 0, from_pair[:, :lower_width], 0.0)
    for mask, got_ref in enumerate(round_one, start=2):
        lower = lower + jnp.where(lower_level == mask.bit_length() - 1, got_ref[:, :lower_width], 0.0)
    upper = None
    for mask, got_ref in enumerate(round_two, start=1):
        term = jnp.where(upper_level == mask.bit_length() - 1, got_ref[...], 0.0)
        upper = term if upper is None else upper + term
    sibling = jnp.concatenate([lower, upper], axis=1)
    factor = jnp.zeros((1, rank * levels), jnp.float32)
    for bit in range(levels):
        factor = jnp.where(column_level == bit, 1.0 / math.sqrt(rank * local_points * 2**bit), factor)
    scaled = (sibling * factor).astype(jnp.bfloat16)
    stacked = basis_ref[loc_bits : loc_bits + levels].reshape(levels * rank, local_points)
    far = nn_dot(scaled, stacked)

    even = lax.axis_index("sub") % 2 == 0
    halo_pair = pair[: lv.width_e + nrhs]
    left, right = jnp.where(even, cross, halo_pair), jnp.where(even, halo_pair, cross)
    halo = {}
    for j, received, offset in ((0, left, -1), (lv.count - 1, right, 1)):
        halo_points = received[: lv.width_e, :]
        halo_float = halo_points.astype(jnp.float32)
        halo_norms = -DISTANCE_SCALE * jnp.sum(halo_float * halo_float, axis=0, keepdims=True)
        weights = lv.block(j, halo_points, halo_norms)
        term = lv.weight(j, offset) * nt_dot(received[lv.width_e :, :], weights)
        halo[j] = term if j not in halo else halo[j] + term
    for j in range(lv.count):
        total = local_ref[:, j * LEAF : (j + 1) * LEAF] + far[:, j * LEAF : (j + 1) * LEAF]
        if j in halo:
            total = total + halo[j]
        out_ref[:, j * LEAF : (j + 1) * LEAF] = total


def on_device(embeddings, directions, level_basis, neighbours, counts):
    axes = ("leaf", "sub")
    width_e = embeddings.shape[0]
    local_points = embeddings.shape[1]
    rank = level_basis.shape[1]
    nrhs = directions.shape[0]
    sub_size = lax.axis_size("sub")
    leaf_size = lax.axis_size("leaf")
    sub_bits = sub_size.bit_length() - 1
    leaf_bits = leaf_size.bit_length() - 1
    dev_bits = sub_bits + leaf_bits
    loc_bits = level_basis.shape[0] - dev_bits

    step = nrhs * rank * dev_bits // LEAF
    pair_shape = jax.ShapeDtypeStruct((width_e + nrhs + 3 * step, LEAF), jnp.bfloat16)
    cross_shape = jax.ShapeDtypeStruct((width_e + nrhs, LEAF), jnp.bfloat16)
    parts_shape = jax.ShapeDtypeStruct((nrhs, rank * dev_bits), jnp.float32)
    pair, cross, parts = pl.pallas_call(
        functools.partial(send_kernel, loc_bits),
        out_shape=(pair_shape, cross_shape, parts_shape),
        in_specs=[VMEM, VMEM, VMEM],
        out_specs=(VMEM, VMEM, VMEM),
    )(embeddings, directions, level_basis)

    ndev = sub_size * leaf_size
    from_pair = lax.ppermute(pair, axes, [(i, i ^ 1) for i in range(ndev)])
    round_one = [from_mask(parts, "sub", mask) for mask in range(2, sub_size)]
    upper = slice(rank * sub_bits, rank * dev_bits)
    line = parts[:, upper] + unpack_parts(from_pair, width_e + nrhs, step, rank * dev_bits)[:, upper]
    for got in round_one:
        line = line + got[:, upper]
    cross, line = lax.optimization_barrier((cross, line))
    round_two = [from_mask(line, "leaf", mask) for mask in range(1, leaf_size)]
    from_cross = lax.ppermute(cross, axes, [(i, i - 1 + 2 * (i % 2)) for i in range(1, ndev - 1)])

    out = jax.ShapeDtypeStruct((nrhs, local_points), jnp.float32)
    local = pl.pallas_call(
        functools.partial(local_kernel, sub_size),
        out_shape=out,
        in_specs=[VMEM, VMEM, VMEM, SMEM, SMEM],
        out_specs=VMEM,
    )(*in_vmem(embeddings, directions, level_basis), neighbours, counts)

    remote = round_one + round_two
    return pl.pallas_call(
        functools.partial(final_kernel, sub_size, sub_bits, leaf_bits, loc_bits),
        out_shape=out,
        in_specs=[VMEM] * 6 + [SMEM, SMEM] + [VMEM] * len(remote),
        out_specs=VMEM,
        input_output_aliases={2: 0},
    )(
        *in_vmem(embeddings, directions, local, from_pair, from_cross, level_basis),
        neighbours,
        counts,
        *in_vmem(*remote),
    )


def solution(mesh):
    placed = (
        P(None, ("groups", "leaf", "sub")),
        P(None, ("groups", "leaf", "sub")),
        P(None, None, ("groups", "leaf", "sub")),
        P(("groups", "leaf", "sub"), None),
        P(("groups", "leaf", "sub")),
    )
    return jax.shard_map(
        on_device,
        mesh=mesh,
        in_specs=placed,
        out_specs=P(None, ("groups", "leaf", "sub")),
        check_vma=False,
    )
```

```python
import functools
import math

import jax
import jax.numpy as jnp
from jax import lax
from jax.experimental import pallas as pl
from jax.experimental.pallas import tpu as pltpu
from jax.sharding import PartitionSpec as P

LEAF = 512


AMPLITUDE = 0.5
DISTANCE_SCALE = 0.125
RIDGE = 0.5

VMEM = pl.BlockSpec(memory_space=pltpu.VMEM)
SMEM = pl.BlockSpec(memory_space=pltpu.SMEM)


def from_mask(x, axis, mask):
    pairs = [(i, i ^ mask) for i in range(lax.axis_size(axis))]
    return lax.ppermute(x, axis, pairs)


def in_vmem(*arrays):
    return [pltpu.with_memory_space_constraint(a, pltpu.VMEM) for a in arrays]


def nt_dot(a, b):
    return lax.dot_general(a, b, (((1,), (1,)), ((), ())), preferred_element_type=jnp.float32)


def nn_dot(a, b):
    return lax.dot_general(a, b, (((1,), (0,)), ((), ())), preferred_element_type=jnp.float32)


def split_rows(x, width):
    groups = width // x.shape[1]
    step = x.shape[0] // groups
    return jnp.concatenate([x[g * step : (g + 1) * step] for g in range(groups)], axis=1)


def join_rows(x, columns):
    groups = x.shape[1] // columns
    return jnp.concatenate([x[:, g * columns : (g + 1) * columns] for g in range(groups)], axis=0)


def cross_kernel(emb_ref, dirs_ref, cross_ref):
    width_e = emb_ref.shape[0]
    local_points = emb_ref.shape[1]
    values = dirs_ref[...].astype(jnp.bfloat16)
    even = lax.axis_index("sub") % 2 == 0
    cross_ref[:width_e, :] = jnp.where(even, emb_ref[:, :LEAF], emb_ref[:, local_points - LEAF :])
    cross_ref[width_e:, :] = jnp.where(even, values[:, :LEAF], values[:, local_points - LEAF :])


def send_kernel(loc_bits, emb_ref, dirs_ref, basis_ref, pair_ref, parts_ref):
    width_e = emb_ref.shape[0]
    local_points = emb_ref.shape[1]
    nrhs = dirs_ref.shape[0]
    values = dirs_ref[...].astype(jnp.bfloat16)
    even = lax.axis_index("sub") % 2 == 0
    head_points, tail_points = emb_ref[:, :LEAF], emb_ref[:, local_points - LEAF :]
    head_values, tail_values = values[:, :LEAF], values[:, local_points - LEAF :]
    pair_ref[:width_e, :] = jnp.where(even, tail_points, head_points)
    pair_ref[width_e : width_e + nrhs, :] = jnp.where(even, tail_values, head_values)
    levels, rank = parts_ref.shape[1] // basis_ref.shape[1], basis_ref.shape[1]
    stacked = basis_ref[loc_bits : loc_bits + levels].reshape(levels * rank, local_points)
    parts = nt_dot(values, stacked)
    parts_ref[...] = parts
    rows = split_rows(parts, LEAF)
    high = rows.astype(jnp.bfloat16)
    rest = rows - high.astype(jnp.float32)
    middle = rest.astype(jnp.bfloat16)
    low = (rest - middle.astype(jnp.float32)).astype(jnp.bfloat16)
    start = width_e + nrhs
    step = rows.shape[0]
    pair_ref[start : start + step, :] = high
    pair_ref[start + step : start + 2 * step, :] = middle
    pair_ref[start + 2 * step : start + 3 * step, :] = low


def unpack_parts(pair, start, step, columns):
    pieces = pair[start : start + 3 * step].astype(jnp.float32)
    rows = (pieces[:step] + pieces[step : 2 * step]) + pieces[2 * step :]
    return join_rows(rows, columns)


class Leaves:
    def __init__(self, emb_ref, dirs_ref, neighbours_ref, counts_ref, sub_size):
        self.width_e = emb_ref.shape[0]
        self.local_points = emb_ref.shape[1]
        self.count = self.local_points // LEAF
        self.directions = dirs_ref[...]
        self.values = self.directions.astype(jnp.bfloat16)
        emb_float = emb_ref[...].astype(jnp.float32)
        row_norms = jnp.sum(emb_float * emb_float, axis=0, keepdims=True)
        emb_t = emb_float.T
        self.col_terms = -DISTANCE_SCALE * jnp.sum(emb_t * emb_t, axis=1, keepdims=True)
        self.emb_t = (emb_t * (2.0 * DISTANCE_SCALE)).astype(jnp.bfloat16)
        self.points = [emb_ref[:, j * LEAF : (j + 1) * LEAF] for j in range(self.count)]
        self.norms = [-DISTANCE_SCALE * row_norms[:, j * LEAF : (j + 1) * LEAF] for j in range(self.count)]
        self.leaf_values = [self.values[:, j * LEAF : (j + 1) * LEAF] for j in range(self.count)]
        self.neighbours_ref = neighbours_ref
        self.counts_ref = counts_ref
        self.me = lax.axis_index("leaf") * sub_size + lax.axis_index("sub")

    def block(self, j, source_points, source_terms):
        inner = nn_dot(self.emb_t[j * LEAF : (j + 1) * LEAF], source_points)
        exponent = (self.col_terms[j * LEAF : (j + 1) * LEAF] + source_terms) + inner
        return (AMPLITUDE * jnp.exp(exponent)).astype(jnp.bfloat16)

    def weight(self, j, offset):
        leaf = self.me * self.count + j
        total = jnp.int32(0)
        for slot in range(self.neighbours_ref.shape[1]):
            hit = (slot < self.counts_ref[j]) & (self.neighbours_ref[j, slot] == leaf + offset)
            total = total + hit.astype(jnp.int32)
        return total.astype(jnp.float32)


def local_kernel(sub_size, emb_ref, dirs_ref, basis_ref, neighbours_ref, counts_ref, out_ref):
    lv = Leaves(emb_ref, dirs_ref, neighbours_ref, counts_ref, sub_size)
    rank = basis_ref.shape[1]
    near = [nt_dot(lv.leaf_values[j], lv.block(j, lv.points[j], lv.norms[j])) for j in range(lv.count)]
    for j in range(lv.count - 1):
        pair = lv.block(j, lv.points[j + 1], lv.norms[j + 1])
        near[j] = near[j] + lv.weight(j, 1) * nt_dot(lv.leaf_values[j + 1], pair)
        near[j + 1] = near[j + 1] + lv.weight(j + 1, -1) * nn_dot(lv.leaf_values[j], pair)
    basis0 = basis_ref[0]
    factor0 = 1.0 / math.sqrt(rank * LEAF)
    scaled0 = [
        (nt_dot(lv.leaf_values[q], basis0[:, q * LEAF : (q + 1) * LEAF]) * factor0).astype(jnp.bfloat16)
        for q in range(lv.count)
    ]
    for q in range(lv.count):
        far0 = nn_dot(scaled0[q ^ 1], basis0[:, q * LEAF : (q + 1) * LEAF])
        out_ref[:, q * LEAF : (q + 1) * LEAF] = (
            RIDGE * lv.directions[:, q * LEAF : (q + 1) * LEAF] + near[q] + far0
        )


def final_kernel(sub_size, sub_bits, leaf_bits, loc_bits, *refs):
    sub_masks = 2**sub_bits - 1
    leaf_masks = 2**leaf_bits - 1
    emb_ref, dirs_ref, local_ref, pair_ref, cross_ref, basis_ref, neighbours_ref, counts_ref = refs[:8]
    round_one = refs[8 : 8 + sub_masks - 1]
    round_two = refs[8 + sub_masks - 1 : 8 + sub_masks - 1 + leaf_masks]
    out_ref = refs[8 + sub_masks - 1 + leaf_masks]
    lv = Leaves(emb_ref, dirs_ref, neighbours_ref, counts_ref, sub_size)
    rank = basis_ref.shape[1]
    nrhs = dirs_ref.shape[0]
    local_points = lv.local_points
    levels = sub_bits + leaf_bits
    lower_width = rank * sub_bits

    pair, cross = pair_ref[...], cross_ref[...]
    step = nrhs * rank * levels // LEAF
    from_pair = unpack_parts(pair, lv.width_e + nrhs, step, rank * levels)
    column_level = lax.broadcasted_iota(jnp.int32, (1, rank * levels), 1) // rank
    lower_level = column_level[:, :lower_width]
    upper_level = column_level[:, : rank * leaf_bits]
    lower = jnp.where(lower_level == 0, from_pair[:, :lower_width], 0.0)
    for mask, got_ref in enumerate(round_one, start=2):
        lower = lower + jnp.where(lower_level == mask.bit_length() - 1, got_ref[:, :lower_width], 0.0)
    upper = None
    for mask, got_ref in enumerate(round_two, start=1):
        term = jnp.where(upper_level == mask.bit_length() - 1, got_ref[...], 0.0)
        upper = term if upper is None else upper + term
    sibling = jnp.concatenate([lower, upper], axis=1)
    factor = jnp.zeros((1, rank * levels), jnp.float32)
    for bit in range(levels):
        factor = jnp.where(column_level == bit, 1.0 / math.sqrt(rank * local_points * 2**bit), factor)
    scaled = (sibling * factor).astype(jnp.bfloat16)
    stacked = basis_ref[loc_bits : loc_bits + levels].reshape(levels * rank, local_points)
    far = nn_dot(scaled, stacked)

    even = lax.axis_index("sub") % 2 == 0
    halo_pair = pair[: lv.width_e + nrhs]
    left, right = jnp.where(even, cross, halo_pair), jnp.where(even, halo_pair, cross)
    halo = {}
    for j, received, offset in ((0, left, -1), (lv.count - 1, right, 1)):
        halo_points = received[: lv.width_e, :]
        halo_float = halo_points.astype(jnp.float32)
        halo_norms = -DISTANCE_SCALE * jnp.sum(halo_float * halo_float, axis=0, keepdims=True)
        weights = lv.block(j, halo_points, halo_norms)
        term = lv.weight(j, offset) * nt_dot(received[lv.width_e :, :], weights)
        halo[j] = term if j not in halo else halo[j] + term
    for j in range(lv.count):
        total = local_ref[:, j * LEAF : (j + 1) * LEAF] + far[:, j * LEAF : (j + 1) * LEAF]
        if j in halo:
            total = total + halo[j]
        out_ref[:, j * LEAF : (j + 1) * LEAF] = total


def on_device(embeddings, directions, level_basis, neighbours, counts):
    axes = ("leaf", "sub")
    width_e = embeddings.shape[0]
    local_points = embeddings.shape[1]
    rank = level_basis.shape[1]
    nrhs = directions.shape[0]
    sub_size = lax.axis_size("sub")
    leaf_size = lax.axis_size("leaf")
    sub_bits = sub_size.bit_length() - 1
    leaf_bits = leaf_size.bit_length() - 1
    dev_bits = sub_bits + leaf_bits
    loc_bits = level_basis.shape[0] - dev_bits

    step = nrhs * rank * dev_bits // LEAF
    pair_shape = jax.ShapeDtypeStruct((width_e + nrhs + 3 * step, LEAF), jnp.bfloat16)
    cross_shape = jax.ShapeDtypeStruct((width_e + nrhs, LEAF), jnp.bfloat16)
    parts_shape = jax.ShapeDtypeStruct((nrhs, rank * dev_bits), jnp.float32)
    cross = pl.pallas_call(
        cross_kernel, out_shape=cross_shape, in_specs=[VMEM, VMEM], out_specs=VMEM
    )(embeddings, directions)
    ndev = sub_size * leaf_size
    from_cross = lax.ppermute(cross, axes, [(i, i - 1 + 2 * (i % 2)) for i in range(1, ndev - 1)])
    pair, parts = pl.pallas_call(
        functools.partial(send_kernel, loc_bits),
        out_shape=(pair_shape, parts_shape),
        in_specs=[VMEM, VMEM, VMEM],
        out_specs=(VMEM, VMEM),
    )(embeddings, directions, *in_vmem(level_basis))

    ndev = sub_size * leaf_size
    from_pair = lax.ppermute(pair, axes, [(i, i ^ 1) for i in range(ndev)])
    round_one = [from_mask(parts, "sub", mask) for mask in range(2, sub_size)]
    upper = slice(rank * sub_bits, rank * dev_bits)
    line = parts[:, upper] + unpack_parts(from_pair, width_e + nrhs, step, rank * dev_bits)[:, upper]
    for got in round_one:
        line = line + got[:, upper]
    round_two = [from_mask(line, "leaf", mask) for mask in range(1, leaf_size)]

    out = jax.ShapeDtypeStruct((nrhs, local_points), jnp.float32)
    local = pl.pallas_call(
        functools.partial(local_kernel, sub_size),
        out_shape=out,
        in_specs=[VMEM, VMEM, VMEM, SMEM, SMEM],
        out_specs=VMEM,
    )(*in_vmem(embeddings, directions, level_basis), neighbours, counts)

    remote = round_one + round_two
    return pl.pallas_call(
        functools.partial(final_kernel, sub_size, sub_bits, leaf_bits, loc_bits),
        out_shape=out,
        in_specs=[VMEM] * 6 + [SMEM, SMEM] + [VMEM] * len(remote),
        out_specs=VMEM,
        input_output_aliases={2: 0},
    )(
        *in_vmem(embeddings, directions, local, from_pair, from_cross, level_basis),
        neighbours,
        counts,
        *in_vmem(*remote),
    )


def solution(mesh):
    placed = (
        P(None, ("groups", "leaf", "sub")),
        P(None, ("groups", "leaf", "sub")),
        P(None, None, ("groups", "leaf", "sub")),
        P(("groups", "leaf", "sub"), None),
        P(("groups", "leaf", "sub")),
    )
    return jax.shard_map(
        on_device,
        mesh=mesh,
        in_specs=placed,
        out_specs=P(None, ("groups", "leaf", "sub")),
        check_vma=False,
    )
```
